32 devices in a mesh: row: 8 (over z, x), col: 4 (over y, core).
Axes of the slice: x: 2, y: 2, z: 4, core: 2. Of those that a mesh axis runs over, the one named last changes fastest.
Arguments:
- eigvecs: bfloat16 [64, 2048, 128], P('row'), may hold values from -0.125 to 0.125
- coupling: bfloat16 [64, 2048, 2, 512], P('row', None, None, 'col'), may hold values from -0.25 to 0.25
- mode_counts: int32 [64], P('row'), may hold values from 32 to 128, as said below
- tree_segments: int32 [64, 2], P('row'), may hold values from 0 to 15, all different within a row; in each aligned block of 8 rows (0 to 7, 8 to 15, ...) at most 2 rows name the same one
- eigvals: float32 [64, 128], P('row'), may hold values from 0.5 to 8
- interface_stiffness: float32 [8192, 8192], P('row', 'col'), as said below
Outputs:
- reduced_ii: float32 [8192, 8192], P('row', 'col')
- reduced_mi: float32 [8192, 8192], P('row', 'col')
- reduced_mm: float32 [8192, 8192], P('row', 'col')
The draws below stay inside these ranges and needn't reach their ends.
Inputs may be any that keep to these rules, and one draw needn't show every extreme that they name: `mode_counts`: some substructure has exactly 128 live modes. `tree_segments`: each substructure names two different segments; among the 8 substructures of one index of row no segment is named more than 2 times, a bound that some block reaches. `interface_stiffness`: symmetric; its leading 512 x 512 block is positive definite.
All inputs are finite; a program needn't handle non-finite values.
Results may differ from the reference program's by a relative error of at most 0.0003.
Values sent between devices are 32-bit elements; how exact they have to be, the bound alone decides.
No kernel may reach another device: no remote copies, remote signals or barrier semaphores. Data moves between devices by JAX's collectives and lax.ppermute only.
A program may use at most 128 MiB of HBM per device.

```python
import math
import jax
import jax.numpy as jnp
import numpy as np
from jax import lax

SUB_ROW = 8
NINT = 2048
MSLOT = 128
PANEL = 512
NSEG = 16
MOST = 2
SUBS = 64
NMODE = 8192
NIF = 8192


def draw_mode_counts(key, part):
    first_key, second_key = jax.random.split(jax.random.fold_in(key, 11))
    counts = jax.random.randint(first_key, (SUBS,), MSLOT // 4, MSLOT + 1)
    chosen = jax.random.randint(second_key, (), 0, SUBS)
    return jnp.where(jnp.arange(SUBS) == chosen, MSLOT, counts).astype(jnp.int32)


def draw_interface_stiffness(key, part):
    first_key, second_key = jax.random.split(jax.random.fold_in(key, 23))
    uniform_part = jax.random.uniform(first_key, (NIF, NIF), jnp.float32, -1.0, 1.0)
    off_diagonal = (uniform_part + uniform_part.T) * (0.4 * PANEL ** (-0.5))
    diagonal = jax.random.uniform(second_key, (NIF,), jnp.float32, 1.0, 2.0)
    positions = jnp.arange(NIF)
    on_diagonal = positions[:, None] == positions[None, :]
    return jnp.where(on_diagonal, diagonal[:, None], off_diagonal).astype(jnp.float32)


def shard_levels(key, shape, cuts, least, largest):
    def one(dim, shards_of):
        heights = jax.random.uniform(jax.random.fold_in(jax.random.fold_in(key, 6), dim), (shards_of,), jnp.float32, least / len(cuts), largest / len(cuts))
        return jnp.repeat(jnp.exp(heights), shape[dim] // shards_of).reshape((-1,) + (1,) * (len(shape) - dim - 1))

    loudness = one(*cuts[0])
    for cut in cuts[1:]:
        loudness = loudness * one(*cut)
    return loudness


def deal_out(own_key, own, number, rows, number_of, top, most, lean):
    sequence = jax.random.permutation(own_key, number_of)
    heavy_load, ordinary = portions_of(number_of, rows * top, most, lean, True), portions_of(number_of, rows * top, most, lean, False)
    places = jnp.arange(number_of)

    def named(tallies, turn):
        used = int((tallies > 0).sum())
        fixed = max(1, used // 4)
        passed = fixed + (places - fixed + turn * (used - fixed)) % max(1, number_of - fixed)
        return jnp.zeros((number_of,), jnp.int32).at[sequence[jnp.where(places < fixed, places, passed)]].set(jnp.asarray(tallies, jnp.int32))

    tallies = jnp.where(number % 4 == 0, named(heavy_load, number // 4), named(ordinary, number - number // 4 - 1))
    mixed = jax.random.permutation(jax.random.fold_in(own, 3), number_of)
    giver, sink = mixed[0:number_of // 2 * 2:2], mixed[1:number_of // 2 * 2:2]
    room = jnp.minimum(tallies[giver] - 1, most - tallies[sink]) // 2
    room = jnp.where((giver == sequence[0]) | (sink == sequence[0]) | (tallies[sink] == 0), 0, jnp.maximum(room, 0))
    passed = jax.random.randint(jax.random.fold_in(own, 4), (number_of // 2,), 0, 1 << 20) % (room + 1)
    tallies = tallies.at[giver].add(-passed).at[sink].add(passed)
    items = jnp.searchsorted(jnp.cumsum(tallies), jnp.arange(rows * top), side="right").astype(jnp.int32)
    listing = items.reshape(top, rows).T
    listing = listing[jax.random.permutation(jax.random.fold_in(own, 1), rows)]
    turn = jax.random.randint(jax.random.fold_in(own, 2), (rows, 1), 0, top)
    return jnp.take_along_axis(listing, (jnp.arange(top)[None, :] + turn) % top, axis=1)


def portions_of(amount, total, bound, skew, full):
    portions = [(1 << 20) // math.isqrt(rank ** skew) + 1 for rank in range(1, amount + 1)]
    largest = bound if full else min(bound, max(-(-total // amount), total * portions[0] // sum(portions)))
    least = 1 if total - largest >= amount - 1 else 0
    given, spare = [largest] + [least] * (amount - 1), total - largest - least * (amount - 1)
    while spare > 0:
        movable = [i for i in range(1, amount) if given[i] < largest] or [i for i in range(1, amount) if given[i] < bound]
        whole, budget = sum([portions[i] for i in movable]), spare
        for i in movable:
            addition = min(bound - given[i], max(1, budget * portions[i] // whole), spare)
            given[i] = given[i] + addition
            spare = spare - addition
    return np.array(given)


def noise(key, dims, spread, bound, cuts=(), held_as=jnp.bfloat16):
    factor_of = shard_levels(key, dims, cuts, -0.22, 0.18) if cuts else 1.0
    array = jax.random.normal(key, dims, jnp.float32) * spread * factor_of
    return jnp.minimum(jnp.maximum(array, -bound), bound).astype(held_as)


def setup_inputs(seed: int = 0) -> dict:
    splits = jax.random.split(jax.random.key(seed), 7)
    eigvecs = noise(splits[0], (SUBS, NINT, MSLOT), NINT ** -0.5, 0.125, ((0, 8),))
    coupling = noise(splits[1], (SUBS, NINT, 2, PANEL), PANEL ** -0.5, 0.25, ((0, 8), (3, 4)))
    mode_counts = draw_mode_counts(jax.random.fold_in(splits[6], 71), 0)
    tree_segments_keys = jax.random.split(jax.random.fold_in(splits[3], 1), SUBS // SUB_ROW)
    tree_segments_turns = jax.random.permutation(jax.random.fold_in(splits[3], 3), SUBS // SUB_ROW)
    tree_segments = jax.vmap(lambda own, number: deal_out(jax.random.fold_in(splits[3], 2), own, number, SUB_ROW, NSEG, 2, MOST, 2))(tree_segments_keys, tree_segments_turns).reshape((SUBS, 2))
    eigvals = jnp.clip(jnp.exp(math.log(8.0) - 2.7725887 * jax.random.uniform(splits[4], (SUBS, MSLOT), jnp.float32) ** shard_levels(splits[4], (SUBS, MSLOT), ((0, 8),), -0.2, 0.2)), 0.5, 8.0)
    interface_stiffness = draw_interface_stiffness(jax.random.fold_in(splits[6], 71), 0)
    return {"eigvecs": eigvecs, "coupling": coupling, "mode_counts": mode_counts, "tree_segments": tree_segments, "eigvals": eigvals, "interface_stiffness": interface_stiffness}


def reference(eigvecs, coupling, mode_counts, tree_segments, eigvals, interface_stiffness):
    highest = lax.Precision.HIGHEST
    slot_ids = jnp.arange(MSLOT, dtype=jnp.int32)
    live = slot_ids[None, :] < mode_counts[:, None]
    pieces = jnp.einsum('sim,sitp->stmp', eigvecs.astype(jnp.float32), coupling.astype(jnp.float32), precision=highest)
    pieces = pieces * live.astype(jnp.float32)[:, None, :, None]
    seg_ids = jnp.arange(NSEG, dtype=jnp.int32)
    matches = (tree_segments[:, :, None] == seg_ids[None, None, :]).astype(jnp.float32)
    assembled = jnp.einsum('stg,stmp->smgp', matches, pieces, precision=highest).reshape(NMODE, NIF)
    diag_values = jnp.where(live, eigvals, 1.0).reshape(NMODE)
    factor = jnp.linalg.cholesky(interface_stiffness[:PANEL, :PANEL])
    low_ii = lax.linalg.triangular_solve(factor, interface_stiffness[:, :PANEL], left_side=False, lower=True, transpose_a=True)
    low_mi = lax.linalg.triangular_solve(factor, assembled[:, :PANEL], left_side=False, lower=True, transpose_a=True)
    contract = (((1,), (1,)), ((), ()))
    in_panel = jnp.arange(NIF, dtype=jnp.int32)[None, :] < PANEL
    padded_ii = jnp.pad(low_ii, ((0, 0), (0, NIF - PANEL)))
    padded_mi = jnp.pad(low_mi, ((0, 0), (0, NIF - PANEL)))
    reduced_ii = jnp.where(in_panel, padded_ii, interface_stiffness - lax.dot_general(low_ii, low_ii, contract, precision=highest))
    reduced_mi = jnp.where(in_panel, padded_mi, assembled - lax.dot_general(low_mi, low_ii, contract, precision=highest))
    positions = jnp.arange(NMODE, dtype=jnp.int32)
    reduced_mm = -lax.dot_general(low_mi, low_mi, contract, precision=highest)
    reduced_mm = reduced_mm.at[positions, positions].add(diag_values)
    return (reduced_ii, reduced_mi, reduced_mm)
```

```python
import jax
import jax.numpy as jnp
from jax import lax
from jax.sharding import PartitionSpec as P

MSLOT = 128
PANEL = 512
MOST = 2
SUB_ROW = 8

AXES = ("row", "col")


def dot_t(left, right, precision):
    contract = (((1,), (1,)), ((), ()))
    return lax.dot_general(left, right, contract, precision=precision)


def pick(index, options):
    out = options[0]
    for i in range(1, len(options)):
        out = jnp.where(index == i, options[i], out)
    return out


def seg0_slots(tseg, cap0):
    has0 = jnp.any(tseg == 0, axis=1)
    rank0 = jnp.cumsum(has0.astype(jnp.int32)) - 1
    slot = jnp.where(has0, rank0, cap0)
    return has0, rank0, slot


def per_device(eigvecs, coupling, mode_counts, tree_segments, eigvals, stiff):
    high = lax.Precision.HIGH
    R = lax.axis_size("row")
    C = lax.axis_size("col")
    r = lax.axis_index("row")
    c = lax.axis_index("col")
    nsub = eigvecs.shape[0]
    H, W = stiff.shape
    Ec = coupling.shape[3]
    G = W // PANEL
    ratio = R // C
    npair = 2 * nsub
    cap = min(MOST * G * ((nsub + SUB_ROW - 1) // SUB_ROW), npair)
    cap0 = min(MOST * ((nsub + SUB_ROW - 1) // SUB_ROW), nsub)

    live = jnp.arange(MSLOT, dtype=jnp.int32)[None, :] < mode_counts[:, None]
    pieces = jnp.einsum("sim,sitp->stmp", eigvecs, coupling, preferred_element_type=jnp.float32)
    pieces = pieces * live.astype(jnp.float32)[:, None, :, None]
    flat = pieces.reshape(npair, MSLOT, Ec)
    flat_pad = jnp.concatenate([flat, jnp.zeros((1, MSLOT, Ec), jnp.float32)], axis=0)

    tseg = tree_segments
    dest = (tseg // G).reshape(npair)
    onehot = dest[:, None] == jnp.arange(C, dtype=jnp.int32)[None, :]
    rank_pd = jnp.cumsum(onehot.astype(jnp.int32), axis=0) - 1
    rank = jnp.sum(jnp.where(onehot, rank_pd, 0), axis=1)
    match = onehot[:, :, None] & (rank_pd[:, :, None] == jnp.arange(cap, dtype=jnp.int32)[None, None, :])
    send_idx = jnp.where(jnp.any(match, axis=0), jnp.argmax(match, axis=0), npair)
    send = flat_pad[send_idx]
    recv = lax.all_to_all(send, "col", 0, 0, tiled=True)
    recv_pad = jnp.concatenate([recv, jnp.zeros((C, 1, MSLOT, Ec), jnp.float32)], axis=1)
    my_seg = c * G + jnp.arange(G, dtype=jnp.int32)
    seg_hit = tseg[:, :, None] == my_seg[None, None, :]
    rank2 = rank.reshape(nsub, 2)
    slot_tab = jnp.where(
        jnp.any(seg_hit, axis=1), jnp.sum(jnp.where(seg_hit, rank2[:, :, None], 0), axis=1), cap
    )
    gathered = recv_pad[:, slot_tab]
    block_mi = gathered.transpose(1, 3, 2, 0, 4).reshape(nsub * MSLOT, W)

    has0, rank0, slot_r = seg0_slots(tseg, cap0)
    t0 = jnp.where(tseg[:, 0] == 0, 0, 1)
    sel = has0[:, None] & (rank0[:, None] == jnp.arange(cap0, dtype=jnp.int32)[None, :])
    sel_sub = jnp.argmax(sel, axis=0)
    zidx = jnp.where(jnp.any(sel, axis=0), sel_sub * 2 + t0[sel_sub], npair)
    z_local = flat_pad[zidx]
    z_all = lax.all_gather(z_local, "col", axis=0, tiled=False)
    z_rows = z_all.transpose(1, 2, 0, 3).reshape(cap0 * MSLOT, C * Ec)

    kpp_src = stiff[:PANEL, :PANEL]
    rs = PANEL // R
    got = [kpp_src[:rs]]
    for i in range(1, R):
        got.append(lax.ppermute(kpp_src[i * rs:(i + 1) * rs], AXES, [(0, i * C)]))
    kpp_part = pick(r, got)
    kpp_col0 = lax.all_gather(kpp_part, "row", axis=0, tiled=True)
    cs = PANEL // C
    got = [kpp_col0[:cs]]
    for k in range(1, C):
        got.append(lax.ppermute(kpp_col0[k * cs:(k + 1) * cs], AXES, [(i * C, i * C + k) for i in range(R)]))
    kpp = lax.all_gather(pick(c, got), "col", axis=0, tiled=True)

    m_src = stiff[:, :PANEL]
    rps = W // R
    zps = cap0 * MSLOT // C
    got = [m_src[:rps]]
    for k in range(1, C):
        got.append(lax.ppermute(m_src[k * rps:(k + 1) * rps], AXES, [(i * C, i * C + k) for i in range(R)]))
    m_row = lax.all_gather(pick(c, got), "col", axis=0, tiled=True)
    got = []
    for k in range(C):
        payload = jnp.concatenate([m_src[k * rps:(k + 1) * rps], z_rows[k * zps:(k + 1) * zps]], axis=0)
        perm = [(i * C, ((i % ratio) * C + k) * C + i // ratio) for i in range(R)]
        got.append(lax.ppermute(payload, AXES, perm))
    col_parts = lax.all_gather(pick(r % C, got), "row", axis=0, tiled=False)
    m_col = col_parts[:, :rps].reshape(W, PANEL)
    z_col = col_parts[:, rps:].reshape(ratio * cap0 * MSLOT, PANEL)

    tseg_all = lax.all_gather(tseg, "row", axis=0, tiled=False)
    tseg_c = lax.dynamic_slice_in_dim(tseg_all, c * ratio, ratio, axis=0)
    slot_c = []
    for j in range(ratio):
        has_j, rank_j, _ = seg0_slots(tseg_c[j], cap0)
        slot_c.append(jnp.where(has_j, j * cap0 + rank_j, ratio * cap0))
    slot_c = jnp.concatenate(slot_c)

    factor = jnp.linalg.cholesky(kpp)
    stacked = jnp.concatenate([m_row, m_col, z_rows, z_col], axis=0)
    solved = lax.linalg.triangular_solve(factor, stacked, left_side=False, lower=True, transpose_a=True)
    low_r = solved[:H]
    low_c = solved[H:H + W]
    lowmi_r = solved[H + W:H + W + cap0 * MSLOT]
    lowmi_c = solved[H + W + cap0 * MSLOT:]

    col_ids = c * W + jnp.arange(W, dtype=jnp.int32)
    in_panel = col_ids[None, :] < PANEL
    reduced_ii = jnp.where(
        in_panel, jnp.pad(low_r, ((0, 0), (0, W - PANEL))), stiff - dot_t(low_r, low_c, high)
    )

    upd = dot_t(lowmi_r, low_c, high).reshape(cap0, MSLOT, W)
    upd = jnp.concatenate([upd, jnp.zeros((1, MSLOT, W), jnp.float32)], axis=0)
    upd_full = upd[slot_r].reshape(nsub * MSLOT, W)
    lmi = jnp.concatenate(
        [lowmi_r.reshape(cap0, MSLOT, PANEL), jnp.zeros((1, MSLOT, PANEL), jnp.float32)], axis=0
    )
    lmi_full = lmi[slot_r].reshape(nsub * MSLOT, PANEL)
    reduced_mi = jnp.where(
        in_panel, jnp.pad(lmi_full, ((0, 0), (0, W - PANEL))), block_mi - upd_full
    )

    nc = ratio * cap0
    vv = dot_t(lowmi_r, lowmi_c, high).reshape(cap0, MSLOT, nc, MSLOT)
    vv = jnp.pad(vv, ((0, 1), (0, 0), (0, 1), (0, 0)))
    vv_full = vv[slot_r][:, :, slot_c].reshape(nsub * MSLOT, ratio * nsub * MSLOT)
    diag_values = jnp.where(live, eigvals, 1.0).reshape(-1)
    mode_rows = diag_values.shape[0]
    mode_width = ratio * nsub * MSLOT
    row_ids = r * mode_rows + jnp.arange(mode_rows, dtype=jnp.int32)
    mode_cols = c * mode_width + jnp.arange(mode_width, dtype=jnp.int32)
    base_mm = jnp.where(row_ids[:, None] == mode_cols[None, :], diag_values[:, None], 0.0)
    reduced_mm = base_mm - vv_full
    return (reduced_ii, reduced_mi, reduced_mm)


def solution(mesh):
    in_specs = (
        P("row", None, None),
        P("row", None, None, "col"),
        P("row"),
        P("row", None),
        P("row", None),
        P("row", "col"),
    )
    out_specs = (P("row", "col"), P("row", "col"), P("row", "col"))
    return jax.shard_map(
        per_device, mesh=mesh, in_specs=in_specs, out_specs=out_specs, check_vma=False
    )
```

```python
import functools

import jax
import jax.numpy as jnp
from jax import lax
from jax.sharding import PartitionSpec as P
from jax.experimental import pallas as pl
from jax.experimental.pallas import tpu as pltpu

MSLOT = 128
PANEL = 512
MOST = 2
SUB_ROW = 8

AXES = ("row", "col")


def split_bf16(x):
    hi = lax.reduce_precision(x, exponent_bits=8, mantissa_bits=7)
    return hi.astype(jnp.bfloat16), (x - hi).astype(jnp.bfloat16)


def update_kernel(kind, tm, tn, flags_ref, info_ref, slots_ref, base_ref, a_ref, bhi_ref, blo_ref, out_ref):
    j = pl.program_id(0)
    i = pl.program_id(1)
    is_panel = (info_ref[0] == 1) & (info_ref[1] + j * tn == 0)
    active = jnp.logical_and(jnp.logical_not(is_panel), flags_ref[i] != 0)

    def base():
        if kind == "gather":
            return base_ref[0]
        if kind == "diag":
            rows = info_ref[2] + i * tm + lax.broadcasted_iota(jnp.int32, (tm, tn), 0)
            cols = info_ref[1] + j * tn + lax.broadcasted_iota(jnp.int32, (tm, tn), 1)
            return jnp.where(rows == cols, base_ref[...], 0.0)
        return base_ref[...]

    @pl.when(is_panel)
    def _():
        out_ref[...] = a_ref[...]

    @pl.when(active)
    def _():
        a = a_ref[...]
        a_hi = a.astype(jnp.bfloat16)
        a_lo = (a - a_hi.astype(jnp.float32)).astype(jnp.bfloat16)
        dn = (((1,), (1,)), ((), ()))
        b_hi = bhi_ref[...]
        acc = lax.dot_general(a_hi, b_hi, dn, preferred_element_type=jnp.float32)
        acc = acc + lax.dot_general(a_hi, blo_ref[...], dn, preferred_element_type=jnp.float32)
        acc = acc + lax.dot_general(a_lo, b_hi, dn, preferred_element_type=jnp.float32)
        out_ref[...] = base() - acc

    @pl.when(jnp.logical_and(jnp.logical_not(is_panel), flags_ref[i] == 0))
    def _():
        out_ref[...] = base()


def panel_update(kind, base, a, b, flags, info, slots, rows, width):
    tm, tn = MSLOT, PANEL
    b_hi, b_lo = split_bf16(b)
    if kind == "gather":
        nseg = width // tn
        base_spec = pl.BlockSpec((1, tm, tn), lambda j, i, f, n, s: (s[i * nseg + j], 0, 0))
    elif kind == "diag":
        base_spec = pl.BlockSpec((tm, 1), lambda j, i, f, n, s: (i, 0))
    else:
        base_spec = pl.BlockSpec((tm, tn), lambda j, i, f, n, s: (i, j))
    grid_spec = pltpu.PrefetchScalarGridSpec(
        num_scalar_prefetch=3,
        grid=(width // tn, rows // tm),
        in_specs=[
            base_spec,
            pl.BlockSpec((tm, PANEL), lambda j, i, f, n, s: (i, 0)),
            pl.BlockSpec((tn, PANEL), lambda j, i, f, n, s: (j, 0)),
            pl.BlockSpec((tn, PANEL), lambda j, i, f, n, s: (j, 0)),
        ],
        out_specs=pl.BlockSpec((tm, tn), lambda j, i, f, n, s: (i, j)),
    )
    flops = 6 * rows * width * PANEL
    cost = pl.CostEstimate(flops=flops, transcendentals=0, bytes_accessed=rows * width * 8 + width * PANEL * 4)
    return pl.pallas_call(
        functools.partial(update_kernel, kind, tm, tn),
        grid_spec=grid_spec,
        out_shape=jax.ShapeDtypeStruct((rows, width), jnp.float32),
        cost_estimate=cost,
    )(flags, info, slots, base, a, b_hi, b_lo)


def dot_t(left, right):
    contract = (((1,), (1,)), ((), ()))
    l_hi, l_lo = split_bf16(left)
    r_hi, r_lo = split_bf16(right)
    out = lax.dot_general(l_hi, r_hi, contract, preferred_element_type=jnp.float32)
    out = out + lax.dot_general(l_hi, r_lo, contract, preferred_element_type=jnp.float32)
    return out + lax.dot_general(l_lo, r_hi, contract, preferred_element_type=jnp.float32)


def pick(index, options):
    out = options[0]
    for i in range(1, len(options)):
        out = jnp.where(index == i, options[i], out)
    return out


def seg0_slots(tseg, cap0):
    has0 = jnp.any(tseg == 0, axis=1)
    rank0 = jnp.cumsum(has0.astype(jnp.int32)) - 1
    slot = jnp.where(has0, rank0, cap0)
    return has0, rank0, slot


def per_device(eigvecs, coupling, mode_counts, tree_segments, eigvals, stiff):
    R = lax.axis_size("row")
    C = lax.axis_size("col")
    r = lax.axis_index("row")
    c = lax.axis_index("col")
    nsub = eigvecs.shape[0]
    H, W = stiff.shape
    Ec = coupling.shape[3]
    G = W // PANEL
    ratio = R // C
    npair = 2 * nsub
    cap = min(MOST * G * ((nsub + SUB_ROW - 1) // SUB_ROW), npair)
    cap0 = min(MOST * ((nsub + SUB_ROW - 1) // SUB_ROW), nsub)

    live = jnp.arange(MSLOT, dtype=jnp.int32)[None, :] < mode_counts[:, None]
    pieces = jnp.einsum("sim,sitp->stmp", eigvecs, coupling, preferred_element_type=jnp.float32)
    pieces = pieces * live.astype(jnp.float32)[:, None, :, None]
    flat = pieces.reshape(npair, MSLOT, Ec)
    flat_pad = jnp.concatenate([flat, jnp.zeros((1, MSLOT, Ec), jnp.float32)], axis=0)

    tseg = tree_segments
    dest = (tseg // G).reshape(npair)
    onehot = dest[:, None] == jnp.arange(C, dtype=jnp.int32)[None, :]
    rank_pd = jnp.cumsum(onehot.astype(jnp.int32), axis=0) - 1
    rank = jnp.sum(jnp.where(onehot, rank_pd, 0), axis=1)
    match = onehot[:, :, None] & (rank_pd[:, :, None] == jnp.arange(cap, dtype=jnp.int32)[None, None, :])
    send_idx = jnp.where(jnp.any(match, axis=0), jnp.argmax(match, axis=0), npair)
    send = flat_pad[send_idx]
    shifted = [send[c]]
    for k in range(1, C):
        out_k = lax.dynamic_index_in_dim(send, (c + k) % C, axis=0, keepdims=False)
        shifted.append(lax.ppermute(out_k, "col", [(i, (i + k) % C) for i in range(C)]))
    shifted = jnp.stack(shifted)
    recv = shifted[(c - jnp.arange(C, dtype=jnp.int32)) % C]
    recv_t = recv.transpose(1, 2, 0, 3).reshape(cap, MSLOT, C * Ec)
    recv_t = jnp.concatenate([recv_t, jnp.zeros((1, MSLOT, PANEL), jnp.float32)], axis=0)
    my_seg = c * G + jnp.arange(G, dtype=jnp.int32)
    seg_hit = tseg[:, :, None] == my_seg[None, None, :]
    rank2 = rank.reshape(nsub, 2)
    slot_tab = jnp.where(
        jnp.any(seg_hit, axis=1), jnp.sum(jnp.where(seg_hit, rank2[:, :, None], 0), axis=1), cap
    )

    has0, rank0, slot_r = seg0_slots(tseg, cap0)
    t0 = jnp.where(tseg[:, 0] == 0, 0, 1)
    sel = has0[:, None] & (rank0[:, None] == jnp.arange(cap0, dtype=jnp.int32)[None, :])
    sel_sub = jnp.argmax(sel, axis=0)
    zidx = jnp.where(jnp.any(sel, axis=0), sel_sub * 2 + t0[sel_sub], npair)
    z_local = flat_pad[zidx]
    z_all = lax.all_gather(z_local, "col", axis=0, tiled=False)
    z_rows = z_all.transpose(1, 2, 0, 3).reshape(cap0 * MSLOT, C * Ec)

    kpp_src = stiff[:PANEL, :PANEL]
    rs = PANEL // R
    got = [kpp_src[:rs]]
    for i in range(1, R):
        got.append(lax.ppermute(kpp_src[i * rs:(i + 1) * rs], AXES, [(0, i * C)]))
    kpp_part = pick(r, got)
    kpp_col0 = lax.all_gather(kpp_part, "row", axis=0, tiled=True)
    cs = PANEL // C
    got = [kpp_col0[:cs]]
    for k in range(1, C):
        got.append(lax.ppermute(kpp_col0[k * cs:(k + 1) * cs], AXES, [(i * C, i * C + k) for i in range(R)]))
    kpp = lax.all_gather(pick(c, got), "col", axis=0, tiled=True)

    m_src = stiff[:, :PANEL]
    rps = W // R
    zps = cap0 * MSLOT // C
    got = [m_src[:rps]]
    for k in range(1, C):
        got.append(lax.ppermute(m_src[k * rps:(k + 1) * rps], AXES, [(i * C, i * C + k) for i in range(R)]))
    m_row = lax.all_gather(pick(c, got), "col", axis=0, tiled=True)
    got = []
    for k in range(C):
        payload = jnp.concatenate([m_src[k * rps:(k + 1) * rps], z_rows[k * zps:(k + 1) * zps]], axis=0)
        perm = [(i * C, ((i % ratio) * C + k) * C + i // ratio) for i in range(R)]
        got.append(lax.ppermute(payload, AXES, perm))
    col_parts = lax.all_gather(pick(r % C, got), "row", axis=0, tiled=False)
    m_col = col_parts[:, :rps].reshape(W, PANEL)
    z_col = col_parts[:, rps:].reshape(ratio * cap0 * MSLOT, PANEL)

    tseg_all = lax.all_gather(tseg, "row", axis=0, tiled=False)
    tseg_c = lax.dynamic_slice_in_dim(tseg_all, c * ratio, ratio, axis=0)
    slot_c = []
    for j in range(ratio):
        has_j, rank_j, _ = seg0_slots(tseg_c[j], cap0)
        slot_c.append(jnp.where(has_j, j * cap0 + rank_j, ratio * cap0))
    slot_c = jnp.concatenate(slot_c)

    factor = jnp.linalg.cholesky(kpp)
    eye = jnp.eye(PANEL, dtype=jnp.float32)
    finv = lax.linalg.triangular_solve(factor, eye, left_side=True, lower=True)
    stacked = jnp.concatenate([m_row, m_col, z_rows, z_col], axis=0)
    solved = dot_t(stacked, finv)
    low_r = solved[:H]
    low_c = solved[H:H + W]
    lowmi_r = solved[H + W:H + W + cap0 * MSLOT]
    lowmi_c = solved[H + W + cap0 * MSLOT:]

    ones = jnp.ones((H // MSLOT,), jnp.int32)
    none = jnp.zeros((1,), jnp.int32)
    info = jnp.stack([jnp.int32(1), c * W, r * H, jnp.int32(0)]).astype(jnp.int32)
    reduced_ii = panel_update("array", stiff, low_r, low_c, ones, info, none, H, W)

    lmi = jnp.concatenate(
        [lowmi_r.reshape(cap0, MSLOT, PANEL), jnp.zeros((1, MSLOT, PANEL), jnp.float32)], axis=0
    )
    lmi_full = lmi[slot_r].reshape(nsub * MSLOT, PANEL)
    flags = has0.astype(jnp.int32)
    reduced_mi = panel_update(
        "gather", recv_t, lmi_full, low_c, flags, info, slot_tab.reshape(-1).astype(jnp.int32), nsub * MSLOT, W
    )

    nc = ratio * cap0
    lmc = jnp.concatenate(
        [lowmi_c.reshape(nc, MSLOT, PANEL), jnp.zeros((1, MSLOT, PANEL), jnp.float32)], axis=0
    )
    mode_width = ratio * nsub * MSLOT
    lmc_full = lmc[slot_c].reshape(mode_width, PANEL)
    diag_values = jnp.where(live, eigvals, 1.0).reshape(-1, 1)
    mode_rows = diag_values.shape[0]
    info_mm = jnp.stack([jnp.int32(0), c * mode_width, r * mode_rows, jnp.int32(0)]).astype(jnp.int32)
    reduced_mm = panel_update("diag", diag_values, lmi_full, lmc_full, flags, info_mm, none, mode_rows, mode_width)
    return (reduced_ii, reduced_mi, reduced_mm)


def solution(mesh):
    in_specs = (
        P("row", None, None),
        P("row", None, None, "col"),
        P("row"),
        P("row", None),
        P("row", None),
        P("row", "col"),
    )
    out_specs = (P("row", "col"), P("row", "col"), P("row", "col"))
    return jax.shard_map(
        per_device, mesh=mesh, in_specs=in_specs, out_specs=out_specs, check_vma=False
    )
```

```python
import functools

import jax
import jax.numpy as jnp
from jax import lax
from jax.sharding import PartitionSpec as P
from jax.experimental import pallas as pl
from jax.experimental.pallas import tpu as pltpu

MSLOT = 128
PANEL = 512
MOST = 2
SUB_ROW = 8

AXES = ("row", "col")


def split_bf16(x):
    hi = lax.reduce_precision(x, exponent_bits=8, mantissa_bits=7)
    return hi.astype(jnp.bfloat16), (x - hi).astype(jnp.bfloat16)


def update_kernel(kind, tm, width, nbase, flags_ref, info_ref, slots_ref, *refs):
    base_refs = refs[:nbase]
    a_ref, bhi_ref, blo_ref, out_ref = refs[nbase:]
    i = pl.program_id(0)
    active = flags_ref[i] != 0

    def base_cols(g):
        cols = pl.ds(g * PANEL, PANEL)
        if kind == "gather":
            return base_refs[g][0]
        if kind == "diag":
            rows = info_ref[2] + i * tm + lax.broadcasted_iota(jnp.int32, (tm, PANEL), 0)
            ids = info_ref[1] + g * PANEL + lax.broadcasted_iota(jnp.int32, (tm, PANEL), 1)
            return jnp.where(rows == ids, base_refs[0][...], 0.0)
        return base_refs[0][:, cols]

    @pl.when(active)
    def _():
        a = a_ref[...]
        a_hi = a.astype(jnp.bfloat16)
        a_lo = (a - a_hi.astype(jnp.float32)).astype(jnp.bfloat16)
        dn = (((1,), (1,)), ((), ()))
        for g in range(width // PANEL):
            rows = pl.ds(g * PANEL, PANEL)
            b_hi = bhi_ref[rows, :]
            acc = lax.dot_general(a_hi, b_hi, dn, preferred_element_type=jnp.float32)
            acc = acc + lax.dot_general(a_hi, blo_ref[rows, :], dn, preferred_element_type=jnp.float32)
            acc = acc + lax.dot_general(a_lo, b_hi, dn, preferred_element_type=jnp.float32)
            out_ref[:, pl.ds(g * PANEL, PANEL)] = base_cols(g) - acc

    @pl.when(jnp.logical_not(active))
    def _():
        for g in range(width // PANEL):
            out_ref[:, pl.ds(g * PANEL, PANEL)] = base_cols(g)

    @pl.when((info_ref[0] == 1) & (info_ref[1] == 0))
    def _():
        out_ref[:, pl.ds(0, PANEL)] = a_ref[...]


def panel_update(kind, base, a, b, flags, info, slots, rows, width):
    tm = MSLOT
    b_hi, b_lo = split_bf16(b)
    nseg = width // PANEL
    if kind == "gather":
        bases = [base] * nseg
        base_specs = [
            pl.BlockSpec((1, tm, PANEL), lambda i, f, n, s, g=g: (s[i * nseg + g], 0, 0)) for g in range(nseg)
        ]
    elif kind == "diag":
        bases = [base]
        base_specs = [pl.BlockSpec((tm, 1), lambda i, f, n, s: (i, 0))]
    else:
        bases = [base]
        base_specs = [pl.BlockSpec((tm, width), lambda i, f, n, s: (i, 0))]
    grid_spec = pltpu.PrefetchScalarGridSpec(
        num_scalar_prefetch=3,
        grid=(rows // tm,),
        in_specs=base_specs + [
            pl.BlockSpec((tm, PANEL), lambda i, f, n, s: (i, 0)),
            pl.BlockSpec((width, PANEL), lambda i, f, n, s: (0, 0)),
            pl.BlockSpec((width, PANEL), lambda i, f, n, s: (0, 0)),
        ],
        out_specs=pl.BlockSpec((tm, width), lambda i, f, n, s: (i, 0)),
    )
    flops = 6 * rows * width * PANEL
    cost = pl.CostEstimate(flops=flops, transcendentals=0, bytes_accessed=rows * width * 8 + width * PANEL * 4)
    return pl.pallas_call(
        functools.partial(update_kernel, kind, tm, width, len(bases)),
        grid_spec=grid_spec,
        out_shape=jax.ShapeDtypeStruct((rows, width), jnp.float32),
        cost_estimate=cost,
        compiler_params=pltpu.CompilerParams(vmem_limit_bytes=48 * 1024 * 1024),
    )(flags, info, slots, *bases, a, b_hi, b_lo)


def dot_t(left, right):
    contract = (((1,), (1,)), ((), ()))
    l_hi, l_lo = split_bf16(left)
    r_hi, r_lo = split_bf16(right)
    out = lax.dot_general(l_hi, r_hi, contract, preferred_element_type=jnp.float32)
    out = out + lax.dot_general(l_hi, r_lo, contract, preferred_element_type=jnp.float32)
    return out + lax.dot_general(l_lo, r_hi, contract, preferred_element_type=jnp.float32)


def pick(index, options):
    out = options[0]
    for i in range(1, len(options)):
        out = jnp.where(index == i, options[i], out)
    return out


def seg0_slots(tseg, cap0):
    has0 = jnp.any(tseg == 0, axis=1)
    rank0 = jnp.cumsum(has0.astype(jnp.int32)) - 1
    slot = jnp.where(has0, rank0, cap0)
    return has0, rank0, slot


def per_device(eigvecs, coupling, mode_counts, tree_segments, eigvals, stiff):
    R = lax.axis_size("row")
    C = lax.axis_size("col")
    r = lax.axis_index("row")
    c = lax.axis_index("col")
    nsub = eigvecs.shape[0]
    H, W = stiff.shape
    Ec = coupling.shape[3]
    G = W // PANEL
    ratio = R // C
    npair = 2 * nsub
    cap = min(MOST * G * ((nsub + SUB_ROW - 1) // SUB_ROW), npair)
    cap0 = min(MOST * ((nsub + SUB_ROW - 1) // SUB_ROW), nsub)

    live = jnp.arange(MSLOT, dtype=jnp.int32)[None, :] < mode_counts[:, None]
    pieces = jnp.einsum("sim,sitp->stmp", eigvecs, coupling, preferred_element_type=jnp.float32)
    pieces = pieces * live.astype(jnp.float32)[:, None, :, None]
    flat = pieces.reshape(npair, MSLOT, Ec)
    flat_pad = jnp.concatenate([flat, jnp.zeros((1, MSLOT, Ec), jnp.float32)], axis=0)

    tseg = tree_segments
    dest = (tseg // G).reshape(npair)
    onehot = dest[:, None] == jnp.arange(C, dtype=jnp.int32)[None, :]
    rank_pd = jnp.cumsum(onehot.astype(jnp.int32), axis=0) - 1
    rank = jnp.sum(jnp.where(onehot, rank_pd, 0), axis=1)
    match = onehot[:, :, None] & (rank_pd[:, :, None] == jnp.arange(cap, dtype=jnp.int32)[None, None, :])
    send_idx = jnp.where(jnp.any(match, axis=0), jnp.argmax(match, axis=0), npair)
    send = flat_pad[send_idx]
    shifted = [send[c]]
    for k in range(1, C):
        out_k = lax.dynamic_index_in_dim(send, (c + k) % C, axis=0, keepdims=False)
        shifted.append(lax.ppermute(out_k, "col", [(i, (i + k) % C) for i in range(C)]))
    shifted = jnp.stack(shifted)
    recv = shifted[(c - jnp.arange(C, dtype=jnp.int32)) % C]
    recv_t = recv.transpose(1, 2, 0, 3).reshape(cap, MSLOT, C * Ec)
    recv_t = jnp.concatenate([recv_t, jnp.zeros((1, MSLOT, PANEL), jnp.float32)], axis=0)
    my_seg = c * G + jnp.arange(G, dtype=jnp.int32)
    seg_hit = tseg[:, :, None] == my_seg[None, None, :]
    rank2 = rank.reshape(nsub, 2)
    slot_tab = jnp.where(
        jnp.any(seg_hit, axis=1), jnp.sum(jnp.where(seg_hit, rank2[:, :, None], 0), axis=1), cap
    )

    has0, rank0, slot_r = seg0_slots(tseg, cap0)
    t0 = jnp.where(tseg[:, 0] == 0, 0, 1)
    sel = has0[:, None] & (rank0[:, None] == jnp.arange(cap0, dtype=jnp.int32)[None, :])
    sel_sub = jnp.argmax(sel, axis=0)
    zidx = jnp.where(jnp.any(sel, axis=0), sel_sub * 2 + t0[sel_sub], npair)
    z_local = flat_pad[zidx]
    z_all = lax.all_gather(z_local, "col", axis=0, tiled=False)
    z_rows = z_all.transpose(1, 2, 0, 3).reshape(cap0 * MSLOT, C * Ec)

    kpp_src = stiff[:PANEL, :PANEL]
    rs = PANEL // R
    got = [kpp_src[:rs]]
    for i in range(1, R):
        got.append(lax.ppermute(kpp_src[i * rs:(i + 1) * rs], AXES, [(0, i * C)]))
    kpp_part = pick(r, got)
    kpp_col0 = lax.all_gather(kpp_part, "row", axis=0, tiled=True)
    cs = PANEL // C
    got = [kpp_col0[:cs]]
    for k in range(1, C):
        got.append(lax.ppermute(kpp_col0[k * cs:(k + 1) * cs], AXES, [(i * C, i * C + k) for i in range(R)]))
    kpp = lax.all_gather(pick(c, got), "col", axis=0, tiled=True)

    m_src = stiff[:, :PANEL]
    rps = W // R
    zps = cap0 * MSLOT // C
    got = [m_src[:rps]]
    for k in range(1, C):
        got.append(lax.ppermute(m_src[k * rps:(k + 1) * rps], AXES, [(i * C, i * C + k) for i in range(R)]))
    m_row = lax.all_gather(pick(c, got), "col", axis=0, tiled=True)
    got = []
    for k in range(C):
        payload = jnp.concatenate([m_src[k * rps:(k + 1) * rps], z_rows[k * zps:(k + 1) * zps]], axis=0)
        perm = [(i * C, ((i % ratio) * C + k) * C + i // ratio) for i in range(R)]
        got.append(lax.ppermute(payload, AXES, perm))
    col_parts = lax.all_gather(pick(r % C, got), "row", axis=0, tiled=False)
    m_col = col_parts[:, :rps].reshape(W, PANEL)
    z_col = col_parts[:, rps:].reshape(ratio * cap0 * MSLOT, PANEL)

    tseg_all = lax.all_gather(tseg, "row", axis=0, tiled=False)
    tseg_c = lax.dynamic_slice_in_dim(tseg_all, c * ratio, ratio, axis=0)
    slot_c = []
    for j in range(ratio):
        has_j, rank_j, _ = seg0_slots(tseg_c[j], cap0)
        slot_c.append(jnp.where(has_j, j * cap0 + rank_j, ratio * cap0))
    slot_c = jnp.concatenate(slot_c)

    factor = jnp.linalg.cholesky(kpp)
    eye = jnp.eye(PANEL, dtype=jnp.float32)
    finv = lax.linalg.triangular_solve(factor, eye, left_side=True, lower=True)
    stacked = jnp.concatenate([m_row, m_col, z_rows, z_col], axis=0)
    solved = dot_t(stacked, finv)
    low_r = solved[:H]
    low_c = solved[H:H + W]
    lowmi_r = solved[H + W:H + W + cap0 * MSLOT]
    lowmi_c = solved[H + W + cap0 * MSLOT:]

    ones = jnp.ones((H // MSLOT,), jnp.int32)
    none = jnp.zeros((1,), jnp.int32)
    info = jnp.stack([jnp.int32(1), c * W, r * H, jnp.int32(0)]).astype(jnp.int32)
    reduced_ii = panel_update("array", stiff, low_r, low_c, ones, info, none, H, W)

    lmi = jnp.concatenate(
        [lowmi_r.reshape(cap0, MSLOT, PANEL), jnp.zeros((1, MSLOT, PANEL), jnp.float32)], axis=0
    )
    lmi_full = lmi[slot_r].reshape(nsub * MSLOT, PANEL)
    flags = has0.astype(jnp.int32)
    reduced_mi = panel_update(
        "gather", recv_t, lmi_full, low_c, flags, info, slot_tab.reshape(-1).astype(jnp.int32), nsub * MSLOT, W
    )

    nc = ratio * cap0
    lmc = jnp.concatenate(
        [lowmi_c.reshape(nc, MSLOT, PANEL), jnp.zeros((1, MSLOT, PANEL), jnp.float32)], axis=0
    )
    mode_width = ratio * nsub * MSLOT
    lmc_full = lmc[slot_c].reshape(mode_width, PANEL)
    diag_values = jnp.where(live, eigvals, 1.0).reshape(-1, 1)
    mode_rows = diag_values.shape[0]
    info_mm = jnp.stack([jnp.int32(0), c * mode_width, r * mode_rows, jnp.int32(0)]).astype(jnp.int32)
    reduced_mm = panel_update("diag", diag_values, lmi_full, lmc_full, flags, info_mm, none, mode_rows, mode_width)
    return (reduced_ii, reduced_mi, reduced_mm)


def solution(mesh):
    in_specs = (
        P("row", None, None),
        P("row", None, None, "col"),
        P("row"),
        P("row", None),
        P("row", None),
        P("row", "col"),
    )
    out_specs = (P("row", "col"), P("row", "col"), P("row", "col"))
    return jax.shard_map(
        per_device, mesh=mesh, in_specs=in_specs, out_specs=out_specs, check_vma=False
    )
```

```python
import functools

import jax
import jax.numpy as jnp
from jax import lax
from jax.sharding import PartitionSpec as P
from jax.experimental import pallas as pl
from jax.experimental.pallas import tpu as pltpu

MSLOT = 128
PANEL = 512
MOST = 2
SUB_ROW = 8

AXES = ("row", "col")
LEAF = 128


def mm3(a, b, dn):
    a_hi = a.astype(jnp.bfloat16)
    a_lo = (a - a_hi.astype(jnp.float32)).astype(jnp.bfloat16)
    b_hi = b.astype(jnp.bfloat16)
    b_lo = (b - b_hi.astype(jnp.float32)).astype(jnp.bfloat16)
    out = lax.dot_general(a_hi, b_hi, dn, preferred_element_type=jnp.float32)
    out = out + lax.dot_general(a_hi, b_lo, dn, preferred_element_type=jnp.float32)
    return out + lax.dot_general(a_lo, b_hi, dn, preferred_element_type=jnp.float32)


NN = (((1,), (0,)), ((), ()))
NT = (((1,), (1,)), ((), ()))


def leaf_inverse(d):
    n = d.shape[0]
    sub = lax.broadcasted_iota(jnp.int32, (n, n), 0)
    lane = lax.broadcasted_iota(jnp.int32, (n, n), 1)
    sub_c = lax.broadcasted_iota(jnp.int32, (n, 1), 0)
    lane_r = lax.broadcasted_iota(jnp.int32, (1, n), 1)
    eye = jnp.where(sub == lane, 1.0, 0.0).astype(jnp.float32)

    def step(k, carry):
        dm, em, xm = carry
        colk = jnp.sum(jnp.where(lane == k, dm, 0.0), axis=1, keepdims=True)
        rowk = jnp.sum(jnp.where(sub == k, dm, 0.0), axis=0, keepdims=True)
        dkk = jnp.sum(jnp.where(lane_r == k, rowk, 0.0), axis=1, keepdims=True)
        s = 1.0 / jnp.sqrt(dkk)
        lc = jnp.where(sub_c > k, colk * s, 0.0)
        lr = jnp.where(lane_r > k, rowk * s, 0.0)
        dm = dm - lc * lr
        erow = jnp.sum(jnp.where(sub == k, em, 0.0), axis=0, keepdims=True)
        xk = erow * s
        xm = jnp.where(sub == k, xk, xm)
        em = em - lc * xk
        return dm, em, xm

    _, _, xm = lax.fori_loop(0, n, step, (d, eye, jnp.zeros_like(d)))
    return xm


def chol_inv_kernel(a_ref, x_ref, w_ref, l_ref):
    n = a_ref.shape[0]
    nb = n // LEAF
    w_ref[...] = a_ref[...]
    for kb in range(nb):
        o = kb * LEAF
        blk = pl.ds(o, LEAF)
        xkk = leaf_inverse(w_ref[blk, blk])
        x_ref[blk, blk] = xkk
        if kb + 1 < nb:
            rest = pl.ds(o + LEAF, n - o - LEAF)
            panel = mm3(w_ref[rest, blk], xkk, NT)
            l_ref[rest, blk] = panel
            w_ref[rest, rest] = w_ref[rest, rest] - mm3(panel, panel, NT)
    for i in range(1, nb):
        bi = pl.ds(i * LEAF, LEAF)
        xii = x_ref[bi, bi]
        for j in range(i):
            bj = pl.ds(j * LEAF, LEAF)
            acc = None
            for k in range(j, i):
                bk = pl.ds(k * LEAF, LEAF)
                term = mm3(l_ref[bi, bk], x_ref[bk, bj], NN)
                acc = term if acc is None else acc + term
            x_ref[bi, bj] = -mm3(xii, acc, NN)
        for j in range(i + 1, nb):
            x_ref[bi, pl.ds(j * LEAF, LEAF)] = jnp.zeros((LEAF, LEAF), jnp.float32)
    x_ref[pl.ds(0, LEAF), pl.ds(LEAF, n - LEAF)] = jnp.zeros((LEAF, n - LEAF), jnp.float32)


def chol_inverse(a):
    n = a.shape[0]
    return pl.pallas_call(
        chol_inv_kernel,
        out_shape=jax.ShapeDtypeStruct((n, n), jnp.float32),
        in_specs=[pl.BlockSpec(memory_space=pltpu.VMEM)],
        out_specs=pl.BlockSpec(memory_space=pltpu.VMEM),
        scratch_shapes=[pltpu.VMEM((n, n), jnp.float32), pltpu.VMEM((n, n), jnp.float32)],
    )(a)


def split_bf16(x):
    hi = lax.reduce_precision(x, exponent_bits=8, mantissa_bits=7)
    return hi.astype(jnp.bfloat16), (x - hi).astype(jnp.bfloat16)


def update_kernel(kind, tm, width, nbase, flags_ref, info_ref, slots_ref, *refs):
    base_refs = refs[:nbase]
    a_ref, bhi_ref, blo_ref, out_ref = refs[nbase:]
    i = pl.program_id(0)
    active = flags_ref[i] != 0

    def base_cols(g):
        cols = pl.ds(g * PANEL, PANEL)
        if kind == "gather":
            return base_refs[g][0]
        if kind == "diag":
            rows = info_ref[2] + i * tm + lax.broadcasted_iota(jnp.int32, (tm, PANEL), 0)
            ids = info_ref[1] + g * PANEL + lax.broadcasted_iota(jnp.int32, (tm, PANEL), 1)
            return jnp.where(rows == ids, base_refs[0][...], 0.0)
        return base_refs[0][:, cols]

    @pl.when(active)
    def _():
        a = a_ref[...]
        a_hi = a.astype(jnp.bfloat16)
        a_lo = (a - a_hi.astype(jnp.float32)).astype(jnp.bfloat16)
        dn = (((1,), (1,)), ((), ()))
        for g in range(width // PANEL):
            rows = pl.ds(g * PANEL, PANEL)
            b_hi = bhi_ref[rows, :]
            acc = lax.dot_general(a_hi, b_hi, dn, preferred_element_type=jnp.float32)
            acc = acc + lax.dot_general(a_hi, blo_ref[rows, :], dn, preferred_element_type=jnp.float32)
            acc = acc + lax.dot_general(a_lo, b_hi, dn, preferred_element_type=jnp.float32)
            out_ref[:, pl.ds(g * PANEL, PANEL)] = base_cols(g) - acc

    @pl.when(jnp.logical_not(active))
    def _():
        for g in range(width // PANEL):
            out_ref[:, pl.ds(g * PANEL, PANEL)] = base_cols(g)

    @pl.when((info_ref[0] == 1) & (info_ref[1] == 0))
    def _():
        out_ref[:, pl.ds(0, PANEL)] = a_ref[...]


def panel_update(kind, base, a, b, flags, info, slots, rows, width):
    tm = MSLOT
    b_hi, b_lo = split_bf16(b)
    nseg = width // PANEL
    if kind == "gather":
        bases = [base] * nseg
        base_specs = [
            pl.BlockSpec((1, tm, PANEL), lambda i, f, n, s, g=g: (s[i * nseg + g], 0, 0)) for g in range(nseg)
        ]
    elif kind == "diag":
        bases = [base]
        base_specs = [pl.BlockSpec((tm, 1), lambda i, f, n, s: (i, 0))]
    else:
        bases = [base]
        base_specs = [pl.BlockSpec((tm, width), lambda i, f, n, s: (i, 0))]
    grid_spec = pltpu.PrefetchScalarGridSpec(
        num_scalar_prefetch=3,
        grid=(rows // tm,),
        in_specs=base_specs + [
            pl.BlockSpec((tm, PANEL), lambda i, f, n, s: (i, 0)),
            pl.BlockSpec((width, PANEL), lambda i, f, n, s: (0, 0)),
            pl.BlockSpec((width, PANEL), lambda i, f, n, s: (0, 0)),
        ],
        out_specs=pl.BlockSpec((tm, width), lambda i, f, n, s: (i, 0)),
    )
    flops = 6 * rows * width * PANEL
    cost = pl.CostEstimate(flops=flops, transcendentals=0, bytes_accessed=rows * width * 8 + width * PANEL * 4)
    return pl.pallas_call(
        functools.partial(update_kernel, kind, tm, width, len(bases)),
        grid_spec=grid_spec,
        out_shape=jax.ShapeDtypeStruct((rows, width), jnp.float32),
        cost_estimate=cost,
        compiler_params=pltpu.CompilerParams(vmem_limit_bytes=48 * 1024 * 1024),
    )(flags, info, slots, *bases, a, b_hi, b_lo)


def dot_t(left, right):
    contract = (((1,), (1,)), ((), ()))
    l_hi, l_lo = split_bf16(left)
    r_hi, r_lo = split_bf16(right)
    out = lax.dot_general(l_hi, r_hi, contract, preferred_element_type=jnp.float32)
    out = out + lax.dot_general(l_hi, r_lo, contract, preferred_element_type=jnp.float32)
    return out + lax.dot_general(l_lo, r_hi, contract, preferred_element_type=jnp.float32)


def pick(index, options):
    out = options[0]
    for i in range(1, len(options)):
        out = jnp.where(index == i, options[i], out)
    return out


def seg0_slots(tseg, cap0):
    has0 = jnp.any(tseg == 0, axis=1)
    rank0 = jnp.cumsum(has0.astype(jnp.int32)) - 1
    slot = jnp.where(has0, rank0, cap0)
    return has0, rank0, slot


def per_device(eigvecs, coupling, mode_counts, tree_segments, eigvals, stiff):
    R = lax.axis_size("row")
    C = lax.axis_size("col")
    r = lax.axis_index("row")
    c = lax.axis_index("col")
    nsub = eigvecs.shape[0]
    H, W = stiff.shape
    Ec = coupling.shape[3]
    G = W // PANEL
    ratio = R // C
    npair = 2 * nsub
    cap = min(MOST * G * ((nsub + SUB_ROW - 1) // SUB_ROW), npair)
    cap0 = min(MOST * ((nsub + SUB_ROW - 1) // SUB_ROW), nsub)

    live = jnp.arange(MSLOT, dtype=jnp.int32)[None, :] < mode_counts[:, None]
    pieces = jnp.einsum("sim,sitp->stmp", eigvecs, coupling, preferred_element_type=jnp.float32)
    pieces = pieces * live.astype(jnp.float32)[:, None, :, None]
    flat = pieces.reshape(npair, MSLOT, Ec)
    flat_pad = jnp.concatenate([flat, jnp.zeros((1, MSLOT, Ec), jnp.float32)], axis=0)

    tseg = tree_segments
    dest = (tseg // G).reshape(npair)
    onehot = dest[:, None] == jnp.arange(C, dtype=jnp.int32)[None, :]
    rank_pd = jnp.cumsum(onehot.astype(jnp.int32), axis=0) - 1
    rank = jnp.sum(jnp.where(onehot, rank_pd, 0), axis=1)
    match = onehot[:, :, None] & (rank_pd[:, :, None] == jnp.arange(cap, dtype=jnp.int32)[None, None, :])
    send_idx = jnp.where(jnp.any(match, axis=0), jnp.argmax(match, axis=0), npair)
    send = flat_pad[send_idx]
    shifted = [send[c]]
    for k in range(1, C):
        out_k = lax.dynamic_index_in_dim(send, (c + k) % C, axis=0, keepdims=False)
        shifted.append(lax.ppermute(out_k, "col", [(i, (i + k) % C) for i in range(C)]))
    shifted = jnp.stack(shifted)
    recv = shifted[(c - jnp.arange(C, dtype=jnp.int32)) % C]
    recv_t = recv.transpose(1, 2, 0, 3).reshape(cap, MSLOT, C * Ec)
    recv_t = jnp.concatenate([recv_t, jnp.zeros((1, MSLOT, PANEL), jnp.float32)], axis=0)
    my_seg = c * G + jnp.arange(G, dtype=jnp.int32)
    seg_hit = tseg[:, :, None] == my_seg[None, None, :]
    rank2 = rank.reshape(nsub, 2)
    slot_tab = jnp.where(
        jnp.any(seg_hit, axis=1), jnp.sum(jnp.where(seg_hit, rank2[:, :, None], 0), axis=1), cap
    )

    has0, rank0, slot_r = seg0_slots(tseg, cap0)
    t0 = jnp.where(tseg[:, 0] == 0, 0, 1)
    sel = has0[:, None] & (rank0[:, None] == jnp.arange(cap0, dtype=jnp.int32)[None, :])
    sel_sub = jnp.argmax(sel, axis=0)
    zidx = jnp.where(jnp.any(sel, axis=0), sel_sub * 2 + t0[sel_sub], npair)
    z_local = flat_pad[zidx]
    z_all = lax.all_gather(z_local, "col", axis=0, tiled=False)
    z_rows = z_all.transpose(1, 2, 0, 3).reshape(cap0 * MSLOT, C * Ec)

    kpp_src = stiff[:PANEL, :PANEL]
    rs = PANEL // R
    got = [kpp_src[:rs]]
    for i in range(1, R):
        got.append(lax.ppermute(kpp_src[i * rs:(i + 1) * rs], AXES, [(0, i * C)]))
    kpp_part = pick(r, got)
    kpp_col0 = lax.all_gather(kpp_part, "row", axis=0, tiled=True)
    cs = PANEL // C
    got = [kpp_col0[:cs]]
    for k in range(1, C):
        got.append(lax.ppermute(kpp_col0[k * cs:(k + 1) * cs], AXES, [(i * C, i * C + k) for i in range(R)]))
    kpp = lax.all_gather(pick(c, got), "col", axis=0, tiled=True)

    m_src = stiff[:, :PANEL]
    rps = W // R
    zps = cap0 * MSLOT // C
    got = [m_src[:rps]]
    for k in range(1, C):
        got.append(lax.ppermute(m_src[k * rps:(k + 1) * rps], AXES, [(i * C, i * C + k) for i in range(R)]))
    m_row = lax.all_gather(pick(c, got), "col", axis=0, tiled=True)
    got = []
    for k in range(C):
        payload = jnp.concatenate([m_src[k * rps:(k + 1) * rps], z_rows[k * zps:(k + 1) * zps]], axis=0)
        perm = [(i * C, ((i % ratio) * C + k) * C + i // ratio) for i in range(R)]
        got.append(lax.ppermute(payload, AXES, perm))
    col_parts = lax.all_gather(pick(r % C, got), "row", axis=0, tiled=False)
    m_col = col_parts[:, :rps].reshape(W, PANEL)
    z_col = col_parts[:, rps:].reshape(ratio * cap0 * MSLOT, PANEL)

    tseg_all = lax.all_gather(tseg, "row", axis=0, tiled=False)
    tseg_c = lax.dynamic_slice_in_dim(tseg_all, c * ratio, ratio, axis=0)
    slot_c = []
    for j in range(ratio):
        has_j, rank_j, _ = seg0_slots(tseg_c[j], cap0)
        slot_c.append(jnp.where(has_j, j * cap0 + rank_j, ratio * cap0))
    slot_c = jnp.concatenate(slot_c)

    finv = chol_inverse(kpp)
    stacked = jnp.concatenate([m_row, m_col, z_rows, z_col], axis=0)
    solved = dot_t(stacked, finv)
    low_r = solved[:H]
    low_c = solved[H:H + W]
    lowmi_r = solved[H + W:H + W + cap0 * MSLOT]
    lowmi_c = solved[H + W + cap0 * MSLOT:]

    ones = jnp.ones((H // MSLOT,), jnp.int32)
    none = jnp.zeros((1,), jnp.int32)
    info = jnp.stack([jnp.int32(1), c * W, r * H, jnp.int32(0)]).astype(jnp.int32)
    reduced_ii = panel_update("array", stiff, low_r, low_c, ones, info, none, H, W)

    lmi = jnp.concatenate(
        [lowmi_r.reshape(cap0, MSLOT, PANEL), jnp.zeros((1, MSLOT, PANEL), jnp.float32)], axis=0
    )
    lmi_full = lmi[slot_r].reshape(nsub * MSLOT, PANEL)
    flags = has0.astype(jnp.int32)
    reduced_mi = panel_update(
        "gather", recv_t, lmi_full, low_c, flags, info, slot_tab.reshape(-1).astype(jnp.int32), nsub * MSLOT, W
    )

    nc = ratio * cap0
    lmc = jnp.concatenate(
        [lowmi_c.reshape(nc, MSLOT, PANEL), jnp.zeros((1, MSLOT, PANEL), jnp.float32)], axis=0
    )
    mode_width = ratio * nsub * MSLOT
    lmc_full = lmc[slot_c].reshape(mode_width, PANEL)
    diag_values = jnp.where(live, eigvals, 1.0).reshape(-1, 1)
    mode_rows = diag_values.shape[0]
    info_mm = jnp.stack([jnp.int32(0), c * mode_width, r * mode_rows, jnp.int32(0)]).astype(jnp.int32)
    reduced_mm = panel_update("diag", diag_values, lmi_full, lmc_full, flags, info_mm, none, mode_rows, mode_width)
    return (reduced_ii, reduced_mi, reduced_mm)


def solution(mesh):
    in_specs = (
        P("row", None, None),
        P("row", None, None, "col"),
        P("row"),
        P("row", None),
        P("row", None),
        P("row", "col"),
    )
    out_specs = (P("row", "col"), P("row", "col"), P("row", "col"))
    return jax.shard_map(
        per_device, mesh=mesh, in_specs=in_specs, out_specs=out_specs, check_vma=False
    )
```

```python
import functools

import jax
import jax.numpy as jnp
from jax import lax
from jax.sharding import PartitionSpec as P
from jax.experimental import pallas as pl
from jax.experimental.pallas import tpu as pltpu

MSLOT = 128
PANEL = 512
MOST = 2
SUB_ROW = 8

AXES = ("row", "col")
LEAF = 128


def mm3(a, b, dn):
    a_hi = a.astype(jnp.bfloat16)
    a_lo = (a - a_hi.astype(jnp.float32)).astype(jnp.bfloat16)
    b_hi = b.astype(jnp.bfloat16)
    b_lo = (b - b_hi.astype(jnp.float32)).astype(jnp.bfloat16)
    out = lax.dot_general(a_hi, b_hi, dn, preferred_element_type=jnp.float32)
    out = out + lax.dot_general(a_hi, b_lo, dn, preferred_element_type=jnp.float32)
    return out + lax.dot_general(a_lo, b_hi, dn, preferred_element_type=jnp.float32)


NN = (((1,), (0,)), ((), ()))
NT = (((1,), (1,)), ((), ()))


def leaf_inverse(d):
    n = d.shape[0]
    sub = lax.broadcasted_iota(jnp.int32, (n, n), 0)
    lane = lax.broadcasted_iota(jnp.int32, (n, n), 1)
    sub_c = lax.broadcasted_iota(jnp.int32, (n, 1), 0)
    lane_r = lax.broadcasted_iota(jnp.int32, (1, n), 1)
    eye = jnp.where(sub == lane, 1.0, 0.0).astype(jnp.float32)

    def step(k, carry):
        dm, em, xm = carry
        colk = jnp.sum(jnp.where(lane == k, dm, 0.0), axis=1, keepdims=True)
        rowk = jnp.sum(jnp.where(sub == k, dm, 0.0), axis=0, keepdims=True)
        dkk = jnp.sum(jnp.where(lane_r == k, rowk, 0.0), axis=1, keepdims=True)
        s = 1.0 / jnp.sqrt(dkk)
        lc = jnp.where(sub_c > k, colk * s, 0.0)
        lr = jnp.where(lane_r > k, rowk * s, 0.0)
        dm = dm - lc * lr
        erow = jnp.sum(jnp.where(sub == k, em, 0.0), axis=0, keepdims=True)
        xk = erow * s
        xm = jnp.where(sub == k, xk, xm)
        em = em - lc * xk
        return dm, em, xm

    _, _, xm = lax.fori_loop(0, n, step, (d, eye, jnp.zeros_like(d)))
    return xm


def chol_inv_kernel(a_ref, x_ref, w_ref, l_ref):
    n = a_ref.shape[0]
    nb = n // LEAF
    w_ref[...] = a_ref[...]
    for kb in range(nb):
        o = kb * LEAF
        blk = pl.ds(o, LEAF)
        xkk = leaf_inverse(w_ref[blk, blk])
        x_ref[blk, blk] = xkk
        if kb + 1 < nb:
            rest = pl.ds(o + LEAF, n - o - LEAF)
            panel = mm3(w_ref[rest, blk], xkk, NT)
            l_ref[rest, blk] = panel
            w_ref[rest, rest] = w_ref[rest, rest] - mm3(panel, panel, NT)
    for i in range(1, nb):
        bi = pl.ds(i * LEAF, LEAF)
        xii = x_ref[bi, bi]
        for j in range(i):
            bj = pl.ds(j * LEAF, LEAF)
            acc = None
            for k in range(j, i):
                bk = pl.ds(k * LEAF, LEAF)
                term = mm3(l_ref[bi, bk], x_ref[bk, bj], NN)
                acc = term if acc is None else acc + term
            x_ref[bi, bj] = -mm3(xii, acc, NN)
        for j in range(i + 1, nb):
            x_ref[bi, pl.ds(j * LEAF, LEAF)] = jnp.zeros((LEAF, LEAF), jnp.float32)
    x_ref[pl.ds(0, LEAF), pl.ds(LEAF, n - LEAF)] = jnp.zeros((LEAF, n - LEAF), jnp.float32)


def chol_inverse(a):
    n = a.shape[0]
    return pl.pallas_call(
        chol_inv_kernel,
        out_shape=jax.ShapeDtypeStruct((n, n), jnp.float32),
        cost_estimate=pl.CostEstimate(flops=60 * n ** 3, transcendentals=n, bytes_accessed=8 * n * n),
        in_specs=[pl.BlockSpec(memory_space=pltpu.VMEM)],
        out_specs=pl.BlockSpec(memory_space=pltpu.VMEM),
        scratch_shapes=[pltpu.VMEM((n, n), jnp.float32), pltpu.VMEM((n, n), jnp.float32)],
    )(a)


def split_bf16(x):
    hi = lax.reduce_precision(x, exponent_bits=8, mantissa_bits=7)
    return hi.astype(jnp.bfloat16), (x - hi).astype(jnp.bfloat16)


def update_kernel(kind, tm, width, nbase, flags_ref, info_ref, slots_ref, *refs):
    base_refs = refs[:nbase]
    a_ref, bhi_ref, blo_ref, out_ref = refs[nbase:]
    i = pl.program_id(0)
    active = flags_ref[i] != 0

    def base_cols(g):
        cols = pl.ds(g * PANEL, PANEL)
        if kind == "gather":
            return base_refs[g][0]
        if kind == "diag":
            rows = info_ref[2] + i * tm + lax.broadcasted_iota(jnp.int32, (tm, PANEL), 0)
            ids = info_ref[1] + g * PANEL + lax.broadcasted_iota(jnp.int32, (tm, PANEL), 1)
            return jnp.where(rows == ids, base_refs[0][...], 0.0)
        return base_refs[0][:, cols]

    @pl.when(active)
    def _():
        a = a_ref[...]
        a_hi = a.astype(jnp.bfloat16)
        a_lo = (a - a_hi.astype(jnp.float32)).astype(jnp.bfloat16)
        dn = (((1,), (1,)), ((), ()))
        for g in range(width // PANEL):
            rows = pl.ds(g * PANEL, PANEL)
            b_hi = bhi_ref[rows, :]
            acc = lax.dot_general(a_hi, b_hi, dn, preferred_element_type=jnp.float32)
            acc = acc + lax.dot_general(a_hi, blo_ref[rows, :], dn, preferred_element_type=jnp.float32)
            acc = acc + lax.dot_general(a_lo, b_hi, dn, preferred_element_type=jnp.float32)
            out_ref[:, pl.ds(g * PANEL, PANEL)] = base_cols(g) - acc

    @pl.when(jnp.logical_not(active))
    def _():
        for g in range(width // PANEL):
            out_ref[:, pl.ds(g * PANEL, PANEL)] = base_cols(g)

    @pl.when((info_ref[0] == 1) & (info_ref[1] == 0))
    def _():
        out_ref[:, pl.ds(0, PANEL)] = a_ref[...]


def panel_update(kind, base, a, b, flags, info, slots, rows, width):
    tm = MSLOT
    b_hi, b_lo = split_bf16(b)
    nseg = width // PANEL
    if kind == "gather":
        bases = [base] * nseg
        base_specs = [
            pl.BlockSpec((1, tm, PANEL), lambda i, f, n, s, g=g: (s[i * nseg + g], 0, 0)) for g in range(nseg)
        ]
    elif kind == "diag":
        bases = [base]
        base_specs = [pl.BlockSpec((tm, 1), lambda i, f, n, s: (i, 0))]
    else:
        bases = [base]
        base_specs = [pl.BlockSpec((tm, width), lambda i, f, n, s: (i, 0))]
    grid_spec = pltpu.PrefetchScalarGridSpec(
        num_scalar_prefetch=3,
        grid=(rows // tm,),
        in_specs=base_specs + [
            pl.BlockSpec((tm, PANEL), lambda i, f, n, s: (i, 0)),
            pl.BlockSpec((width, PANEL), lambda i, f, n, s: (0, 0)),
            pl.BlockSpec((width, PANEL), lambda i, f, n, s: (0, 0)),
        ],
        out_specs=pl.BlockSpec((tm, width), lambda i, f, n, s: (i, 0)),
    )
    flops = 6 * rows * width * PANEL
    cost = pl.CostEstimate(flops=flops, transcendentals=0, bytes_accessed=rows * width * 8 + width * PANEL * 4)
    return pl.pallas_call(
        functools.partial(update_kernel, kind, tm, width, len(bases)),
        grid_spec=grid_spec,
        out_shape=jax.ShapeDtypeStruct((rows, width), jnp.float32),
        cost_estimate=cost,
        compiler_params=pltpu.CompilerParams(vmem_limit_bytes=48 * 1024 * 1024),
    )(flags, info, slots, *bases, a, b_hi, b_lo)


def solve_kernel(x_ref, fhi_ref, flo_ref, out_ref):
    x = x_ref[...]
    x_hi = x.astype(jnp.bfloat16)
    x_lo = (x - x_hi.astype(jnp.float32)).astype(jnp.bfloat16)
    f_hi = fhi_ref[...]
    acc = lax.dot_general(x_hi, f_hi, NT, preferred_element_type=jnp.float32)
    acc = acc + lax.dot_general(x_hi, flo_ref[...], NT, preferred_element_type=jnp.float32)
    out_ref[...] = acc + lax.dot_general(x_lo, f_hi, NT, preferred_element_type=jnp.float32)


def apply_inverse(x, finv):
    rows = x.shape[0]
    tm = 256 if rows % 256 == 0 else MSLOT
    f_hi, f_lo = split_bf16(finv)
    return pl.pallas_call(
        solve_kernel,
        grid=(rows // tm,),
        in_specs=[
            pl.BlockSpec((tm, PANEL), lambda i: (i, 0)),
            pl.BlockSpec((PANEL, PANEL), lambda i: (0, 0)),
            pl.BlockSpec((PANEL, PANEL), lambda i: (0, 0)),
        ],
        out_specs=pl.BlockSpec((tm, PANEL), lambda i: (i, 0)),
        out_shape=jax.ShapeDtypeStruct((rows, PANEL), jnp.float32),
        cost_estimate=pl.CostEstimate(flops=6 * rows * PANEL * PANEL, transcendentals=0, bytes_accessed=8 * rows * PANEL),
    )(x, f_hi, f_lo)


def dot_t(left, right):
    contract = (((1,), (1,)), ((), ()))
    l_hi, l_lo = split_bf16(left)
    r_hi, r_lo = split_bf16(right)
    out = lax.dot_general(l_hi, r_hi, contract, preferred_element_type=jnp.float32)
    out = out + lax.dot_general(l_hi, r_lo, contract, preferred_element_type=jnp.float32)
    return out + lax.dot_general(l_lo, r_hi, contract, preferred_element_type=jnp.float32)


def pick(index, options):
    out = options[0]
    for i in range(1, len(options)):
        out = jnp.where(index == i, options[i], out)
    return out


def seg0_slots(tseg, cap0):
    has0 = jnp.any(tseg == 0, axis=1)
    rank0 = jnp.cumsum(has0.astype(jnp.int32)) - 1
    slot = jnp.where(has0, rank0, cap0)
    return has0, rank0, slot


def per_device(eigvecs, coupling, mode_counts, tree_segments, eigvals, stiff):
    R = lax.axis_size("row")
    C = lax.axis_size("col")
    r = lax.axis_index("row")
    c = lax.axis_index("col")
    nsub = eigvecs.shape[0]
    H, W = stiff.shape
    Ec = coupling.shape[3]
    G = W // PANEL
    ratio = R // C
    npair = 2 * nsub
    cap = min(MOST * G * ((nsub + SUB_ROW - 1) // SUB_ROW), npair)
    cap0 = min(MOST * ((nsub + SUB_ROW - 1) // SUB_ROW), nsub)

    live = jnp.arange(MSLOT, dtype=jnp.int32)[None, :] < mode_counts[:, None]
    pieces = jnp.einsum("sim,sitp->stmp", eigvecs, coupling, preferred_element_type=jnp.float32)
    pieces = pieces * live.astype(jnp.float32)[:, None, :, None]
    flat = pieces.reshape(npair, MSLOT, Ec)
    flat_pad = jnp.concatenate([flat, jnp.zeros((1, MSLOT, Ec), jnp.float32)], axis=0)

    tseg = tree_segments
    dest = (tseg // G).reshape(npair)
    onehot = dest[:, None] == jnp.arange(C, dtype=jnp.int32)[None, :]
    rank_pd = jnp.cumsum(onehot.astype(jnp.int32), axis=0) - 1
    rank = jnp.sum(jnp.where(onehot, rank_pd, 0), axis=1)
    match = onehot[:, :, None] & (rank_pd[:, :, None] == jnp.arange(cap, dtype=jnp.int32)[None, None, :])
    send_idx = jnp.where(jnp.any(match, axis=0), jnp.argmax(match, axis=0), npair)
    send = flat_pad[send_idx]
    shifted = [send[c]]
    for k in range(1, C):
        out_k = lax.dynamic_index_in_dim(send, (c + k) % C, axis=0, keepdims=False)
        shifted.append(lax.ppermute(out_k, "col", [(i, (i + k) % C) for i in range(C)]))
    shifted = jnp.stack(shifted)
    recv = shifted[(c - jnp.arange(C, dtype=jnp.int32)) % C]
    recv_t = recv.transpose(1, 2, 0, 3).reshape(cap, MSLOT, C * Ec)
    recv_t = jnp.concatenate([recv_t, jnp.zeros((1, MSLOT, PANEL), jnp.float32)], axis=0)
    my_seg = c * G + jnp.arange(G, dtype=jnp.int32)
    seg_hit = tseg[:, :, None] == my_seg[None, None, :]
    rank2 = rank.reshape(nsub, 2)
    slot_tab = jnp.where(
        jnp.any(seg_hit, axis=1), jnp.sum(jnp.where(seg_hit, rank2[:, :, None], 0), axis=1), cap
    )

    has0, rank0, slot_r = seg0_slots(tseg, cap0)
    t0 = jnp.where(tseg[:, 0] == 0, 0, 1)
    sel = has0[:, None] & (rank0[:, None] == jnp.arange(cap0, dtype=jnp.int32)[None, :])
    sel_sub = jnp.argmax(sel, axis=0)
    zidx = jnp.where(jnp.any(sel, axis=0), sel_sub * 2 + t0[sel_sub], npair)
    z_local = flat_pad[zidx]
    z_all = lax.all_gather(z_local, "col", axis=0, tiled=False)
    z_rows = z_all.transpose(1, 2, 0, 3).reshape(cap0 * MSLOT, C * Ec)

    kpp_src = stiff[:PANEL, :PANEL]
    rs = PANEL // R
    got = [kpp_src[:rs]]
    for i in range(1, R):
        got.append(lax.ppermute(kpp_src[i * rs:(i + 1) * rs], AXES, [(0, i * C)]))
    kpp_part = pick(r, got)
    kpp_col0 = lax.all_gather(kpp_part, "row", axis=0, tiled=True)
    cs = PANEL // C
    got = [kpp_col0[:cs]]
    for k in range(1, C):
        got.append(lax.ppermute(kpp_col0[k * cs:(k + 1) * cs], AXES, [(i * C, i * C + k) for i in range(R)]))
    kpp = lax.all_gather(pick(c, got), "col", axis=0, tiled=True)

    m_src = stiff[:, :PANEL]
    rps = W // R
    zps = cap0 * MSLOT // C
    got = [m_src[:rps]]
    for k in range(1, C):
        got.append(lax.ppermute(m_src[k * rps:(k + 1) * rps], AXES, [(i * C, i * C + k) for i in range(R)]))
    m_row = lax.all_gather(pick(c, got), "col", axis=0, tiled=True)
    got = []
    for k in range(C):
        payload = jnp.concatenate([m_src[k * rps:(k + 1) * rps], z_rows[k * zps:(k + 1) * zps]], axis=0)
        perm = [(i * C, ((i % ratio) * C + k) * C + i // ratio) for i in range(R)]
        got.append(lax.ppermute(payload, AXES, perm))
    col_parts = lax.all_gather(pick(r % C, got), "row", axis=0, tiled=False)
    m_col = col_parts[:, :rps].reshape(W, PANEL)
    z_col = col_parts[:, rps:].reshape(ratio * cap0 * MSLOT, PANEL)

    tseg_all = lax.all_gather(tseg, "row", axis=0, tiled=False)
    tseg_c = lax.dynamic_slice_in_dim(tseg_all, c * ratio, ratio, axis=0)
    slot_c = []
    for j in range(ratio):
        has_j, rank_j, _ = seg0_slots(tseg_c[j], cap0)
        slot_c.append(jnp.where(has_j, j * cap0 + rank_j, ratio * cap0))
    slot_c = jnp.concatenate(slot_c)

    finv = chol_inverse(kpp)
    stacked = jnp.concatenate([m_row, m_col, z_rows, z_col], axis=0)
    solved = apply_inverse(stacked, finv)
    low_r = solved[:H]
    low_c = solved[H:H + W]
    lowmi_r = solved[H + W:H + W + cap0 * MSLOT]
    lowmi_c = solved[H + W + cap0 * MSLOT:]

    ones = jnp.ones((H // MSLOT,), jnp.int32)
    none = jnp.zeros((1,), jnp.int32)
    info = jnp.stack([jnp.int32(1), c * W, r * H, jnp.int32(0)]).astype(jnp.int32)
    reduced_ii = panel_update("array", stiff, low_r, low_c, ones, info, none, H, W)

    lmi = jnp.concatenate(
        [lowmi_r.reshape(cap0, MSLOT, PANEL), jnp.zeros((1, MSLOT, PANEL), jnp.float32)], axis=0
    )
    lmi_full = lmi[slot_r].reshape(nsub * MSLOT, PANEL)
    flags = has0.astype(jnp.int32)
    reduced_mi = panel_update(
        "gather", recv_t, lmi_full, low_c, flags, info, slot_tab.reshape(-1).astype(jnp.int32), nsub * MSLOT, W
    )

    nc = ratio * cap0
    lmc = jnp.concatenate(
        [lowmi_c.reshape(nc, MSLOT, PANEL), jnp.zeros((1, MSLOT, PANEL), jnp.float32)], axis=0
    )
    mode_width = ratio * nsub * MSLOT
    lmc_full = lmc[slot_c].reshape(mode_width, PANEL)
    diag_values = jnp.where(live, eigvals, 1.0).reshape(-1, 1)
    mode_rows = diag_values.shape[0]
    info_mm = jnp.stack([jnp.int32(0), c * mode_width, r * mode_rows, jnp.int32(0)]).astype(jnp.int32)
    reduced_mm = panel_update("diag", diag_values, lmi_full, lmc_full, flags, info_mm, none, mode_rows, mode_width)
    return (reduced_ii, reduced_mi, reduced_mm)


def solution(mesh):
    in_specs = (
        P("row", None, None),
        P("row", None, None, "col"),
        P("row"),
        P("row", None),
        P("row", None),
        P("row", "col"),
    )
    out_specs = (P("row", "col"), P("row", "col"), P("row", "col"))
    return jax.shard_map(
        per_device, mesh=mesh, in_specs=in_specs, out_specs=out_specs, check_vma=False
    )
```

```python
import functools

import jax
import jax.numpy as jnp
from jax import lax
from jax.sharding import PartitionSpec as P
from jax.experimental import pallas as pl
from jax.experimental.pallas import tpu as pltpu

MSLOT = 128
PANEL = 512
MOST = 2
SUB_ROW = 8

AXES = ("row", "col")
LEAF = 128


def mm3(a, b, dn):
    a_hi = a.astype(jnp.bfloat16)
    a_lo = (a - a_hi.astype(jnp.float32)).astype(jnp.bfloat16)
    b_hi = b.astype(jnp.bfloat16)
    b_lo = (b - b_hi.astype(jnp.float32)).astype(jnp.bfloat16)
    out = lax.dot_general(a_hi, b_hi, dn, preferred_element_type=jnp.float32)
    out = out + lax.dot_general(a_hi, b_lo, dn, preferred_element_type=jnp.float32)
    return out + lax.dot_general(a_lo, b_hi, dn, preferred_element_type=jnp.float32)


NN = (((1,), (0,)), ((), ()))
NT = (((1,), (1,)), ((), ()))


def leaf_inverse(d):
    n = d.shape[0]
    sub = lax.broadcasted_iota(jnp.int32, (n, n), 0)
    lane = lax.broadcasted_iota(jnp.int32, (n, n), 1)
    sub_c = lax.broadcasted_iota(jnp.int32, (n, 1), 0)
    lane_r = lax.broadcasted_iota(jnp.int32, (1, n), 1)
    eye = jnp.where(sub == lane, 1.0, 0.0).astype(jnp.float32)

    def step(k, carry):
        dm, em, xm = carry
        colk = jnp.sum(jnp.where(lane == k, dm, 0.0), axis=1, keepdims=True)
        rowk = jnp.sum(jnp.where(sub == k, dm, 0.0), axis=0, keepdims=True)
        dkk = jnp.sum(jnp.where(lane_r == k, rowk, 0.0), axis=1, keepdims=True)
        s = 1.0 / jnp.sqrt(dkk)
        lc = jnp.where(sub_c > k, colk * s, 0.0)
        lr = jnp.where(lane_r > k, rowk * s, 0.0)
        dm = dm - lc * lr
        erow = jnp.sum(jnp.where(sub == k, em, 0.0), axis=0, keepdims=True)
        xk = erow * s
        xm = jnp.where(sub == k, xk, xm)
        em = em - lc * xk
        return dm, em, xm

    _, _, xm = lax.fori_loop(0, n, step, (d, eye, jnp.zeros_like(d)))
    return xm


def chol_inv_kernel(a_ref, x_ref, w_ref, l_ref):
    n = a_ref.shape[0]
    nb = n // LEAF
    w_ref[...] = a_ref[...]
    for kb in range(nb):
        o = kb * LEAF
        blk = pl.ds(o, LEAF)
        xkk = leaf_inverse(w_ref[blk, blk])
        x_ref[blk, blk] = xkk
        if kb + 1 < nb:
            rest = pl.ds(o + LEAF, n - o - LEAF)
            panel = mm3(w_ref[rest, blk], xkk, NT)
            l_ref[rest, blk] = panel
            w_ref[rest, rest] = w_ref[rest, rest] - mm3(panel, panel, NT)
    for i in range(1, nb):
        bi = pl.ds(i * LEAF, LEAF)
        xii = x_ref[bi, bi]
        for j in range(i):
            bj = pl.ds(j * LEAF, LEAF)
            acc = None
            for k in range(j, i):
                bk = pl.ds(k * LEAF, LEAF)
                term = mm3(l_ref[bi, bk], x_ref[bk, bj], NN)
                acc = term if acc is None else acc + term
            x_ref[bi, bj] = -mm3(xii, acc, NN)
        for j in range(i + 1, nb):
            x_ref[bi, pl.ds(j * LEAF, LEAF)] = jnp.zeros((LEAF, LEAF), jnp.float32)
    x_ref[pl.ds(0, LEAF), pl.ds(LEAF, n - LEAF)] = jnp.zeros((LEAF, n - LEAF), jnp.float32)


def chol_inverse(a):
    n = a.shape[0]
    return pl.pallas_call(
        chol_inv_kernel,
        out_shape=jax.ShapeDtypeStruct((n, n), jnp.float32),
        cost_estimate=pl.CostEstimate(flops=60 * n ** 3, transcendentals=n, bytes_accessed=8 * n * n),
        in_specs=[pl.BlockSpec(memory_space=pltpu.VMEM)],
        out_specs=pl.BlockSpec(memory_space=pltpu.VMEM),
        scratch_shapes=[pltpu.VMEM((n, n), jnp.float32), pltpu.VMEM((n, n), jnp.float32)],
    )(a)


def split_bf16(x):
    hi = lax.reduce_precision(x, exponent_bits=8, mantissa_bits=7)
    return hi.astype(jnp.bfloat16), (x - hi).astype(jnp.bfloat16)


def update_kernel(kind, tm, width, nbase, flags_ref, info_ref, slots_ref, *refs):
    base_refs = refs[:nbase]
    a_ref, bhi_ref, blo_ref, out_ref = refs[nbase:]
    i = pl.program_id(0)
    active = flags_ref[i] != 0

    def base_cols(g):
        cols = pl.ds(g * PANEL, PANEL)
        if kind == "gather":
            return base_refs[g][0]
        if kind == "diag":
            rows = info_ref[2] + i * tm + lax.broadcasted_iota(jnp.int32, (tm, PANEL), 0)
            ids = info_ref[1] + g * PANEL + lax.broadcasted_iota(jnp.int32, (tm, PANEL), 1)
            return jnp.where(rows == ids, base_refs[0][...], 0.0)
        return base_refs[0][:, cols]

    @pl.when(active)
    def _():
        a = a_ref[...]
        a_hi = a.astype(jnp.bfloat16)
        a_lo = (a - a_hi.astype(jnp.float32)).astype(jnp.bfloat16)
        dn = (((1,), (1,)), ((), ()))
        for g in range(width // PANEL):
            rows = pl.ds(g * PANEL, PANEL)
            b_hi = bhi_ref[rows, :]
            acc = lax.dot_general(a_hi, b_hi, dn, preferred_element_type=jnp.float32)
            acc = acc + lax.dot_general(a_hi, blo_ref[rows, :], dn, preferred_element_type=jnp.float32)
            acc = acc + lax.dot_general(a_lo, b_hi, dn, preferred_element_type=jnp.float32)
            out_ref[:, pl.ds(g * PANEL, PANEL)] = base_cols(g) - acc

    @pl.when(jnp.logical_not(active))
    def _():
        for g in range(width // PANEL):
            out_ref[:, pl.ds(g * PANEL, PANEL)] = base_cols(g)

    @pl.when((info_ref[0] == 1) & (info_ref[1] == 0))
    def _():
        out_ref[:, pl.ds(0, PANEL)] = a_ref[...]


def panel_update(kind, base, a, b, flags, info, slots, rows, width):
    tm = MSLOT
    b_hi, b_lo = split_bf16(b)
    nseg = width // PANEL
    if kind == "gather":
        bases = [base] * nseg
        base_specs = [
            pl.BlockSpec((1, tm, PANEL), lambda i, f, n, s, g=g: (s[i * nseg + g], 0, 0)) for g in range(nseg)
        ]
    elif kind == "diag":
        bases = [base]
        base_specs = [pl.BlockSpec((tm, 1), lambda i, f, n, s: (i, 0))]
    else:
        bases = [base]
        base_specs = [pl.BlockSpec((tm, width), lambda i, f, n, s: (i, 0))]
    grid_spec = pltpu.PrefetchScalarGridSpec(
        num_scalar_prefetch=3,
        grid=(rows // tm,),
        in_specs=base_specs + [
            pl.BlockSpec((tm, PANEL), lambda i, f, n, s: (i, 0)),
            pl.BlockSpec((width, PANEL), lambda i, f, n, s: (0, 0)),
            pl.BlockSpec((width, PANEL), lambda i, f, n, s: (0, 0)),
        ],
        out_specs=pl.BlockSpec((tm, width), lambda i, f, n, s: (i, 0)),
    )
    flops = 6 * rows * width * PANEL
    cost = pl.CostEstimate(flops=flops, transcendentals=0, bytes_accessed=rows * width * 8 + width * PANEL * 4)
    return pl.pallas_call(
        functools.partial(update_kernel, kind, tm, width, len(bases)),
        grid_spec=grid_spec,
        out_shape=jax.ShapeDtypeStruct((rows, width), jnp.float32),
        cost_estimate=cost,
        compiler_params=pltpu.CompilerParams(vmem_limit_bytes=48 * 1024 * 1024),
    )(flags, info, slots, *bases, a, b_hi, b_lo)


def solve_kernel(x_ref, fhi_ref, flo_ref, out_ref):
    x = x_ref[...]
    x_hi = x.astype(jnp.bfloat16)
    x_lo = (x - x_hi.astype(jnp.float32)).astype(jnp.bfloat16)
    f_hi = fhi_ref[...]
    acc = lax.dot_general(x_hi, f_hi, NT, preferred_element_type=jnp.float32)
    acc = acc + lax.dot_general(x_hi, flo_ref[...], NT, preferred_element_type=jnp.float32)
    out_ref[...] = acc + lax.dot_general(x_lo, f_hi, NT, preferred_element_type=jnp.float32)


def apply_inverse(x, finv):
    rows = x.shape[0]
    tm = 256 if rows % 256 == 0 else MSLOT
    f_hi, f_lo = split_bf16(finv)
    return pl.pallas_call(
        solve_kernel,
        grid=(rows // tm,),
        in_specs=[
            pl.BlockSpec((tm, PANEL), lambda i: (i, 0)),
            pl.BlockSpec((PANEL, PANEL), lambda i: (0, 0)),
            pl.BlockSpec((PANEL, PANEL), lambda i: (0, 0)),
        ],
        out_specs=pl.BlockSpec((tm, PANEL), lambda i: (i, 0)),
        out_shape=jax.ShapeDtypeStruct((rows, PANEL), jnp.float32),
        cost_estimate=pl.CostEstimate(flops=6 * rows * PANEL * PANEL, transcendentals=0, bytes_accessed=8 * rows * PANEL),
    )(x, f_hi, f_lo)


def dot_t(left, right):
    contract = (((1,), (1,)), ((), ()))
    l_hi, l_lo = split_bf16(left)
    r_hi, r_lo = split_bf16(right)
    out = lax.dot_general(l_hi, r_hi, contract, preferred_element_type=jnp.float32)
    out = out + lax.dot_general(l_hi, r_lo, contract, preferred_element_type=jnp.float32)
    return out + lax.dot_general(l_lo, r_hi, contract, preferred_element_type=jnp.float32)


def pick(index, options):
    out = options[0]
    for i in range(1, len(options)):
        out = jnp.where(index == i, options[i], out)
    return out


def seg0_slots(tseg, cap0):
    has0 = jnp.any(tseg == 0, axis=1)
    rank0 = jnp.cumsum(has0.astype(jnp.int32)) - 1
    slot = jnp.where(has0, rank0, cap0)
    return has0, rank0, slot


def per_device(eigvecs, coupling, mode_counts, tree_segments, eigvals, stiff):
    R = lax.axis_size("row")
    C = lax.axis_size("col")
    r = lax.axis_index("row")
    c = lax.axis_index("col")
    nsub = eigvecs.shape[0]
    H, W = stiff.shape
    Ec = coupling.shape[3]
    G = W // PANEL
    ratio = R // C
    npair = 2 * nsub
    cap = min(MOST * G * ((nsub + SUB_ROW - 1) // SUB_ROW), npair)
    cap0 = min(MOST * ((nsub + SUB_ROW - 1) // SUB_ROW), nsub)

    live = jnp.arange(MSLOT, dtype=jnp.int32)[None, :] < mode_counts[:, None]
    pieces = jnp.einsum("sim,sitp->stmp", eigvecs, coupling, preferred_element_type=jnp.float32)
    pieces = pieces * live.astype(jnp.float32)[:, None, :, None]
    flat = pieces.reshape(npair, MSLOT, Ec)
    flat_pad = jnp.concatenate([flat, jnp.zeros((1, MSLOT, Ec), jnp.float32)], axis=0)

    kpp_src = stiff[:PANEL, :PANEL]
    rs = PANEL // R
    got = [kpp_src[:rs]]
    for i in range(1, R):
        got.append(lax.ppermute(kpp_src[i * rs:(i + 1) * rs], AXES, [(0, i * C)]))
    kpp_part = pick(r, got)
    kpp_col0 = lax.all_gather(kpp_part, "row", axis=0, tiled=True)
    cs = PANEL // C
    got = [kpp_col0[:cs]]
    for k in range(1, C):
        got.append(lax.ppermute(kpp_col0[k * cs:(k + 1) * cs], AXES, [(i * C, i * C + k) for i in range(R)]))
    kpp = lax.all_gather(pick(c, got), "col", axis=0, tiled=True)

    finv = chol_inverse(kpp)

    tseg = tree_segments
    dest = (tseg // G).reshape(npair)
    onehot = dest[:, None] == jnp.arange(C, dtype=jnp.int32)[None, :]
    rank_pd = jnp.cumsum(onehot.astype(jnp.int32), axis=0) - 1
    rank = jnp.sum(jnp.where(onehot, rank_pd, 0), axis=1)
    match = onehot[:, :, None] & (rank_pd[:, :, None] == jnp.arange(cap, dtype=jnp.int32)[None, None, :])
    send_idx = jnp.where(jnp.any(match, axis=0), jnp.argmax(match, axis=0), npair)
    send = flat_pad[send_idx]
    send, _ = lax.optimization_barrier((send, finv))
    shifted = [send[c]]
    for k in range(1, C):
        out_k = lax.dynamic_index_in_dim(send, (c + k) % C, axis=0, keepdims=False)
        shifted.append(lax.ppermute(out_k, "col", [(i, (i + k) % C) for i in range(C)]))
    shifted = jnp.stack(shifted)
    recv = shifted[(c - jnp.arange(C, dtype=jnp.int32)) % C]
    recv_t = recv.transpose(1, 2, 0, 3).reshape(cap, MSLOT, C * Ec)
    recv_t = jnp.concatenate([recv_t, jnp.zeros((1, MSLOT, PANEL), jnp.float32)], axis=0)
    my_seg = c * G + jnp.arange(G, dtype=jnp.int32)
    seg_hit = tseg[:, :, None] == my_seg[None, None, :]
    rank2 = rank.reshape(nsub, 2)
    slot_tab = jnp.where(
        jnp.any(seg_hit, axis=1), jnp.sum(jnp.where(seg_hit, rank2[:, :, None], 0), axis=1), cap
    )

    has0, rank0, slot_r = seg0_slots(tseg, cap0)
    t0 = jnp.where(tseg[:, 0] == 0, 0, 1)
    sel = has0[:, None] & (rank0[:, None] == jnp.arange(cap0, dtype=jnp.int32)[None, :])
    sel_sub = jnp.argmax(sel, axis=0)
    zidx = jnp.where(jnp.any(sel, axis=0), sel_sub * 2 + t0[sel_sub], npair)
    z_local = flat_pad[zidx]
    z_all = lax.all_gather(z_local, "col", axis=0, tiled=False)
    z_rows = z_all.transpose(1, 2, 0, 3).reshape(cap0 * MSLOT, C * Ec)

    m_src = stiff[:, :PANEL]
    rps = W // R
    zps = cap0 * MSLOT // C
    got = [m_src[:rps]]
    for k in range(1, C):
        got.append(lax.ppermute(m_src[k * rps:(k + 1) * rps], AXES, [(i * C, i * C + k) for i in range(R)]))
    m_row = lax.all_gather(pick(c, got), "col", axis=0, tiled=True)
    got = []
    for k in range(C):
        payload = jnp.concatenate([m_src[k * rps:(k + 1) * rps], z_rows[k * zps:(k + 1) * zps]], axis=0)
        perm = [(i * C, ((i % ratio) * C + k) * C + i // ratio) for i in range(R)]
        got.append(lax.ppermute(payload, AXES, perm))
    col_parts = lax.all_gather(pick(r % C, got), "row", axis=0, tiled=False)
    m_col = col_parts[:, :rps].reshape(W, PANEL)
    z_col = col_parts[:, rps:].reshape(ratio * cap0 * MSLOT, PANEL)

    tseg_late, _ = lax.optimization_barrier((tseg, finv))
    tseg_all = lax.all_gather(tseg_late, "row", axis=0, tiled=False)
    tseg_c = lax.dynamic_slice_in_dim(tseg_all, c * ratio, ratio, axis=0)
    slot_c = []
    for j in range(ratio):
        has_j, rank_j, _ = seg0_slots(tseg_c[j], cap0)
        slot_c.append(jnp.where(has_j, j * cap0 + rank_j, ratio * cap0))
    slot_c = jnp.concatenate(slot_c)

    stacked = jnp.concatenate([m_row, m_col, z_rows, z_col], axis=0)
    solved = apply_inverse(stacked, finv)
    low_r = solved[:H]
    low_c = solved[H:H + W]
    lowmi_r = solved[H + W:H + W + cap0 * MSLOT]
    lowmi_c = solved[H + W + cap0 * MSLOT:]

    ones = jnp.ones((H // MSLOT,), jnp.int32)
    none = jnp.zeros((1,), jnp.int32)
    info = jnp.stack([jnp.int32(1), c * W, r * H, jnp.int32(0)]).astype(jnp.int32)
    reduced_ii = panel_update("array", stiff, low_r, low_c, ones, info, none, H, W)

    lmi = jnp.concatenate(
        [lowmi_r.reshape(cap0, MSLOT, PANEL), jnp.zeros((1, MSLOT, PANEL), jnp.float32)], axis=0
    )
    lmi_full = lmi[slot_r].reshape(nsub * MSLOT, PANEL)
    flags = has0.astype(jnp.int32)
    reduced_mi = panel_update(
        "gather", recv_t, lmi_full, low_c, flags, info, slot_tab.reshape(-1).astype(jnp.int32), nsub * MSLOT, W
    )

    nc = ratio * cap0
    lmc = jnp.concatenate(
        [lowmi_c.reshape(nc, MSLOT, PANEL), jnp.zeros((1, MSLOT, PANEL), jnp.float32)], axis=0
    )
    mode_width = ratio * nsub * MSLOT
    lmc_full = lmc[slot_c].reshape(mode_width, PANEL)
    diag_values = jnp.where(live, eigvals, 1.0).reshape(-1, 1)
    mode_rows = diag_values.shape[0]
    info_mm = jnp.stack([jnp.int32(0), c * mode_width, r * mode_rows, jnp.int32(0)]).astype(jnp.int32)
    reduced_mm = panel_update("diag", diag_values, lmi_full, lmc_full, flags, info_mm, none, mode_rows, mode_width)
    return (reduced_ii, reduced_mi, reduced_mm)


def solution(mesh):
    in_specs = (
        P("row", None, None),
        P("row", None, None, "col"),
        P("row"),
        P("row", None),
        P("row", None),
        P("row", "col"),
    )
    out_specs = (P("row", "col"), P("row", "col"), P("row", "col"))
    return jax.shard_map(
        per_device, mesh=mesh, in_specs=in_specs, out_specs=out_specs, check_vma=False
    )
```

```python
import functools

import jax
import jax.numpy as jnp
from jax import lax
from jax.sharding import PartitionSpec as P
from jax.experimental import pallas as pl
from jax.experimental.pallas import tpu as pltpu

MSLOT = 128
PANEL = 512
MOST = 2
SUB_ROW = 8

AXES = ("row", "col")
LEAF = 128


def mm3(a, b, dn):
    a_hi = a.astype(jnp.bfloat16)
    a_lo = (a - a_hi.astype(jnp.float32)).astype(jnp.bfloat16)
    b_hi = b.astype(jnp.bfloat16)
    b_lo = (b - b_hi.astype(jnp.float32)).astype(jnp.bfloat16)
    out = lax.dot_general(a_hi, b_hi, dn, preferred_element_type=jnp.float32)
    out = out + lax.dot_general(a_hi, b_lo, dn, preferred_element_type=jnp.float32)
    return out + lax.dot_general(a_lo, b_hi, dn, preferred_element_type=jnp.float32)


NN = (((1,), (0,)), ((), ()))
NT = (((1,), (1,)), ((), ()))


def leaf_inverse(d):
    n = d.shape[0]
    sub = lax.broadcasted_iota(jnp.int32, (n, n), 0)
    lane = lax.broadcasted_iota(jnp.int32, (n, n), 1)
    sub_c = lax.broadcasted_iota(jnp.int32, (n, 1), 0)
    lane_r = lax.broadcasted_iota(jnp.int32, (1, n), 1)
    eye = jnp.where(sub == lane, 1.0, 0.0).astype(jnp.float32)

    def step(k, carry):
        dm, em, xm = carry
        colk = jnp.sum(jnp.where(lane == k, dm, 0.0), axis=1, keepdims=True)
        rowk = jnp.sum(jnp.where(sub == k, dm, 0.0), axis=0, keepdims=True)
        dkk = jnp.sum(jnp.where(lane_r == k, rowk, 0.0), axis=1, keepdims=True)
        s = 1.0 / jnp.sqrt(dkk)
        lc = jnp.where(sub_c > k, colk * s, 0.0)
        lr = jnp.where(lane_r > k, rowk * s, 0.0)
        dm = dm - lc * lr
        erow = jnp.sum(jnp.where(sub == k, em, 0.0), axis=0, keepdims=True)
        xk = erow * s
        xm = jnp.where(sub == k, xk, xm)
        em = em - lc * xk
        return dm, em, xm

    _, _, xm = lax.fori_loop(0, n, step, (d, eye, jnp.zeros_like(d)))
    return xm


def chol_inv_kernel(a_ref, x_ref, w_ref, l_ref):
    n = a_ref.shape[0]
    nb = n // LEAF
    w_ref[...] = a_ref[...]
    for kb in range(nb):
        o = kb * LEAF
        blk = pl.ds(o, LEAF)
        xkk = leaf_inverse(w_ref[blk, blk])
        x_ref[blk, blk] = xkk
        if kb + 1 < nb:
            rest = pl.ds(o + LEAF, n - o - LEAF)
            panel = mm3(w_ref[rest, blk], xkk, NT)
            l_ref[rest, blk] = panel
            w_ref[rest, rest] = w_ref[rest, rest] - mm3(panel, panel, NT)
    for i in range(1, nb):
        bi = pl.ds(i * LEAF, LEAF)
        xii = x_ref[bi, bi]
        for j in range(i):
            bj = pl.ds(j * LEAF, LEAF)
            acc = None
            for k in range(j, i):
                bk = pl.ds(k * LEAF, LEAF)
                term = mm3(l_ref[bi, bk], x_ref[bk, bj], NN)
                acc = term if acc is None else acc + term
            x_ref[bi, bj] = -mm3(xii, acc, NN)
        for j in range(i + 1, nb):
            x_ref[bi, pl.ds(j * LEAF, LEAF)] = jnp.zeros((LEAF, LEAF), jnp.float32)
    x_ref[pl.ds(0, LEAF), pl.ds(LEAF, n - LEAF)] = jnp.zeros((LEAF, n - LEAF), jnp.float32)


def chol_inverse(a):
    n = a.shape[0]
    return pl.pallas_call(
        chol_inv_kernel,
        out_shape=jax.ShapeDtypeStruct((n, n), jnp.float32),
        cost_estimate=pl.CostEstimate(flops=60 * n ** 3, transcendentals=n, bytes_accessed=8 * n * n),
        in_specs=[pl.BlockSpec(memory_space=pltpu.VMEM)],
        out_specs=pl.BlockSpec(memory_space=pltpu.VMEM),
        scratch_shapes=[pltpu.VMEM((n, n), jnp.float32), pltpu.VMEM((n, n), jnp.float32)],
    )(a)


def split_bf16(x):
    hi = lax.reduce_precision(x, exponent_bits=8, mantissa_bits=7)
    return hi.astype(jnp.bfloat16), (x - hi).astype(jnp.bfloat16)


def update_kernel(kind, tm, width, nbase, flags_ref, info_ref, slots_ref, *refs):
    base_refs = refs[:nbase]
    a_ref, bhi_ref, blo_ref, out_ref = refs[nbase:]
    i = pl.program_id(0)
    active = flags_ref[i] != 0

    def base_cols(g):
        cols = pl.ds(g * PANEL, PANEL)
        if kind == "gather":
            return base_refs[g][0]
        if kind == "diag":
            rows = info_ref[2] + i * tm + lax.broadcasted_iota(jnp.int32, (tm, PANEL), 0)
            ids = info_ref[1] + g * PANEL + lax.broadcasted_iota(jnp.int32, (tm, PANEL), 1)
            return jnp.where(rows == ids, base_refs[0][...], 0.0)
        return base_refs[0][:, cols]

    @pl.when(active)
    def _():
        a = a_ref[...]
        a_hi = a.astype(jnp.bfloat16)
        a_lo = (a - a_hi.astype(jnp.float32)).astype(jnp.bfloat16)
        dn = (((1,), (1,)), ((), ()))
        for g in range(width // PANEL):
            rows = pl.ds(g * PANEL, PANEL)
            b_hi = bhi_ref[rows, :]
            acc = lax.dot_general(a_hi, b_hi, dn, preferred_element_type=jnp.float32)
            acc = acc + lax.dot_general(a_hi, blo_ref[rows, :], dn, preferred_element_type=jnp.float32)
            acc = acc + lax.dot_general(a_lo, b_hi, dn, preferred_element_type=jnp.float32)
            out_ref[:, pl.ds(g * PANEL, PANEL)] = base_cols(g) - acc

    @pl.when(jnp.logical_not(active))
    def _():
        for g in range(width // PANEL):
            out_ref[:, pl.ds(g * PANEL, PANEL)] = base_cols(g)

    @pl.when((info_ref[0] == 1) & (info_ref[1] == 0))
    def _():
        out_ref[:, pl.ds(0, PANEL)] = a_ref[...]


def panel_update(kind, base, a, b, flags, info, slots, rows, width):
    tm = MSLOT
    b_hi, b_lo = split_bf16(b)
    nseg = width // PANEL
    if kind == "gather":
        bases = [base] * nseg
        base_specs = [
            pl.BlockSpec((1, tm, PANEL), lambda i, f, n, s, g=g: (s[i * nseg + g], 0, 0)) for g in range(nseg)
        ]
    elif kind == "diag":
        bases = [base]
        base_specs = [pl.BlockSpec((tm, 1), lambda i, f, n, s: (i, 0))]
    else:
        bases = [base]
        base_specs = [pl.BlockSpec((tm, width), lambda i, f, n, s: (i, 0))]
    grid_spec = pltpu.PrefetchScalarGridSpec(
        num_scalar_prefetch=3,
        grid=(rows // tm,),
        in_specs=base_specs + [
            pl.BlockSpec((tm, PANEL), lambda i, f, n, s: (i, 0)),
            pl.BlockSpec((width, PANEL), lambda i, f, n, s: (0, 0)),
            pl.BlockSpec((width, PANEL), lambda i, f, n, s: (0, 0)),
        ],
        out_specs=pl.BlockSpec((tm, width), lambda i, f, n, s: (i, 0)),
    )
    flops = 6 * rows * width * PANEL
    cost = pl.CostEstimate(flops=flops, transcendentals=0, bytes_accessed=rows * width * 8 + width * PANEL * 4)
    return pl.pallas_call(
        functools.partial(update_kernel, kind, tm, width, len(bases)),
        grid_spec=grid_spec,
        out_shape=jax.ShapeDtypeStruct((rows, width), jnp.float32),
        cost_estimate=cost,
        compiler_params=pltpu.CompilerParams(vmem_limit_bytes=48 * 1024 * 1024),
    )(flags, info, slots, *bases, a, b_hi, b_lo)


def solve_kernel(x_ref, fhi_ref, flo_ref, out_ref):
    x = x_ref[...]
    x_hi = x.astype(jnp.bfloat16)
    x_lo = (x - x_hi.astype(jnp.float32)).astype(jnp.bfloat16)
    f_hi = fhi_ref[...]
    acc = lax.dot_general(x_hi, f_hi, NT, preferred_element_type=jnp.float32)
    acc = acc + lax.dot_general(x_hi, flo_ref[...], NT, preferred_element_type=jnp.float32)
    out_ref[...] = acc + lax.dot_general(x_lo, f_hi, NT, preferred_element_type=jnp.float32)


def apply_inverse(x, finv):
    rows = x.shape[0]
    tm = 256 if rows % 256 == 0 else MSLOT
    f_hi, f_lo = split_bf16(finv)
    return pl.pallas_call(
        solve_kernel,
        grid=(rows // tm,),
        in_specs=[
            pl.BlockSpec((tm, PANEL), lambda i: (i, 0)),
            pl.BlockSpec((PANEL, PANEL), lambda i: (0, 0)),
            pl.BlockSpec((PANEL, PANEL), lambda i: (0, 0)),
        ],
        out_specs=pl.BlockSpec((tm, PANEL), lambda i: (i, 0)),
        out_shape=jax.ShapeDtypeStruct((rows, PANEL), jnp.float32),
        cost_estimate=pl.CostEstimate(flops=6 * rows * PANEL * PANEL, transcendentals=0, bytes_accessed=8 * rows * PANEL),
    )(x, f_hi, f_lo)


def dot_t(left, right):
    contract = (((1,), (1,)), ((), ()))
    l_hi, l_lo = split_bf16(left)
    r_hi, r_lo = split_bf16(right)
    out = lax.dot_general(l_hi, r_hi, contract, preferred_element_type=jnp.float32)
    out = out + lax.dot_general(l_hi, r_lo, contract, preferred_element_type=jnp.float32)
    return out + lax.dot_general(l_lo, r_hi, contract, preferred_element_type=jnp.float32)


def pick(index, options):
    out = options[0]
    for i in range(1, len(options)):
        out = jnp.where(index == i, options[i], out)
    return out


def seg0_slots(tseg, cap0):
    has0 = jnp.any(tseg == 0, axis=1)
    rank0 = jnp.cumsum(has0.astype(jnp.int32)) - 1
    slot = jnp.where(has0, rank0, cap0)
    return has0, rank0, slot


def per_device(eigvecs, coupling, mode_counts, tree_segments, eigvals, stiff):
    R = lax.axis_size("row")
    C = lax.axis_size("col")
    r = lax.axis_index("row")
    c = lax.axis_index("col")
    nsub = eigvecs.shape[0]
    H, W = stiff.shape
    Ec = coupling.shape[3]
    G = W // PANEL
    ratio = R // C
    npair = 2 * nsub
    cap = min(MOST * G * ((nsub + SUB_ROW - 1) // SUB_ROW), npair)
    cap0 = min(MOST * ((nsub + SUB_ROW - 1) // SUB_ROW), nsub)

    live = jnp.arange(MSLOT, dtype=jnp.int32)[None, :] < mode_counts[:, None]
    pieces = jnp.einsum("sim,sitp->stmp", eigvecs, coupling, preferred_element_type=jnp.float32)
    pieces = pieces * live.astype(jnp.float32)[:, None, :, None]
    flat = pieces.reshape(npair, MSLOT, Ec)
    flat_pad = jnp.concatenate([flat, jnp.zeros((1, MSLOT, Ec), jnp.float32)], axis=0)

    kpp_src = stiff[:PANEL, :PANEL]
    rs = PANEL // R
    got = [kpp_src[:rs]]
    for i in range(1, R):
        got.append(lax.ppermute(kpp_src[i * rs:(i + 1) * rs], AXES, [(0, i * C)]))
    kpp_part = pick(r, got)
    kpp_col0 = lax.all_gather(kpp_part, "row", axis=0, tiled=True)
    cs = PANEL // C
    got = [kpp_col0[:cs]]
    for k in range(1, C):
        got.append(lax.ppermute(kpp_col0[k * cs:(k + 1) * cs], AXES, [(i * C, i * C + k) for i in range(R)]))
    kpp = lax.all_gather(pick(c, got), "col", axis=0, tiled=True)

    finv = chol_inverse(kpp)

    tseg = tree_segments
    dest = (tseg // G).reshape(npair)
    onehot = dest[:, None] == jnp.arange(C, dtype=jnp.int32)[None, :]
    rank_pd = jnp.cumsum(onehot.astype(jnp.int32), axis=0) - 1
    rank = jnp.sum(jnp.where(onehot, rank_pd, 0), axis=1)
    match = onehot[:, :, None] & (rank_pd[:, :, None] == jnp.arange(cap, dtype=jnp.int32)[None, None, :])
    send_idx = jnp.where(jnp.any(match, axis=0), jnp.argmax(match, axis=0), npair)
    send = flat_pad[send_idx]
    send, _ = lax.optimization_barrier((send, finv))
    shifted = [send[c]]
    for k in range(1, C):
        out_k = lax.dynamic_index_in_dim(send, (c + k) % C, axis=0, keepdims=False)
        shifted.append(lax.ppermute(out_k, "col", [(i, (i + k) % C) for i in range(C)]))
    shifted = jnp.stack(shifted)
    recv = shifted[(c - jnp.arange(C, dtype=jnp.int32)) % C]
    recv_t = recv.transpose(1, 2, 0, 3).reshape(cap, MSLOT, C * Ec)
    recv_t = jnp.concatenate([recv_t, jnp.zeros((1, MSLOT, PANEL), jnp.float32)], axis=0)
    my_seg = c * G + jnp.arange(G, dtype=jnp.int32)
    seg_hit = tseg[:, :, None] == my_seg[None, None, :]
    rank2 = rank.reshape(nsub, 2)
    slot_tab = jnp.where(
        jnp.any(seg_hit, axis=1), jnp.sum(jnp.where(seg_hit, rank2[:, :, None], 0), axis=1), cap
    )

    has0, rank0, slot_r = seg0_slots(tseg, cap0)
    t0 = jnp.where(tseg[:, 0] == 0, 0, 1)
    sel = has0[:, None] & (rank0[:, None] == jnp.arange(cap0, dtype=jnp.int32)[None, :])
    sel_sub = jnp.argmax(sel, axis=0)
    zidx = jnp.where(jnp.any(sel, axis=0), sel_sub * 2 + t0[sel_sub], npair)
    z_local = flat_pad[zidx]
    z_all = lax.all_gather(z_local, "col", axis=0, tiled=False)
    z_rows = z_all.transpose(1, 2, 0, 3).reshape(cap0 * MSLOT, C * Ec)

    m_src = stiff[:, :PANEL]
    rps = W // R
    zps = cap0 * MSLOT // C
    got = [m_src[:rps]]
    for k in range(1, C):
        got.append(lax.ppermute(m_src[k * rps:(k + 1) * rps], AXES, [(i * C, i * C + k) for i in range(R)]))
    m_row = lax.all_gather(pick(c, got), "col", axis=0, tiled=True)
    slot_row = jnp.zeros((8, PANEL), jnp.float32).at[0, :nsub].set(slot_r.astype(jnp.float32))
    got = []
    for k in range(C):
        payload = jnp.concatenate(
            [m_src[k * rps:(k + 1) * rps], z_rows[k * zps:(k + 1) * zps], slot_row], axis=0
        )
        perm = [(i * C, ((i % ratio) * C + k) * C + i // ratio) for i in range(R)]
        got.append(lax.ppermute(payload, AXES, perm))
    col_parts = lax.all_gather(pick(r % C, got), "row", axis=0, tiled=False)
    m_col = col_parts[:, :rps].reshape(W, PANEL)
    z_col = col_parts[:, rps:rps + zps].reshape(ratio * cap0 * MSLOT, PANEL)

    slot_c = []
    for j in range(ratio):
        got_slot = col_parts[j * C, rps + zps, :nsub].astype(jnp.int32)
        slot_c.append(jnp.where(got_slot < cap0, j * cap0 + got_slot, ratio * cap0))
    slot_c = jnp.concatenate(slot_c)

    stacked = jnp.concatenate([m_row, m_col, z_rows, z_col], axis=0)
    solved = apply_inverse(stacked, finv)
    low_r = solved[:H]
    low_c = solved[H:H + W]
    lowmi_r = solved[H + W:H + W + cap0 * MSLOT]
    lowmi_c = solved[H + W + cap0 * MSLOT:]

    ones = jnp.ones((H // MSLOT,), jnp.int32)
    none = jnp.zeros((1,), jnp.int32)
    info = jnp.stack([jnp.int32(1), c * W, r * H, jnp.int32(0)]).astype(jnp.int32)
    reduced_ii = panel_update("array", stiff, low_r, low_c, ones, info, none, H, W)

    lmi = jnp.concatenate(
        [lowmi_r.reshape(cap0, MSLOT, PANEL), jnp.zeros((1, MSLOT, PANEL), jnp.float32)], axis=0
    )
    lmi_full = lmi[slot_r].reshape(nsub * MSLOT, PANEL)
    flags = has0.astype(jnp.int32)
    reduced_mi = panel_update(
        "gather", recv_t, lmi_full, low_c, flags, info, slot_tab.reshape(-1).astype(jnp.int32), nsub * MSLOT, W
    )

    nc = ratio * cap0
    lmc = jnp.concatenate(
        [lowmi_c.reshape(nc, MSLOT, PANEL), jnp.zeros((1, MSLOT, PANEL), jnp.float32)], axis=0
    )
    mode_width = ratio * nsub * MSLOT
    lmc_full = lmc[slot_c].reshape(mode_width, PANEL)
    diag_values = jnp.where(live, eigvals, 1.0).reshape(-1, 1)
    mode_rows = diag_values.shape[0]
    info_mm = jnp.stack([jnp.int32(0), c * mode_width, r * mode_rows, jnp.int32(0)]).astype(jnp.int32)
    reduced_mm = panel_update("diag", diag_values, lmi_full, lmc_full, flags, info_mm, none, mode_rows, mode_width)
    return (reduced_ii, reduced_mi, reduced_mm)


def solution(mesh):
    in_specs = (
        P("row", None, None),
        P("row", None, None, "col"),
        P("row"),
        P("row", None),
        P("row", None),
        P("row", "col"),
    )
    out_specs = (P("row", "col"), P("row", "col"), P("row", "col"))
    return jax.shard_map(
        per_device, mesh=mesh, in_specs=in_specs, out_specs=out_specs, check_vma=False
    )
```

```python
import functools

import jax
import jax.numpy as jnp
from jax import lax
from jax.sharding import PartitionSpec as P
from jax.experimental import pallas as pl
from jax.experimental.pallas import tpu as pltpu

MSLOT = 128
PANEL = 512
MOST = 2
SUB_ROW = 8

AXES = ("row", "col")
LEAF = 128


def mm3(a, b, dn):
    a_hi = a.astype(jnp.bfloat16)
    a_lo = (a - a_hi.astype(jnp.float32)).astype(jnp.bfloat16)
    b_hi = b.astype(jnp.bfloat16)
    b_lo = (b - b_hi.astype(jnp.float32)).astype(jnp.bfloat16)
    out = lax.dot_general(a_hi, b_hi, dn, preferred_element_type=jnp.float32)
    out = out + lax.dot_general(a_hi, b_lo, dn, preferred_element_type=jnp.float32)
    return out + lax.dot_general(a_lo, b_hi, dn, preferred_element_type=jnp.float32)


NN = (((1,), (0,)), ((), ()))
NT = (((1,), (1,)), ((), ()))


def leaf_inverse(d):
    n = d.shape[0]
    sub = lax.broadcasted_iota(jnp.int32, (n, n), 0)
    lane = lax.broadcasted_iota(jnp.int32, (n, n), 1)
    sub_c = lax.broadcasted_iota(jnp.int32, (n, 1), 0)
    lane_r = lax.broadcasted_iota(jnp.int32, (1, n), 1)
    eye = jnp.where(sub == lane, 1.0, 0.0).astype(jnp.float32)

    def step(k, carry):
        dm, em, xm = carry
        colk = jnp.sum(jnp.where(lane == k, dm, 0.0), axis=1, keepdims=True)
        rowk = jnp.sum(jnp.where(sub == k, dm, 0.0), axis=0, keepdims=True)
        dkk = jnp.sum(jnp.where(lane_r == k, rowk, 0.0), axis=1, keepdims=True)
        s = 1.0 / jnp.sqrt(dkk)
        lc = jnp.where(sub_c > k, colk * s, 0.0)
        lr = jnp.where(lane_r > k, rowk * s, 0.0)
        dm = dm - lc * lr
        erow = jnp.sum(jnp.where(sub == k, em, 0.0), axis=0, keepdims=True)
        xk = erow * s
        xm = jnp.where(sub == k, xk, xm)
        em = em - lc * xk
        return dm, em, xm

    _, _, xm = lax.fori_loop(0, n, step, (d, eye, jnp.zeros_like(d)))
    return xm


def chol_inv_kernel(a_ref, x_ref, w_ref, l_ref):
    n = a_ref.shape[0]
    nb = n // LEAF
    w_ref[...] = a_ref[...]
    for kb in range(nb):
        o = kb * LEAF
        blk = pl.ds(o, LEAF)
        xkk = leaf_inverse(w_ref[blk, blk])
        x_ref[blk, blk] = xkk
        if kb + 1 < nb:
            rest = pl.ds(o + LEAF, n - o - LEAF)
            panel = mm3(w_ref[rest, blk], xkk, NT)
            l_ref[rest, blk] = panel
            w_ref[rest, rest] = w_ref[rest, rest] - mm3(panel, panel, NT)
    for i in range(1, nb):
        bi = pl.ds(i * LEAF, LEAF)
        xii = x_ref[bi, bi]
        for j in range(i):
            bj = pl.ds(j * LEAF, LEAF)
            acc = None
            for k in range(j, i):
                bk = pl.ds(k * LEAF, LEAF)
                term = mm3(l_ref[bi, bk], x_ref[bk, bj], NN)
                acc = term if acc is None else acc + term
            x_ref[bi, bj] = -mm3(xii, acc, NN)
        for j in range(i + 1, nb):
            x_ref[bi, pl.ds(j * LEAF, LEAF)] = jnp.zeros((LEAF, LEAF), jnp.float32)
    x_ref[pl.ds(0, LEAF), pl.ds(LEAF, n - LEAF)] = jnp.zeros((LEAF, n - LEAF), jnp.float32)


def chol_inverse(a):
    n = a.shape[0]
    return pl.pallas_call(
        chol_inv_kernel,
        out_shape=jax.ShapeDtypeStruct((n, n), jnp.float32),
        cost_estimate=pl.CostEstimate(flops=60 * n ** 3, transcendentals=n, bytes_accessed=8 * n * n),
        in_specs=[pl.BlockSpec(memory_space=pltpu.VMEM)],
        out_specs=pl.BlockSpec(memory_space=pltpu.VMEM),
        scratch_shapes=[pltpu.VMEM((n, n), jnp.float32), pltpu.VMEM((n, n), jnp.float32)],
    )(a)


def split_bf16(x):
    hi = lax.reduce_precision(x, exponent_bits=8, mantissa_bits=7)
    return hi.astype(jnp.bfloat16), (x - hi).astype(jnp.bfloat16)


def update_kernel(kind, tm, width, nbase, flags_ref, info_ref, slots_ref, *refs):
    base_refs = refs[:nbase]
    a_ref, bhi_ref, blo_ref, out_ref = refs[nbase:]
    i = pl.program_id(0)
    active = flags_ref[i] != 0

    def base_cols(g):
        cols = pl.ds(g * PANEL, PANEL)
        if kind == "gather":
            return base_refs[g][0]
        if kind == "diag":
            rows = info_ref[2] + i * tm + lax.broadcasted_iota(jnp.int32, (tm, PANEL), 0)
            ids = info_ref[1] + g * PANEL + lax.broadcasted_iota(jnp.int32, (tm, PANEL), 1)
            return jnp.where(rows == ids, base_refs[0][...], 0.0)
        return base_refs[0][:, cols]

    @pl.when(active)
    def _():
        a = a_ref[...]
        a_hi = a.astype(jnp.bfloat16)
        a_lo = (a - a_hi.astype(jnp.float32)).astype(jnp.bfloat16)
        dn = (((1,), (1,)), ((), ()))
        for g in range(width // PANEL):
            rows = pl.ds(g * PANEL, PANEL)
            b_hi = bhi_ref[rows, :]
            acc = lax.dot_general(a_hi, b_hi, dn, preferred_element_type=jnp.float32)
            acc = acc + lax.dot_general(a_hi, blo_ref[rows, :], dn, preferred_element_type=jnp.float32)
            acc = acc + lax.dot_general(a_lo, b_hi, dn, preferred_element_type=jnp.float32)
            out_ref[:, pl.ds(g * PANEL, PANEL)] = base_cols(g) - acc

    @pl.when(jnp.logical_not(active))
    def _():
        for g in range(width // PANEL):
            out_ref[:, pl.ds(g * PANEL, PANEL)] = base_cols(g)

    @pl.when((info_ref[0] == 1) & (info_ref[1] == 0))
    def _():
        out_ref[:, pl.ds(0, PANEL)] = a_ref[...]


def panel_update(kind, base, a, b, flags, info, slots, rows, width):
    tm = MSLOT
    b_hi, b_lo = split_bf16(b)
    nseg = width // PANEL
    if kind == "gather":
        bases = [base] * nseg
        base_specs = [
            pl.BlockSpec((1, tm, PANEL), lambda i, f, n, s, g=g: (s[i * nseg + g], 0, 0)) for g in range(nseg)
        ]
    elif kind == "diag":
        bases = [base]
        base_specs = [pl.BlockSpec((tm, 1), lambda i, f, n, s: (i, 0))]
    else:
        bases = [base]
        base_specs = [pl.BlockSpec((tm, width), lambda i, f, n, s: (i, 0))]
    grid_spec = pltpu.PrefetchScalarGridSpec(
        num_scalar_prefetch=3,
        grid=(rows // tm,),
        in_specs=base_specs + [
            pl.BlockSpec((tm, PANEL), lambda i, f, n, s: (i, 0)),
            pl.BlockSpec((width, PANEL), lambda i, f, n, s: (0, 0)),
            pl.BlockSpec((width, PANEL), lambda i, f, n, s: (0, 0)),
        ],
        out_specs=pl.BlockSpec((tm, width), lambda i, f, n, s: (i, 0)),
    )
    flops = 6 * rows * width * PANEL
    cost = pl.CostEstimate(flops=flops, transcendentals=0, bytes_accessed=rows * width * 8 + width * PANEL * 4)
    return pl.pallas_call(
        functools.partial(update_kernel, kind, tm, width, len(bases)),
        grid_spec=grid_spec,
        out_shape=jax.ShapeDtypeStruct((rows, width), jnp.float32),
        cost_estimate=cost,
        compiler_params=pltpu.CompilerParams(vmem_limit_bytes=48 * 1024 * 1024),
    )(flags, info, slots, *bases, a, b_hi, b_lo)


def solve_kernel(x_ref, fhi_ref, flo_ref, out_ref):
    x = x_ref[...]
    x_hi = x.astype(jnp.bfloat16)
    x_lo = (x - x_hi.astype(jnp.float32)).astype(jnp.bfloat16)
    f_hi = fhi_ref[...]
    acc = lax.dot_general(x_hi, f_hi, NT, preferred_element_type=jnp.float32)
    acc = acc + lax.dot_general(x_hi, flo_ref[...], NT, preferred_element_type=jnp.float32)
    out_ref[...] = acc + lax.dot_general(x_lo, f_hi, NT, preferred_element_type=jnp.float32)


def apply_inverse(x, finv):
    rows = x.shape[0]
    tm = 256 if rows % 256 == 0 else MSLOT
    f_hi, f_lo = split_bf16(finv)
    return pl.pallas_call(
        solve_kernel,
        grid=(rows // tm,),
        in_specs=[
            pl.BlockSpec((tm, PANEL), lambda i: (i, 0)),
            pl.BlockSpec((PANEL, PANEL), lambda i: (0, 0)),
            pl.BlockSpec((PANEL, PANEL), lambda i: (0, 0)),
        ],
        out_specs=pl.BlockSpec((tm, PANEL), lambda i: (i, 0)),
        out_shape=jax.ShapeDtypeStruct((rows, PANEL), jnp.float32),
        cost_estimate=pl.CostEstimate(flops=6 * rows * PANEL * PANEL, transcendentals=0, bytes_accessed=8 * rows * PANEL),
    )(x, f_hi, f_lo)


def dot_t(left, right):
    contract = (((1,), (1,)), ((), ()))
    l_hi, l_lo = split_bf16(left)
    r_hi, r_lo = split_bf16(right)
    out = lax.dot_general(l_hi, r_hi, contract, preferred_element_type=jnp.float32)
    out = out + lax.dot_general(l_hi, r_lo, contract, preferred_element_type=jnp.float32)
    return out + lax.dot_general(l_lo, r_hi, contract, preferred_element_type=jnp.float32)


def pick(index, options):
    out = options[0]
    for i in range(1, len(options)):
        out = jnp.where(index == i, options[i], out)
    return out


def seg0_slots(tseg, cap0):
    has0 = jnp.any(tseg == 0, axis=1)
    rank0 = jnp.cumsum(has0.astype(jnp.int32)) - 1
    slot = jnp.where(has0, rank0, cap0)
    return has0, rank0, slot


def per_device(eigvecs, coupling, mode_counts, tree_segments, eigvals, stiff):
    R = lax.axis_size("row")
    C = lax.axis_size("col")
    r = lax.axis_index("row")
    c = lax.axis_index("col")
    nsub = eigvecs.shape[0]
    H, W = stiff.shape
    Ec = coupling.shape[3]
    G = W // PANEL
    ratio = R // C
    npair = 2 * nsub
    cap = min(MOST * G * ((nsub + SUB_ROW - 1) // SUB_ROW), npair)
    cap0 = min(MOST * ((nsub + SUB_ROW - 1) // SUB_ROW), nsub)

    live = jnp.arange(MSLOT, dtype=jnp.int32)[None, :] < mode_counts[:, None]
    pieces = jnp.einsum("sim,sitp->stmp", eigvecs, coupling, preferred_element_type=jnp.float32)
    pieces = pieces * live.astype(jnp.float32)[:, None, :, None]
    flat = pieces.reshape(npair, MSLOT, Ec)
    flat_pad = jnp.concatenate([flat, jnp.zeros((1, MSLOT, Ec), jnp.float32)], axis=0)

    kpp_src = stiff[:PANEL, :PANEL]
    rs = PANEL // R
    got = [kpp_src[:rs]]
    for i in range(1, R):
        got.append(lax.ppermute(kpp_src[i * rs:(i + 1) * rs], AXES, [(0, i * C)]))
    kpp_part = pick(r, got)
    kpp_col0 = lax.all_gather(kpp_part, "row", axis=0, tiled=True)
    cs = PANEL // C
    got = [kpp_col0[:cs]]
    for k in range(1, C):
        got.append(lax.ppermute(kpp_col0[k * cs:(k + 1) * cs], AXES, [(i * C, i * C + k) for i in range(R)]))
    kpp = lax.all_gather(pick(c, got), "col", axis=0, tiled=True)

    finv = chol_inverse(kpp)

    tseg = tree_segments
    dest = (tseg // G).reshape(npair)
    onehot = dest[:, None] == jnp.arange(C, dtype=jnp.int32)[None, :]
    rank_pd = jnp.cumsum(onehot.astype(jnp.int32), axis=0) - 1
    rank = jnp.sum(jnp.where(onehot, rank_pd, 0), axis=1)
    match = onehot[:, :, None] & (rank_pd[:, :, None] == jnp.arange(cap, dtype=jnp.int32)[None, None, :])
    send_idx = jnp.where(jnp.any(match, axis=0), jnp.argmax(match, axis=0), npair)
    send = flat_pad[send_idx]
    send, _ = lax.optimization_barrier((send, finv))
    shifted = [send[c]]
    for k in range(1, C):
        out_k = lax.dynamic_index_in_dim(send, (c + k) % C, axis=0, keepdims=False)
        shifted.append(lax.ppermute(out_k, "col", [(i, (i + k) % C) for i in range(C)]))
    shifted = jnp.stack(shifted)
    recv = shifted[(c - jnp.arange(C, dtype=jnp.int32)) % C]
    recv_t = recv.transpose(1, 2, 0, 3).reshape(cap, MSLOT, C * Ec)
    recv_t = jnp.concatenate([recv_t, jnp.zeros((1, MSLOT, PANEL), jnp.float32)], axis=0)
    my_seg = c * G + jnp.arange(G, dtype=jnp.int32)
    seg_hit = tseg[:, :, None] == my_seg[None, None, :]
    rank2 = rank.reshape(nsub, 2)
    slot_tab = jnp.where(
        jnp.any(seg_hit, axis=1), jnp.sum(jnp.where(seg_hit, rank2[:, :, None], 0), axis=1), cap
    )

    has0, rank0, slot_r = seg0_slots(tseg, cap0)
    t0 = jnp.where(tseg[:, 0] == 0, 0, 1)
    sel = has0[:, None] & (rank0[:, None] == jnp.arange(cap0, dtype=jnp.int32)[None, :])
    sel_sub = jnp.argmax(sel, axis=0)
    zidx = jnp.where(jnp.any(sel, axis=0), sel_sub * 2 + t0[sel_sub], npair)
    z_local = flat_pad[zidx]
    z_all = lax.all_gather(z_local, "col", axis=0, tiled=False)
    z_rows = z_all.transpose(1, 2, 0, 3).reshape(cap0 * MSLOT, C * Ec)

    m_src = stiff[:, :PANEL]
    rps = W // R
    zps = cap0 * MSLOT // C
    got = [m_src[:rps]]
    for k in range(1, C):
        got.append(lax.ppermute(m_src[k * rps:(k + 1) * rps], AXES, [(i * C, i * C + k) for i in range(R)]))
    a_slice = pick(c, got)
    m_row = lax.all_gather(a_slice, "col", axis=0, tiled=True)
    slot_row = jnp.zeros((8, PANEL), jnp.float32).at[0, :nsub].set(slot_r.astype(jnp.float32))
    payload = jnp.concatenate([a_slice, lax.dynamic_slice_in_dim(z_rows, c * zps, zps), slot_row], axis=0)
    perm = [(i * C + k, ((i % ratio) * C + k) * C + i // ratio) for i in range(R) for k in range(C)]
    b_slice = lax.ppermute(payload, AXES, perm)
    col_parts = lax.all_gather(b_slice, "row", axis=0, tiled=False)
    m_col = col_parts[:, :rps].reshape(W, PANEL)
    z_col = col_parts[:, rps:rps + zps].reshape(ratio * cap0 * MSLOT, PANEL)

    slot_c = []
    for j in range(ratio):
        got_slot = col_parts[j * C, rps + zps, :nsub].astype(jnp.int32)
        slot_c.append(jnp.where(got_slot < cap0, j * cap0 + got_slot, ratio * cap0))
    slot_c = jnp.concatenate(slot_c)

    stacked = jnp.concatenate([m_row, m_col, z_rows, z_col], axis=0)
    solved = apply_inverse(stacked, finv)
    low_r = solved[:H]
    low_c = solved[H:H + W]
    lowmi_r = solved[H + W:H + W + cap0 * MSLOT]
    lowmi_c = solved[H + W + cap0 * MSLOT:]

    ones = jnp.ones((H // MSLOT,), jnp.int32)
    none = jnp.zeros((1,), jnp.int32)
    info = jnp.stack([jnp.int32(1), c * W, r * H, jnp.int32(0)]).astype(jnp.int32)
    reduced_ii = panel_update("array", stiff, low_r, low_c, ones, info, none, H, W)

    lmi = jnp.concatenate(
        [lowmi_r.reshape(cap0, MSLOT, PANEL), jnp.zeros((1, MSLOT, PANEL), jnp.float32)], axis=0
    )
    lmi_full = lmi[slot_r].reshape(nsub * MSLOT, PANEL)
    flags = has0.astype(jnp.int32)
    reduced_mi = panel_update(
        "gather", recv_t, lmi_full, low_c, flags, info, slot_tab.reshape(-1).astype(jnp.int32), nsub * MSLOT, W
    )

    nc = ratio * cap0
    lmc = jnp.concatenate(
        [lowmi_c.reshape(nc, MSLOT, PANEL), jnp.zeros((1, MSLOT, PANEL), jnp.float32)], axis=0
    )
    mode_width = ratio * nsub * MSLOT
    lmc_full = lmc[slot_c].reshape(mode_width, PANEL)
    diag_values = jnp.where(live, eigvals, 1.0).reshape(-1, 1)
    mode_rows = diag_values.shape[0]
    info_mm = jnp.stack([jnp.int32(0), c * mode_width, r * mode_rows, jnp.int32(0)]).astype(jnp.int32)
    reduced_mm = panel_update("diag", diag_values, lmi_full, lmc_full, flags, info_mm, none, mode_rows, mode_width)
    return (reduced_ii, reduced_mi, reduced_mm)


def solution(mesh):
    in_specs = (
        P("row", None, None),
        P("row", None, None, "col"),
        P("row"),
        P("row", None),
        P("row", None),
        P("row", "col"),
    )
    out_specs = (P("row", "col"), P("row", "col"), P("row", "col"))
    return jax.shard_map(
        per_device, mesh=mesh, in_specs=in_specs, out_specs=out_specs, check_vma=False
    )
```

```python
import functools

import jax
import jax.numpy as jnp
from jax import lax
from jax.sharding import PartitionSpec as P
from jax.experimental import pallas as pl
from jax.experimental.pallas import tpu as pltpu

MSLOT = 128
PANEL = 512
MOST = 2
SUB_ROW = 8

AXES = ("row", "col")
LEAF = 128


def mm3(a, b, dn):
    a_hi = a.astype(jnp.bfloat16)
    a_lo = (a - a_hi.astype(jnp.float32)).astype(jnp.bfloat16)
    b_hi = b.astype(jnp.bfloat16)
    b_lo = (b - b_hi.astype(jnp.float32)).astype(jnp.bfloat16)
    out = lax.dot_general(a_hi, b_hi, dn, preferred_element_type=jnp.float32)
    out = out + lax.dot_general(a_hi, b_lo, dn, preferred_element_type=jnp.float32)
    return out + lax.dot_general(a_lo, b_hi, dn, preferred_element_type=jnp.float32)


NN = (((1,), (0,)), ((), ()))
NT = (((1,), (1,)), ((), ()))


def leaf_inverse(d):
    n = d.shape[0]
    sub = lax.broadcasted_iota(jnp.int32, (n, n), 0)
    lane = lax.broadcasted_iota(jnp.int32, (n, n), 1)
    sub_c = lax.broadcasted_iota(jnp.int32, (n, 1), 0)
    lane_r = lax.broadcasted_iota(jnp.int32, (1, n), 1)
    eye = jnp.where(sub == lane, 1.0, 0.0).astype(jnp.float32)

    def step(k, carry):
        dm, em, xm = carry
        colk = jnp.sum(jnp.where(lane == k, dm, 0.0), axis=1, keepdims=True)
        rowk = jnp.sum(jnp.where(sub == k, dm, 0.0), axis=0, keepdims=True)
        dkk = jnp.sum(jnp.where(lane_r == k, rowk, 0.0), axis=1, keepdims=True)
        s = 1.0 / jnp.sqrt(dkk)
        lc = jnp.where(sub_c > k, colk * s, 0.0)
        lr = jnp.where(lane_r > k, rowk * s, 0.0)
        dm = dm - lc * lr
        erow = jnp.sum(jnp.where(sub == k, em, 0.0), axis=0, keepdims=True)
        xk = erow * s
        xm = jnp.where(sub == k, xk, xm)
        em = em - lc * xk
        return dm, em, xm

    _, _, xm = lax.fori_loop(0, n, step, (d, eye, jnp.zeros_like(d)))
    return xm


def chol_inv_kernel(a_ref, x_ref, w_ref, l_ref):
    n = a_ref.shape[0]
    nb = n // LEAF
    w_ref[...] = a_ref[...]
    for kb in range(nb):
        o = kb * LEAF
        blk = pl.ds(o, LEAF)
        xkk = leaf_inverse(w_ref[blk, blk])
        x_ref[blk, blk] = xkk
        if kb + 1 < nb:
            rest = pl.ds(o + LEAF, n - o - LEAF)
            panel = mm3(w_ref[rest, blk], xkk, NT)
            l_ref[rest, blk] = panel
            w_ref[rest, rest] = w_ref[rest, rest] - mm3(panel, panel, NT)
    for i in range(1, nb):
        bi = pl.ds(i * LEAF, LEAF)
        xii = x_ref[bi, bi]
        for j in range(i):
            bj = pl.ds(j * LEAF, LEAF)
            acc = None
            for k in range(j, i):
                bk = pl.ds(k * LEAF, LEAF)
                term = mm3(l_ref[bi, bk], x_ref[bk, bj], NN)
                acc = term if acc is None else acc + term
            x_ref[bi, bj] = -mm3(xii, acc, NN)
        for j in range(i + 1, nb):
            x_ref[bi, pl.ds(j * LEAF, LEAF)] = jnp.zeros((LEAF, LEAF), jnp.float32)
    x_ref[pl.ds(0, LEAF), pl.ds(LEAF, n - LEAF)] = jnp.zeros((LEAF, n - LEAF), jnp.float32)


def chol_inverse(a):
    n = a.shape[0]
    return pl.pallas_call(
        chol_inv_kernel,
        out_shape=jax.ShapeDtypeStruct((n, n), jnp.float32),
        cost_estimate=pl.CostEstimate(flops=800 * n ** 3, transcendentals=n, bytes_accessed=8 * n * n),
        in_specs=[pl.BlockSpec(memory_space=pltpu.VMEM)],
        out_specs=pl.BlockSpec(memory_space=pltpu.VMEM),
        scratch_shapes=[pltpu.VMEM((n, n), jnp.float32), pltpu.VMEM((n, n), jnp.float32)],
    )(a)


def split_bf16(x):
    hi = lax.reduce_precision(x, exponent_bits=8, mantissa_bits=7)
    return hi.astype(jnp.bfloat16), (x - hi).astype(jnp.bfloat16)


def update_kernel(kind, tm, width, nbase, flags_ref, info_ref, slots_ref, *refs):
    base_refs = refs[:nbase]
    a_ref, bhi_ref, blo_ref, out_ref = refs[nbase:]
    i = pl.program_id(0)
    active = flags_ref[i] != 0

    def base_cols(g):
        cols = pl.ds(g * PANEL, PANEL)
        if kind == "gather":
            return base_refs[g][0]
        if kind == "diag":
            rows = info_ref[2] + i * tm + lax.broadcasted_iota(jnp.int32, (tm, PANEL), 0)
            ids = info_ref[1] + g * PANEL + lax.broadcasted_iota(jnp.int32, (tm, PANEL), 1)
            return jnp.where(rows == ids, base_refs[0][...], 0.0)
        return base_refs[0][:, cols]

    @pl.when(active)
    def _():
        a = a_ref[...]
        a_hi = a.astype(jnp.bfloat16)
        a_lo = (a - a_hi.astype(jnp.float32)).astype(jnp.bfloat16)
        dn = (((1,), (1,)), ((), ()))
        for g in range(width // PANEL):
            rows = pl.ds(g * PANEL, PANEL)
            b_hi = bhi_ref[rows, :]
            acc = lax.dot_general(a_hi, b_hi, dn, preferred_element_type=jnp.float32)
            acc = acc + lax.dot_general(a_hi, blo_ref[rows, :], dn, preferred_element_type=jnp.float32)
            acc = acc + lax.dot_general(a_lo, b_hi, dn, preferred_element_type=jnp.float32)
            out_ref[:, pl.ds(g * PANEL, PANEL)] = base_cols(g) - acc

    @pl.when(jnp.logical_not(active))
    def _():
        for g in range(width // PANEL):
            out_ref[:, pl.ds(g * PANEL, PANEL)] = base_cols(g)

    @pl.when((info_ref[0] == 1) & (info_ref[1] == 0))
    def _():
        out_ref[:, pl.ds(0, PANEL)] = a_ref[...]


def panel_update(kind, base, a, b, flags, info, slots, rows, width):
    tm = MSLOT
    b_hi, b_lo = split_bf16(b)
    nseg = width // PANEL
    if kind == "gather":
        bases = [base] * nseg
        base_specs = [
            pl.BlockSpec((1, tm, PANEL), lambda i, f, n, s, g=g: (s[i * nseg + g], 0, 0)) for g in range(nseg)
        ]
    elif kind == "diag":
        bases = [base]
        base_specs = [pl.BlockSpec((tm, 1), lambda i, f, n, s: (i, 0))]
    else:
        bases = [base]
        base_specs = [pl.BlockSpec((tm, width), lambda i, f, n, s: (i, 0))]
    grid_spec = pltpu.PrefetchScalarGridSpec(
        num_scalar_prefetch=3,
        grid=(rows // tm,),
        in_specs=base_specs + [
            pl.BlockSpec((tm, PANEL), lambda i, f, n, s: (i, 0)),
            pl.BlockSpec((width, PANEL), lambda i, f, n, s: (0, 0)),
            pl.BlockSpec((width, PANEL), lambda i, f, n, s: (0, 0)),
        ],
        out_specs=pl.BlockSpec((tm, width), lambda i, f, n, s: (i, 0)),
    )
    flops = 6 * rows * width * PANEL
    cost = pl.CostEstimate(flops=flops, transcendentals=0, bytes_accessed=rows * width * 8 + width * PANEL * 4)
    return pl.pallas_call(
        functools.partial(update_kernel, kind, tm, width, len(bases)),
        grid_spec=grid_spec,
        out_shape=jax.ShapeDtypeStruct((rows, width), jnp.float32),
        cost_estimate=cost,
        compiler_params=pltpu.CompilerParams(vmem_limit_bytes=48 * 1024 * 1024),
    )(flags, info, slots, *bases, a, b_hi, b_lo)


def solve_kernel(x_ref, fhi_ref, flo_ref, out_ref):
    x = x_ref[...]
    x_hi = x.astype(jnp.bfloat16)
    x_lo = (x - x_hi.astype(jnp.float32)).astype(jnp.bfloat16)
    f_hi = fhi_ref[...]
    acc = lax.dot_general(x_hi, f_hi, NT, preferred_element_type=jnp.float32)
    acc = acc + lax.dot_general(x_hi, flo_ref[...], NT, preferred_element_type=jnp.float32)
    out_ref[...] = acc + lax.dot_general(x_lo, f_hi, NT, preferred_element_type=jnp.float32)


def apply_inverse(x, finv):
    rows = x.shape[0]
    tm = 256 if rows % 256 == 0 else MSLOT
    f_hi, f_lo = split_bf16(finv)
    return pl.pallas_call(
        solve_kernel,
        grid=(rows // tm,),
        in_specs=[
            pl.BlockSpec((tm, PANEL), lambda i: (i, 0)),
            pl.BlockSpec((PANEL, PANEL), lambda i: (0, 0)),
            pl.BlockSpec((PANEL, PANEL), lambda i: (0, 0)),
        ],
        out_specs=pl.BlockSpec((tm, PANEL), lambda i: (i, 0)),
        out_shape=jax.ShapeDtypeStruct((rows, PANEL), jnp.float32),
        cost_estimate=pl.CostEstimate(flops=6 * rows * PANEL * PANEL, transcendentals=0, bytes_accessed=8 * rows * PANEL),
    )(x, f_hi, f_lo)


def dot_t(left, right):
    contract = (((1,), (1,)), ((), ()))
    l_hi, l_lo = split_bf16(left)
    r_hi, r_lo = split_bf16(right)
    out = lax.dot_general(l_hi, r_hi, contract, preferred_element_type=jnp.float32)
    out = out + lax.dot_general(l_hi, r_lo, contract, preferred_element_type=jnp.float32)
    return out + lax.dot_general(l_lo, r_hi, contract, preferred_element_type=jnp.float32)


def pick(index, options):
    out = options[0]
    for i in range(1, len(options)):
        out = jnp.where(index == i, options[i], out)
    return out


def seg0_slots(tseg, cap0):
    has0 = jnp.any(tseg == 0, axis=1)
    rank0 = jnp.cumsum(has0.astype(jnp.int32)) - 1
    slot = jnp.where(has0, rank0, cap0)
    return has0, rank0, slot


def per_device(eigvecs, coupling, mode_counts, tree_segments, eigvals, stiff):
    R = lax.axis_size("row")
    C = lax.axis_size("col")
    r = lax.axis_index("row")
    c = lax.axis_index("col")
    nsub = eigvecs.shape[0]
    H, W = stiff.shape
    Ec = coupling.shape[3]
    G = W // PANEL
    ratio = R // C
    npair = 2 * nsub
    cap = min(MOST * G * ((nsub + SUB_ROW - 1) // SUB_ROW), npair)
    cap0 = min(MOST * ((nsub + SUB_ROW - 1) // SUB_ROW), nsub)

    live = jnp.arange(MSLOT, dtype=jnp.int32)[None, :] < mode_counts[:, None]
    pieces = jnp.einsum("sim,sitp->stmp", eigvecs, coupling, preferred_element_type=jnp.float32)
    pieces = pieces * live.astype(jnp.float32)[:, None, :, None]
    flat = pieces.reshape(npair, MSLOT, Ec)
    flat_pad = jnp.concatenate([flat, jnp.zeros((1, MSLOT, Ec), jnp.float32)], axis=0)

    kpp_src = stiff[:PANEL, :PANEL]
    rs = PANEL // R
    got = [kpp_src[:rs]]
    for i in range(1, R):
        got.append(lax.ppermute(kpp_src[i * rs:(i + 1) * rs], AXES, [(0, i * C)]))
    kpp_part = pick(r, got)
    kpp_col0 = lax.all_gather(kpp_part, "row", axis=0, tiled=True)
    cs = PANEL // C
    got = [kpp_col0[:cs]]
    for k in range(1, C):
        got.append(lax.ppermute(kpp_col0[k * cs:(k + 1) * cs], AXES, [(i * C, i * C + k) for i in range(R)]))
    kpp = lax.all_gather(pick(c, got), "col", axis=0, tiled=True)

    finv = chol_inverse(kpp)

    tseg = tree_segments
    dest = (tseg // G).reshape(npair)
    onehot = dest[:, None] == jnp.arange(C, dtype=jnp.int32)[None, :]
    rank_pd = jnp.cumsum(onehot.astype(jnp.int32), axis=0) - 1
    rank = jnp.sum(jnp.where(onehot, rank_pd, 0), axis=1)
    match = onehot[:, :, None] & (rank_pd[:, :, None] == jnp.arange(cap, dtype=jnp.int32)[None, None, :])
    send_idx = jnp.where(jnp.any(match, axis=0), jnp.argmax(match, axis=0), npair)
    send = flat_pad[send_idx]
    shifted = [send[c]]
    for k in range(1, C):
        out_k = lax.dynamic_index_in_dim(send, (c + k) % C, axis=0, keepdims=False)
        shifted.append(lax.ppermute(out_k, "col", [(i, (i + k) % C) for i in range(C)]))
    shifted = jnp.stack(shifted)
    recv = shifted[(c - jnp.arange(C, dtype=jnp.int32)) % C]
    recv_t = recv.transpose(1, 2, 0, 3).reshape(cap, MSLOT, C * Ec)
    recv_t = jnp.concatenate([recv_t, jnp.zeros((1, MSLOT, PANEL), jnp.float32)], axis=0)
    my_seg = c * G + jnp.arange(G, dtype=jnp.int32)
    seg_hit = tseg[:, :, None] == my_seg[None, None, :]
    rank2 = rank.reshape(nsub, 2)
    slot_tab = jnp.where(
        jnp.any(seg_hit, axis=1), jnp.sum(jnp.where(seg_hit, rank2[:, :, None], 0), axis=1), cap
    )

    has0, rank0, slot_r = seg0_slots(tseg, cap0)
    t0 = jnp.where(tseg[:, 0] == 0, 0, 1)
    sel = has0[:, None] & (rank0[:, None] == jnp.arange(cap0, dtype=jnp.int32)[None, :])
    sel_sub = jnp.argmax(sel, axis=0)
    zidx = jnp.where(jnp.any(sel, axis=0), sel_sub * 2 + t0[sel_sub], npair)
    z_local = flat_pad[zidx]
    z_all = lax.all_gather(z_local, "col", axis=0, tiled=False)
    z_rows = z_all.transpose(1, 2, 0, 3).reshape(cap0 * MSLOT, C * Ec)

    m_src = stiff[:, :PANEL]
    rps = W // R
    zps = cap0 * MSLOT // C
    got = [m_src[:rps]]
    for k in range(1, C):
        got.append(lax.ppermute(m_src[k * rps:(k + 1) * rps], AXES, [(i * C, i * C + k) for i in range(R)]))
    a_slice = pick(c, got)
    m_row = lax.all_gather(a_slice, "col", axis=0, tiled=True)
    slot_row = jnp.zeros((8, PANEL), jnp.float32).at[0, :nsub].set(slot_r.astype(jnp.float32))
    payload = jnp.concatenate([a_slice, lax.dynamic_slice_in_dim(z_rows, c * zps, zps), slot_row], axis=0)
    perm = [(i * C + k, ((i % ratio) * C + k) * C + i // ratio) for i in range(R) for k in range(C)]
    b_slice = lax.ppermute(payload, AXES, perm)
    col_parts = lax.all_gather(b_slice, "row", axis=0, tiled=False)
    m_col = col_parts[:, :rps].reshape(W, PANEL)
    z_col = col_parts[:, rps:rps + zps].reshape(ratio * cap0 * MSLOT, PANEL)

    slot_c = []
    for j in range(ratio):
        got_slot = col_parts[j * C, rps + zps, :nsub].astype(jnp.int32)
        slot_c.append(jnp.where(got_slot < cap0, j * cap0 + got_slot, ratio * cap0))
    slot_c = jnp.concatenate(slot_c)

    stacked = jnp.concatenate([m_row, m_col, z_rows, z_col], axis=0)
    solved = apply_inverse(stacked, finv)
    low_r = solved[:H]
    low_c = solved[H:H + W]
    lowmi_r = solved[H + W:H + W + cap0 * MSLOT]
    lowmi_c = solved[H + W + cap0 * MSLOT:]

    ones = jnp.ones((H // MSLOT,), jnp.int32)
    none = jnp.zeros((1,), jnp.int32)
    info = jnp.stack([jnp.int32(1), c * W, r * H, jnp.int32(0)]).astype(jnp.int32)
    reduced_ii = panel_update("array", stiff, low_r, low_c, ones, info, none, H, W)

    lmi = jnp.concatenate(
        [lowmi_r.reshape(cap0, MSLOT, PANEL), jnp.zeros((1, MSLOT, PANEL), jnp.float32)], axis=0
    )
    lmi_full = lmi[slot_r].reshape(nsub * MSLOT, PANEL)
    flags = has0.astype(jnp.int32)
    reduced_mi = panel_update(
        "gather", recv_t, lmi_full, low_c, flags, info, slot_tab.reshape(-1).astype(jnp.int32), nsub * MSLOT, W
    )

    nc = ratio * cap0
    lmc = jnp.concatenate(
        [lowmi_c.reshape(nc, MSLOT, PANEL), jnp.zeros((1, MSLOT, PANEL), jnp.float32)], axis=0
    )
    mode_width = ratio * nsub * MSLOT
    lmc_full = lmc[slot_c].reshape(mode_width, PANEL)
    diag_values = jnp.where(live, eigvals, 1.0).reshape(-1, 1)
    mode_rows = diag_values.shape[0]
    info_mm = jnp.stack([jnp.int32(0), c * mode_width, r * mode_rows, jnp.int32(0)]).astype(jnp.int32)
    reduced_mm = panel_update("diag", diag_values, lmi_full, lmc_full, flags, info_mm, none, mode_rows, mode_width)
    return (reduced_ii, reduced_mi, reduced_mm)


def solution(mesh):
    in_specs = (
        P("row", None, None),
        P("row", None, None, "col"),
        P("row"),
        P("row", None),
        P("row", None),
        P("row", "col"),
    )
    out_specs = (P("row", "col"), P("row", "col"), P("row", "col"))
    return jax.shard_map(
        per_device, mesh=mesh, in_specs=in_specs, out_specs=out_specs, check_vma=False
    )
```

```python
import functools

import jax
import jax.numpy as jnp
from jax import lax
from jax.sharding import PartitionSpec as P
from jax.experimental import pallas as pl
from jax.experimental.pallas import tpu as pltpu

MSLOT = 128
PANEL = 512
MOST = 2
SUB_ROW = 8

AXES = ("row", "col")
LEAF = 128


def mm3(a, b, dn):
    a_hi = a.astype(jnp.bfloat16)
    a_lo = (a - a_hi.astype(jnp.float32)).astype(jnp.bfloat16)
    b_hi = b.astype(jnp.bfloat16)
    b_lo = (b - b_hi.astype(jnp.float32)).astype(jnp.bfloat16)
    out = lax.dot_general(a_hi, b_hi, dn, preferred_element_type=jnp.float32)
    out = out + lax.dot_general(a_hi, b_lo, dn, preferred_element_type=jnp.float32)
    return out + lax.dot_general(a_lo, b_hi, dn, preferred_element_type=jnp.float32)


NN = (((1,), (0,)), ((), ()))
NT = (((1,), (1,)), ((), ()))


def leaf_inverse(d):
    n = d.shape[0]
    sub = lax.broadcasted_iota(jnp.int32, (n, n), 0)
    lane = lax.broadcasted_iota(jnp.int32, (n, n), 1)
    sub_c = lax.broadcasted_iota(jnp.int32, (n, 1), 0)
    lane_r = lax.broadcasted_iota(jnp.int32, (1, n), 1)
    eye = jnp.where(sub == lane, 1.0, 0.0).astype(jnp.float32)

    def step(k, carry):
        dm, em, xm = carry
        colk = jnp.sum(jnp.where(lane == k, dm, 0.0), axis=1, keepdims=True)
        rowk = jnp.sum(jnp.where(sub == k, dm, 0.0), axis=0, keepdims=True)
        dkk = jnp.sum(jnp.where(lane_r == k, rowk, 0.0), axis=1, keepdims=True)
        s = 1.0 / jnp.sqrt(dkk)
        lc = jnp.where(sub_c > k, colk * s, 0.0)
        lr = jnp.where(lane_r > k, rowk * s, 0.0)
        dm = dm - lc * lr
        erow = jnp.sum(jnp.where(sub == k, em, 0.0), axis=0, keepdims=True)
        xk = erow * s
        xm = jnp.where(sub == k, xk, xm)
        em = em - lc * xk
        return dm, em, xm

    _, _, xm = lax.fori_loop(0, n, step, (d, eye, jnp.zeros_like(d)))
    return xm


def chol_inv_kernel(a_ref, x_ref, w_ref, l_ref):
    n = a_ref.shape[0]
    nb = n // LEAF
    w_ref[...] = a_ref[...]
    for kb in range(nb):
        o = kb * LEAF
        blk = pl.ds(o, LEAF)
        xkk = leaf_inverse(w_ref[blk, blk])
        x_ref[blk, blk] = xkk
        if kb + 1 < nb:
            rest = pl.ds(o + LEAF, n - o - LEAF)
            panel = mm3(w_ref[rest, blk], xkk, NT)
            l_ref[rest, blk] = panel
            w_ref[rest, rest] = w_ref[rest, rest] - mm3(panel, panel, NT)
    for i in range(1, nb):
        bi = pl.ds(i * LEAF, LEAF)
        xii = x_ref[bi, bi]
        for j in range(i):
            bj = pl.ds(j * LEAF, LEAF)
            acc = None
            for k in range(j, i):
                bk = pl.ds(k * LEAF, LEAF)
                term = mm3(l_ref[bi, bk], x_ref[bk, bj], NN)
                acc = term if acc is None else acc + term
            x_ref[bi, bj] = -mm3(xii, acc, NN)
        for j in range(i + 1, nb):
            x_ref[bi, pl.ds(j * LEAF, LEAF)] = jnp.zeros((LEAF, LEAF), jnp.float32)
    x_ref[pl.ds(0, LEAF), pl.ds(LEAF, n - LEAF)] = jnp.zeros((LEAF, n - LEAF), jnp.float32)


def chol_inverse(a):
    n = a.shape[0]
    return pl.pallas_call(
        chol_inv_kernel,
        out_shape=jax.ShapeDtypeStruct((n, n), jnp.float32),
        cost_estimate=pl.CostEstimate(flops=800 * n ** 3, transcendentals=n, bytes_accessed=8 * n * n),
        in_specs=[pl.BlockSpec(memory_space=pltpu.VMEM)],
        out_specs=pl.BlockSpec(memory_space=pltpu.VMEM),
        scratch_shapes=[pltpu.VMEM((n, n), jnp.float32), pltpu.VMEM((n, n), jnp.float32)],
    )(a)


def split_bf16(x):
    hi = lax.reduce_precision(x, exponent_bits=8, mantissa_bits=7)
    return hi.astype(jnp.bfloat16), (x - hi).astype(jnp.bfloat16)


def update_kernel(kind, tm, width, nbase, flags_ref, info_ref, slots_ref, *refs):
    base_refs = refs[:nbase]
    a_ref, bhi_ref, blo_ref, out_ref = refs[nbase:]
    i = pl.program_id(0)
    active = flags_ref[i] != 0

    def base_cols(g):
        cols = pl.ds(g * PANEL, PANEL)
        if kind == "gather":
            return base_refs[g][0]
        if kind == "diag":
            rows = info_ref[2] + i * tm + lax.broadcasted_iota(jnp.int32, (tm, PANEL), 0)
            ids = info_ref[1] + g * PANEL + lax.broadcasted_iota(jnp.int32, (tm, PANEL), 1)
            return jnp.where(rows == ids, base_refs[0][...], 0.0)
        return base_refs[0][:, cols]

    @pl.when(active)
    def _():
        a = a_ref[...]
        a_hi = a.astype(jnp.bfloat16)
        a_lo = (a - a_hi.astype(jnp.float32)).astype(jnp.bfloat16)
        dn = (((1,), (1,)), ((), ()))
        for g in range(width // PANEL):
            rows = pl.ds(g * PANEL, PANEL)
            b_hi = bhi_ref[rows, :]
            acc = lax.dot_general(a_hi, b_hi, dn, preferred_element_type=jnp.float32)
            acc = acc + lax.dot_general(a_hi, blo_ref[rows, :], dn, preferred_element_type=jnp.float32)
            acc = acc + lax.dot_general(a_lo, b_hi, dn, preferred_element_type=jnp.float32)
            out_ref[:, pl.ds(g * PANEL, PANEL)] = base_cols(g) - acc

    @pl.when(jnp.logical_not(active))
    def _():
        for g in range(width // PANEL):
            out_ref[:, pl.ds(g * PANEL, PANEL)] = base_cols(g)

    @pl.when((info_ref[0] == 1) & (info_ref[1] == 0))
    def _():
        out_ref[:, pl.ds(0, PANEL)] = a_ref[...]


def panel_update(kind, base, a, b_hi, b_lo, flags, info, slots, rows, width):
    tm = MSLOT
    nseg = width // PANEL
    if kind == "gather":
        bases = [base] * nseg
        base_specs = [
            pl.BlockSpec((1, tm, PANEL), lambda i, f, n, s, g=g: (s[i * nseg + g], 0, 0)) for g in range(nseg)
        ]
    elif kind == "diag":
        bases = [base]
        base_specs = [pl.BlockSpec((tm, 1), lambda i, f, n, s: (i, 0))]
    else:
        bases = [base]
        base_specs = [pl.BlockSpec((tm, width), lambda i, f, n, s: (i, 0))]
    grid_spec = pltpu.PrefetchScalarGridSpec(
        num_scalar_prefetch=3,
        grid=(rows // tm,),
        in_specs=base_specs + [
            pl.BlockSpec((tm, PANEL), lambda i, f, n, s: (i, 0)),
            pl.BlockSpec((width, PANEL), lambda i, f, n, s: (0, 0)),
            pl.BlockSpec((width, PANEL), lambda i, f, n, s: (0, 0)),
        ],
        out_specs=pl.BlockSpec((tm, width), lambda i, f, n, s: (i, 0)),
    )
    flops = 6 * rows * width * PANEL
    cost = pl.CostEstimate(flops=flops, transcendentals=0, bytes_accessed=rows * width * 8 + width * PANEL * 4)
    return pl.pallas_call(
        functools.partial(update_kernel, kind, tm, width, len(bases)),
        grid_spec=grid_spec,
        out_shape=jax.ShapeDtypeStruct((rows, width), jnp.float32),
        cost_estimate=cost,
        compiler_params=pltpu.CompilerParams(vmem_limit_bytes=48 * 1024 * 1024),
    )(flags, info, slots, *bases, a, b_hi, b_lo)


def solve_kernel(x_ref, fhi_ref, flo_ref, out_ref, hi_ref, lo_ref):
    x = x_ref[...]
    x_hi = x.astype(jnp.bfloat16)
    x_lo = (x - x_hi.astype(jnp.float32)).astype(jnp.bfloat16)
    f_hi = fhi_ref[...]
    acc = lax.dot_general(x_hi, f_hi, NT, preferred_element_type=jnp.float32)
    acc = acc + lax.dot_general(x_hi, flo_ref[...], NT, preferred_element_type=jnp.float32)
    acc = acc + lax.dot_general(x_lo, f_hi, NT, preferred_element_type=jnp.float32)
    out_ref[...] = acc
    hi = acc.astype(jnp.bfloat16)
    hi_ref[...] = hi
    lo_ref[...] = (acc - hi.astype(jnp.float32)).astype(jnp.bfloat16)


def apply_inverse(x, f_hi, f_lo):
    rows = x.shape[0]
    tm = 256 if rows % 256 == 0 else MSLOT
    spec = pl.BlockSpec((tm, PANEL), lambda i: (i, 0))
    return pl.pallas_call(
        solve_kernel,
        grid=(rows // tm,),
        in_specs=[
            spec,
            pl.BlockSpec((PANEL, PANEL), lambda i: (0, 0)),
            pl.BlockSpec((PANEL, PANEL), lambda i: (0, 0)),
        ],
        out_specs=[spec, spec, spec],
        out_shape=[
            jax.ShapeDtypeStruct((rows, PANEL), jnp.float32),
            jax.ShapeDtypeStruct((rows, PANEL), jnp.bfloat16),
            jax.ShapeDtypeStruct((rows, PANEL), jnp.bfloat16),
        ],
        cost_estimate=pl.CostEstimate(flops=6 * rows * PANEL * PANEL, transcendentals=0, bytes_accessed=8 * rows * PANEL),
    )(x, f_hi, f_lo)


def dot_t(left, right):
    contract = (((1,), (1,)), ((), ()))
    l_hi, l_lo = split_bf16(left)
    r_hi, r_lo = split_bf16(right)
    out = lax.dot_general(l_hi, r_hi, contract, preferred_element_type=jnp.float32)
    out = out + lax.dot_general(l_hi, r_lo, contract, preferred_element_type=jnp.float32)
    return out + lax.dot_general(l_lo, r_hi, contract, preferred_element_type=jnp.float32)


def pick(index, options):
    out = options[0]
    for i in range(1, len(options)):
        out = jnp.where(index == i, options[i], out)
    return out


def seg0_slots(tseg, cap0):
    has0 = jnp.any(tseg == 0, axis=1)
    rank0 = jnp.cumsum(has0.astype(jnp.int32)) - 1
    slot = jnp.where(has0, rank0, cap0)
    return has0, rank0, slot


def per_device(eigvecs, coupling, mode_counts, tree_segments, eigvals, stiff):
    R = lax.axis_size("row")
    C = lax.axis_size("col")
    r = lax.axis_index("row")
    c = lax.axis_index("col")
    nsub = eigvecs.shape[0]
    H, W = stiff.shape
    Ec = coupling.shape[3]
    G = W // PANEL
    ratio = R // C
    npair = 2 * nsub
    cap = min(MOST * G * ((nsub + SUB_ROW - 1) // SUB_ROW), npair)
    cap0 = min(MOST * ((nsub + SUB_ROW - 1) // SUB_ROW), nsub)

    live = jnp.arange(MSLOT, dtype=jnp.int32)[None, :] < mode_counts[:, None]
    pieces = jnp.einsum("sim,sitp->stmp", eigvecs, coupling, preferred_element_type=jnp.float32)
    pieces = pieces * live.astype(jnp.float32)[:, None, :, None]
    flat = pieces.reshape(npair, MSLOT, Ec)
    flat_pad = jnp.concatenate([flat, jnp.zeros((1, MSLOT, Ec), jnp.float32)], axis=0)

    kpp_src = stiff[:PANEL, :PANEL]
    rs = PANEL // R
    got = [kpp_src[:rs]]
    for i in range(1, R):
        got.append(lax.ppermute(kpp_src[i * rs:(i + 1) * rs], AXES, [(0, i * C)]))
    kpp_part = pick(r, got)
    kpp_col0 = lax.all_gather(kpp_part, "row", axis=0, tiled=True)
    cs = PANEL // C
    got = [kpp_col0[:cs]]
    for k in range(1, C):
        got.append(lax.ppermute(kpp_col0[k * cs:(k + 1) * cs], AXES, [(i * C, i * C + k) for i in range(R)]))
    kpp = lax.all_gather(pick(c, got), "col", axis=0, tiled=True)

    finv = chol_inverse(kpp)

    tseg = tree_segments
    dest = (tseg // G).reshape(npair)
    onehot = dest[:, None] == jnp.arange(C, dtype=jnp.int32)[None, :]
    rank_pd = jnp.cumsum(onehot.astype(jnp.int32), axis=0) - 1
    rank = jnp.sum(jnp.where(onehot, rank_pd, 0), axis=1)
    match = onehot[:, :, None] & (rank_pd[:, :, None] == jnp.arange(cap, dtype=jnp.int32)[None, None, :])
    send_idx = jnp.where(jnp.any(match, axis=0), jnp.argmax(match, axis=0), npair)
    send = flat_pad[send_idx]
    shifted = [send[c]]
    for k in range(1, C):
        out_k = lax.dynamic_index_in_dim(send, (c + k) % C, axis=0, keepdims=False)
        shifted.append(lax.ppermute(out_k, "col", [(i, (i + k) % C) for i in range(C)]))
    shifted = jnp.stack(shifted)
    recv = shifted[(c - jnp.arange(C, dtype=jnp.int32)) % C]
    recv_t = recv.transpose(1, 2, 0, 3).reshape(cap, MSLOT, C * Ec)
    recv_t = jnp.concatenate([recv_t, jnp.zeros((1, MSLOT, PANEL), jnp.float32)], axis=0)
    my_seg = c * G + jnp.arange(G, dtype=jnp.int32)
    seg_hit = tseg[:, :, None] == my_seg[None, None, :]
    rank2 = rank.reshape(nsub, 2)
    slot_tab = jnp.where(
        jnp.any(seg_hit, axis=1), jnp.sum(jnp.where(seg_hit, rank2[:, :, None], 0), axis=1), cap
    )

    has0, rank0, slot_r = seg0_slots(tseg, cap0)
    t0 = jnp.where(tseg[:, 0] == 0, 0, 1)
    sel = has0[:, None] & (rank0[:, None] == jnp.arange(cap0, dtype=jnp.int32)[None, :])
    sel_sub = jnp.argmax(sel, axis=0)
    zidx = jnp.where(jnp.any(sel, axis=0), sel_sub * 2 + t0[sel_sub], npair)
    z_local = flat_pad[zidx]
    z_all = lax.all_gather(z_local, "col", axis=0, tiled=False)
    z_rows = z_all.transpose(1, 2, 0, 3).reshape(cap0 * MSLOT, C * Ec)

    m_src = stiff[:, :PANEL]
    rps = W // R
    zps = cap0 * MSLOT // C
    got = [m_src[:rps]]
    for k in range(1, C):
        got.append(lax.ppermute(m_src[k * rps:(k + 1) * rps], AXES, [(i * C, i * C + k) for i in range(R)]))
    a_slice = pick(c, got)
    m_row = lax.all_gather(a_slice, "col", axis=0, tiled=True)
    slot_row = jnp.zeros((8, PANEL), jnp.float32).at[0, :nsub].set(slot_r.astype(jnp.float32))
    payload = jnp.concatenate([a_slice, lax.dynamic_slice_in_dim(z_rows, c * zps, zps), slot_row], axis=0)
    perm = [(i * C + k, ((i % ratio) * C + k) * C + i // ratio) for i in range(R) for k in range(C)]
    b_slice = lax.ppermute(payload, AXES, perm)
    col_parts = lax.all_gather(b_slice, "row", axis=0, tiled=False)
    m_col = col_parts[:, :rps].reshape(W, PANEL)
    z_col = col_parts[:, rps:rps + zps].reshape(ratio * cap0 * MSLOT, PANEL)

    slot_c = []
    for j in range(ratio):
        got_slot = col_parts[j * C, rps + zps, :nsub].astype(jnp.int32)
        slot_c.append(jnp.where(got_slot < cap0, j * cap0 + got_slot, ratio * cap0))
    slot_c = jnp.concatenate(slot_c)

    f_hi, f_lo = split_bf16(finv)
    low_r, _, _ = apply_inverse(m_row, f_hi, f_lo)
    _, lowc_hi, lowc_lo = apply_inverse(m_col, f_hi, f_lo)
    lowmi_r, _, _ = apply_inverse(z_rows, f_hi, f_lo)
    _, lmc_hi, lmc_lo = apply_inverse(z_col, f_hi, f_lo)

    ones = jnp.ones((H // MSLOT,), jnp.int32)
    none = jnp.zeros((1,), jnp.int32)
    info = jnp.stack([jnp.int32(1), c * W, r * H, jnp.int32(0)]).astype(jnp.int32)
    reduced_ii = panel_update("array", stiff, low_r, lowc_hi, lowc_lo, ones, info, none, H, W)

    lmi = jnp.concatenate(
        [lowmi_r.reshape(cap0, MSLOT, PANEL), jnp.zeros((1, MSLOT, PANEL), jnp.float32)], axis=0
    )
    lmi_full = lmi[slot_r].reshape(nsub * MSLOT, PANEL)
    flags = has0.astype(jnp.int32)
    reduced_mi = panel_update(
        "gather", recv_t, lmi_full, lowc_hi, lowc_lo, flags, info, slot_tab.reshape(-1).astype(jnp.int32), nsub * MSLOT, W
    )

    nc = ratio * cap0
    mode_width = ratio * nsub * MSLOT

    def spread_cols(part):
        part = jnp.concatenate([part.reshape(nc, MSLOT, PANEL), jnp.zeros((1, MSLOT, PANEL), part.dtype)], axis=0)
        return part[slot_c].reshape(mode_width, PANEL)

    diag_values = jnp.where(live, eigvals, 1.0).reshape(-1, 1)
    mode_rows = diag_values.shape[0]
    info_mm = jnp.stack([jnp.int32(0), c * mode_width, r * mode_rows, jnp.int32(0)]).astype(jnp.int32)
    reduced_mm = panel_update("diag", diag_values, lmi_full, spread_cols(lmc_hi), spread_cols(lmc_lo), flags, info_mm, none, mode_rows, mode_width)
    return (reduced_ii, reduced_mi, reduced_mm)


def solution(mesh):
    in_specs = (
        P("row", None, None),
        P("row", None, None, "col"),
        P("row"),
        P("row", None),
        P("row", None),
        P("row", "col"),
    )
    out_specs = (P("row", "col"), P("row", "col"), P("row", "col"))
    return jax.shard_map(
        per_device, mesh=mesh, in_specs=in_specs, out_specs=out_specs, check_vma=False
    )
```

```python
import functools

import jax
import jax.numpy as jnp
from jax import lax
from jax.sharding import PartitionSpec as P
from jax.experimental import pallas as pl
from jax.experimental.pallas import tpu as pltpu

MSLOT = 128
PANEL = 512
MOST = 2
SUB_ROW = 8

AXES = ("row", "col")
LEAF = 128


def mm3(a, b, dn):
    a_hi = a.astype(jnp.bfloat16)
    a_lo = (a - a_hi.astype(jnp.float32)).astype(jnp.bfloat16)
    b_hi = b.astype(jnp.bfloat16)
    b_lo = (b - b_hi.astype(jnp.float32)).astype(jnp.bfloat16)
    out = lax.dot_general(a_hi, b_hi, dn, preferred_element_type=jnp.float32)
    out = out + lax.dot_general(a_hi, b_lo, dn, preferred_element_type=jnp.float32)
    return out + lax.dot_general(a_lo, b_hi, dn, preferred_element_type=jnp.float32)


NN = (((1,), (0,)), ((), ()))
NT = (((1,), (1,)), ((), ()))


def leaf_inverse(d):
    n = d.shape[0]
    sub = lax.broadcasted_iota(jnp.int32, (n, n), 0)
    lane = lax.broadcasted_iota(jnp.int32, (n, n), 1)
    sub_c = lax.broadcasted_iota(jnp.int32, (n, 1), 0)
    lane_r = lax.broadcasted_iota(jnp.int32, (1, n), 1)
    eye = jnp.where(sub == lane, 1.0, 0.0).astype(jnp.float32)

    def step(k, carry):
        dm, em, xm = carry
        colk = jnp.sum(jnp.where(lane == k, dm, 0.0), axis=1, keepdims=True)
        rowk = jnp.sum(jnp.where(sub == k, dm, 0.0), axis=0, keepdims=True)
        dkk = jnp.sum(jnp.where(lane_r == k, rowk, 0.0), axis=1, keepdims=True)
        s = 1.0 / jnp.sqrt(dkk)
        lc = jnp.where(sub_c > k, colk * s, 0.0)
        lr = jnp.where(lane_r > k, rowk * s, 0.0)
        dm = dm - lc * lr
        erow = jnp.sum(jnp.where(sub == k, em, 0.0), axis=0, keepdims=True)
        xk = erow * s
        xm = jnp.where(sub == k, xk, xm)
        em = em - lc * xk
        return dm, em, xm

    _, _, xm = lax.fori_loop(0, n, step, (d, eye, jnp.zeros_like(d)))
    return xm


def chol_inv_kernel(a_ref, x_ref, w_ref, l_ref):
    n = a_ref.shape[0]
    nb = n // LEAF
    w_ref[...] = a_ref[...]
    for kb in range(nb):
        o = kb * LEAF
        blk = pl.ds(o, LEAF)
        xkk = leaf_inverse(w_ref[blk, blk])
        x_ref[blk, blk] = xkk
        if kb + 1 < nb:
            rest = pl.ds(o + LEAF, n - o - LEAF)
            panel = mm3(w_ref[rest, blk], xkk, NT)
            l_ref[rest, blk] = panel
            w_ref[rest, rest] = w_ref[rest, rest] - mm3(panel, panel, NT)
    for i in range(1, nb):
        bi = pl.ds(i * LEAF, LEAF)
        xii = x_ref[bi, bi]
        for j in range(i):
            bj = pl.ds(j * LEAF, LEAF)
            acc = None
            for k in range(j, i):
                bk = pl.ds(k * LEAF, LEAF)
                term = mm3(l_ref[bi, bk], x_ref[bk, bj], NN)
                acc = term if acc is None else acc + term
            x_ref[bi, bj] = -mm3(xii, acc, NN)
        for j in range(i + 1, nb):
            x_ref[bi, pl.ds(j * LEAF, LEAF)] = jnp.zeros((LEAF, LEAF), jnp.float32)
    x_ref[pl.ds(0, LEAF), pl.ds(LEAF, n - LEAF)] = jnp.zeros((LEAF, n - LEAF), jnp.float32)


def chol_inverse(a):
    n = a.shape[0]
    return pl.pallas_call(
        chol_inv_kernel,
        out_shape=jax.ShapeDtypeStruct((n, n), jnp.float32),
        cost_estimate=pl.CostEstimate(flops=800 * n ** 3, transcendentals=n, bytes_accessed=8 * n * n),
        in_specs=[pl.BlockSpec(memory_space=pltpu.VMEM)],
        out_specs=pl.BlockSpec(memory_space=pltpu.VMEM),
        scratch_shapes=[pltpu.VMEM((n, n), jnp.float32), pltpu.VMEM((n, n), jnp.float32)],
    )(a)


def split_bf16(x):
    hi = lax.reduce_precision(x, exponent_bits=8, mantissa_bits=7)
    return hi.astype(jnp.bfloat16), (x - hi).astype(jnp.bfloat16)


def update_kernel(kind, tm, width, nbase, flags_ref, info_ref, slots_ref, *refs):
    base_refs = refs[:nbase]
    a_ref, bhi_ref, blo_ref, out_ref = refs[nbase:]
    i = pl.program_id(0)
    active = flags_ref[i] != 0

    def base_cols(g):
        cols = pl.ds(g * PANEL, PANEL)
        if kind == "gather":
            return base_refs[g][0]
        if kind == "diag":
            rows = info_ref[2] + i * tm + lax.broadcasted_iota(jnp.int32, (tm, PANEL), 0)
            ids = info_ref[1] + g * PANEL + lax.broadcasted_iota(jnp.int32, (tm, PANEL), 1)
            return jnp.where(rows == ids, base_refs[0][...], 0.0)
        return base_refs[0][:, cols]

    @pl.when(active)
    def _():
        a = a_ref[...]
        a_hi = a.astype(jnp.bfloat16)
        a_lo = (a - a_hi.astype(jnp.float32)).astype(jnp.bfloat16)
        dn = (((1,), (1,)), ((), ()))
        for g in range(width // PANEL):
            rows = pl.ds(g * PANEL, PANEL)
            b_hi = bhi_ref[rows, :]
            acc = lax.dot_general(a_hi, b_hi, dn, preferred_element_type=jnp.float32)
            acc = acc + lax.dot_general(a_hi, blo_ref[rows, :], dn, preferred_element_type=jnp.float32)
            acc = acc + lax.dot_general(a_lo, b_hi, dn, preferred_element_type=jnp.float32)
            out_ref[:, pl.ds(g * PANEL, PANEL)] = base_cols(g) - acc

    @pl.when(jnp.logical_not(active))
    def _():
        for g in range(width // PANEL):
            out_ref[:, pl.ds(g * PANEL, PANEL)] = base_cols(g)

    @pl.when((info_ref[0] == 1) & (info_ref[1] == 0))
    def _():
        out_ref[:, pl.ds(0, PANEL)] = a_ref[...]


def panel_update(kind, base, a, b_hi, b_lo, flags, info, slots, rows, width):
    tm = MSLOT
    nseg = width // PANEL
    if kind == "gather":
        bases = [base] * nseg
        base_specs = [
            pl.BlockSpec((1, tm, PANEL), lambda i, f, n, s, g=g: (s[i * nseg + g], 0, 0)) for g in range(nseg)
        ]
    elif kind == "diag":
        bases = [base]
        base_specs = [pl.BlockSpec((tm, 1), lambda i, f, n, s: (i, 0))]
    else:
        bases = [base]
        base_specs = [pl.BlockSpec((tm, width), lambda i, f, n, s: (i, 0))]
    grid_spec = pltpu.PrefetchScalarGridSpec(
        num_scalar_prefetch=3,
        grid=(rows // tm,),
        in_specs=base_specs + [
            pl.BlockSpec((tm, PANEL), lambda i, f, n, s: (i, 0)),
            pl.BlockSpec((width, PANEL), lambda i, f, n, s: (0, 0)),
            pl.BlockSpec((width, PANEL), lambda i, f, n, s: (0, 0)),
        ],
        out_specs=pl.BlockSpec((tm, width), lambda i, f, n, s: (i, 0)),
    )
    flops = 6 * rows * width * PANEL
    cost = pl.CostEstimate(flops=flops, transcendentals=0, bytes_accessed=rows * width * 8 + width * PANEL * 4)
    return pl.pallas_call(
        functools.partial(update_kernel, kind, tm, width, len(bases)),
        grid_spec=grid_spec,
        out_shape=jax.ShapeDtypeStruct((rows, width), jnp.float32),
        cost_estimate=cost,
        compiler_params=pltpu.CompilerParams(vmem_limit_bytes=48 * 1024 * 1024),
    )(flags, info, slots, *bases, a, b_hi, b_lo)


def solve_kernel(x_ref, fhi_ref, flo_ref, out_ref, hi_ref, lo_ref):
    x = x_ref[...]
    x_hi = x.astype(jnp.bfloat16)
    x_lo = (x - x_hi.astype(jnp.float32)).astype(jnp.bfloat16)
    f_hi = fhi_ref[...]
    acc = lax.dot_general(x_hi, f_hi, NT, preferred_element_type=jnp.float32)
    acc = acc + lax.dot_general(x_hi, flo_ref[...], NT, preferred_element_type=jnp.float32)
    acc = acc + lax.dot_general(x_lo, f_hi, NT, preferred_element_type=jnp.float32)
    out_ref[...] = acc
    hi = acc.astype(jnp.bfloat16)
    hi_ref[...] = hi
    lo_ref[...] = (acc - hi.astype(jnp.float32)).astype(jnp.bfloat16)


def apply_inverse(x, f_hi, f_lo):
    rows = x.shape[0]
    tm = 256 if rows % 256 == 0 else MSLOT
    spec = pl.BlockSpec((tm, PANEL), lambda i: (i, 0))
    return pl.pallas_call(
        solve_kernel,
        grid=(rows // tm,),
        in_specs=[
            spec,
            pl.BlockSpec((PANEL, PANEL), lambda i: (0, 0)),
            pl.BlockSpec((PANEL, PANEL), lambda i: (0, 0)),
        ],
        out_specs=[spec, spec, spec],
        out_shape=[
            jax.ShapeDtypeStruct((rows, PANEL), jnp.float32),
            jax.ShapeDtypeStruct((rows, PANEL), jnp.bfloat16),
            jax.ShapeDtypeStruct((rows, PANEL), jnp.bfloat16),
        ],
        cost_estimate=pl.CostEstimate(flops=6 * rows * PANEL * PANEL, transcendentals=0, bytes_accessed=8 * rows * PANEL),
    )(x, f_hi, f_lo)


def dot_t(left, right):
    contract = (((1,), (1,)), ((), ()))
    l_hi, l_lo = split_bf16(left)
    r_hi, r_lo = split_bf16(right)
    out = lax.dot_general(l_hi, r_hi, contract, preferred_element_type=jnp.float32)
    out = out + lax.dot_general(l_hi, r_lo, contract, preferred_element_type=jnp.float32)
    return out + lax.dot_general(l_lo, r_hi, contract, preferred_element_type=jnp.float32)


def pick(index, options):
    out = options[0]
    for i in range(1, len(options)):
        out = jnp.where(index == i, options[i], out)
    return out


def seg0_slots(tseg, cap0):
    has0 = jnp.any(tseg == 0, axis=1)
    rank0 = jnp.cumsum(has0.astype(jnp.int32)) - 1
    slot = jnp.where(has0, rank0, cap0)
    return has0, rank0, slot


def per_device(eigvecs, coupling, mode_counts, tree_segments, eigvals, stiff):
    R = lax.axis_size("row")
    C = lax.axis_size("col")
    r = lax.axis_index("row")
    c = lax.axis_index("col")
    nsub = eigvecs.shape[0]
    H, W = stiff.shape
    Ec = coupling.shape[3]
    G = W // PANEL
    ratio = R // C
    npair = 2 * nsub
    cap = min(MOST * G * ((nsub + SUB_ROW - 1) // SUB_ROW), npair)
    cap0 = min(MOST * ((nsub + SUB_ROW - 1) // SUB_ROW), nsub)

    live = jnp.arange(MSLOT, dtype=jnp.int32)[None, :] < mode_counts[:, None]
    pieces = jnp.einsum("sim,sitp->stmp", eigvecs, coupling, preferred_element_type=jnp.float32)
    pieces = pieces * live.astype(jnp.float32)[:, None, :, None]
    flat = pieces.reshape(npair, MSLOT, Ec)
    flat_pad = jnp.concatenate([flat, jnp.zeros((1, MSLOT, Ec), jnp.float32)], axis=0)

    kpp_src = stiff[:PANEL, :PANEL]
    rs = PANEL // R
    got = [kpp_src[:rs]]
    for i in range(1, R):
        got.append(lax.ppermute(kpp_src[i * rs:(i + 1) * rs], AXES, [(0, i * C)]))
    kpp_part = pick(r, got)
    kpp_col0 = lax.all_gather(kpp_part, "row", axis=0, tiled=True)
    cs = PANEL // C
    got = [kpp_col0[:cs]]
    for k in range(1, C):
        got.append(lax.ppermute(kpp_col0[k * cs:(k + 1) * cs], AXES, [(i * C, i * C + k) for i in range(R)]))
    kpp = lax.all_gather(pick(c, got), "col", axis=0, tiled=True)

    finv = chol_inverse(kpp)

    tseg = tree_segments
    dest = (tseg // G).reshape(npair)
    onehot = dest[:, None] == jnp.arange(C, dtype=jnp.int32)[None, :]
    rank_pd = jnp.cumsum(onehot.astype(jnp.int32), axis=0) - 1
    rank = jnp.sum(jnp.where(onehot, rank_pd, 0), axis=1)
    match = onehot[:, :, None] & (rank_pd[:, :, None] == jnp.arange(cap, dtype=jnp.int32)[None, None, :])
    send_idx = jnp.where(jnp.any(match, axis=0), jnp.argmax(match, axis=0), npair)
    send = flat_pad[send_idx]
    send, _ = lax.optimization_barrier((send, kpp))
    shifted = [send[c]]
    for k in range(1, C):
        out_k = lax.dynamic_index_in_dim(send, (c + k) % C, axis=0, keepdims=False)
        shifted.append(lax.ppermute(out_k, "col", [(i, (i + k) % C) for i in range(C)]))
    shifted = jnp.stack(shifted)
    recv = shifted[(c - jnp.arange(C, dtype=jnp.int32)) % C]
    recv_t = recv.transpose(1, 2, 0, 3).reshape(cap, MSLOT, C * Ec)
    recv_t = jnp.concatenate([recv_t, jnp.zeros((1, MSLOT, PANEL), jnp.float32)], axis=0)
    my_seg = c * G + jnp.arange(G, dtype=jnp.int32)
    seg_hit = tseg[:, :, None] == my_seg[None, None, :]
    rank2 = rank.reshape(nsub, 2)
    slot_tab = jnp.where(
        jnp.any(seg_hit, axis=1), jnp.sum(jnp.where(seg_hit, rank2[:, :, None], 0), axis=1), cap
    )

    has0, rank0, slot_r = seg0_slots(tseg, cap0)
    t0 = jnp.where(tseg[:, 0] == 0, 0, 1)
    sel = has0[:, None] & (rank0[:, None] == jnp.arange(cap0, dtype=jnp.int32)[None, :])
    sel_sub = jnp.argmax(sel, axis=0)
    zidx = jnp.where(jnp.any(sel, axis=0), sel_sub * 2 + t0[sel_sub], npair)
    z_local = flat_pad[zidx]
    z_all = lax.all_gather(z_local, "col", axis=0, tiled=False)
    z_rows = z_all.transpose(1, 2, 0, 3).reshape(cap0 * MSLOT, C * Ec)

    m_src = stiff[:, :PANEL]
    rps = W // R
    zps = cap0 * MSLOT // C
    got = [m_src[:rps]]
    for k in range(1, C):
        got.append(lax.ppermute(m_src[k * rps:(k + 1) * rps], AXES, [(i * C, i * C + k) for i in range(R)]))
    a_slice = pick(c, got)
    m_row = lax.all_gather(a_slice, "col", axis=0, tiled=True)
    slot_row = jnp.zeros((8, PANEL), jnp.float32).at[0, :nsub].set(slot_r.astype(jnp.float32))
    payload = jnp.concatenate([a_slice, lax.dynamic_slice_in_dim(z_rows, c * zps, zps), slot_row], axis=0)
    perm = [(i * C + k, ((i % ratio) * C + k) * C + i // ratio) for i in range(R) for k in range(C)]
    b_slice = lax.ppermute(payload, AXES, perm)
    col_parts = lax.all_gather(b_slice, "row", axis=0, tiled=False)
    m_col = col_parts[:, :rps].reshape(W, PANEL)
    z_col = col_parts[:, rps:rps + zps].reshape(ratio * cap0 * MSLOT, PANEL)

    slot_c = []
    for j in range(ratio):
        got_slot = col_parts[j * C, rps + zps, :nsub].astype(jnp.int32)
        slot_c.append(jnp.where(got_slot < cap0, j * cap0 + got_slot, ratio * cap0))
    slot_c = jnp.concatenate(slot_c)

    f_hi, f_lo = split_bf16(finv)
    low_r, _, _ = apply_inverse(m_row, f_hi, f_lo)
    _, lowc_hi, lowc_lo = apply_inverse(m_col, f_hi, f_lo)
    lowmi_r, _, _ = apply_inverse(z_rows, f_hi, f_lo)
    _, lmc_hi, lmc_lo = apply_inverse(z_col, f_hi, f_lo)

    ones = jnp.ones((H // MSLOT,), jnp.int32)
    none = jnp.zeros((1,), jnp.int32)
    info = jnp.stack([jnp.int32(1), c * W, r * H, jnp.int32(0)]).astype(jnp.int32)
    reduced_ii = panel_update("array", stiff, low_r, lowc_hi, lowc_lo, ones, info, none, H, W)

    lmi = jnp.concatenate(
        [lowmi_r.reshape(cap0, MSLOT, PANEL), jnp.zeros((1, MSLOT, PANEL), jnp.float32)], axis=0
    )
    lmi_full = lmi[slot_r].reshape(nsub * MSLOT, PANEL)
    flags = has0.astype(jnp.int32)
    reduced_mi = panel_update(
        "gather", recv_t, lmi_full, lowc_hi, lowc_lo, flags, info, slot_tab.reshape(-1).astype(jnp.int32), nsub * MSLOT, W
    )

    nc = ratio * cap0
    mode_width = ratio * nsub * MSLOT

    def spread_cols(part):
        part = jnp.concatenate([part.reshape(nc, MSLOT, PANEL), jnp.zeros((1, MSLOT, PANEL), part.dtype)], axis=0)
        return part[slot_c].reshape(mode_width, PANEL)

    diag_values = jnp.where(live, eigvals, 1.0).reshape(-1, 1)
    mode_rows = diag_values.shape[0]
    info_mm = jnp.stack([jnp.int32(0), c * mode_width, r * mode_rows, jnp.int32(0)]).astype(jnp.int32)
    reduced_mm = panel_update("diag", diag_values, lmi_full, spread_cols(lmc_hi), spread_cols(lmc_lo), flags, info_mm, none, mode_rows, mode_width)
    return (reduced_ii, reduced_mi, reduced_mm)


def solution(mesh):
    in_specs = (
        P("row", None, None),
        P("row", None, None, "col"),
        P("row"),
        P("row", None),
        P("row", None),
        P("row", "col"),
    )
    out_specs = (P("row", "col"), P("row", "col"), P("row", "col"))
    return jax.shard_map(
        per_device, mesh=mesh, in_specs=in_specs, out_specs=out_specs, check_vma=False
    )
```

```python
import functools

import jax
import jax.numpy as jnp
from jax import lax
from jax.sharding import PartitionSpec as P
from jax.experimental import pallas as pl
from jax.experimental.pallas import tpu as pltpu

MSLOT = 128
PANEL = 512
MOST = 2
SUB_ROW = 8

AXES = ("row", "col")
LEAF = 128


def mm3(a, b, dn):
    a_hi = a.astype(jnp.bfloat16)
    a_lo = (a - a_hi.astype(jnp.float32)).astype(jnp.bfloat16)
    b_hi = b.astype(jnp.bfloat16)
    b_lo = (b - b_hi.astype(jnp.float32)).astype(jnp.bfloat16)
    out = lax.dot_general(a_hi, b_hi, dn, preferred_element_type=jnp.float32)
    out = out + lax.dot_general(a_hi, b_lo, dn, preferred_element_type=jnp.float32)
    return out + lax.dot_general(a_lo, b_hi, dn, preferred_element_type=jnp.float32)


NN = (((1,), (0,)), ((), ()))
NT = (((1,), (1,)), ((), ()))


def leaf_inverse(d):
    n = d.shape[0]
    sub = lax.broadcasted_iota(jnp.int32, (n, n), 0)
    lane = lax.broadcasted_iota(jnp.int32, (n, n), 1)
    sub_c = lax.broadcasted_iota(jnp.int32, (n, 1), 0)
    lane_r = lax.broadcasted_iota(jnp.int32, (1, n), 1)
    eye = jnp.where(sub == lane, 1.0, 0.0).astype(jnp.float32)

    def step(k, carry):
        dm, em, xm = carry
        colk = jnp.sum(jnp.where(lane == k, dm, 0.0), axis=1, keepdims=True)
        rowk = jnp.sum(jnp.where(sub == k, dm, 0.0), axis=0, keepdims=True)
        dkk = jnp.sum(jnp.where(lane_r == k, rowk, 0.0), axis=1, keepdims=True)
        s = lax.rsqrt(dkk)
        lc = jnp.where(sub_c > k, colk * s, 0.0)
        lr = jnp.where(lane_r > k, rowk * s, 0.0)
        dm = dm - lc * lr
        erow = jnp.sum(jnp.where(sub == k, em, 0.0), axis=0, keepdims=True)
        xk = erow * s
        xm = jnp.where(sub == k, xk, xm)
        em = em - lc * xk
        return dm, em, xm

    _, _, xm = lax.fori_loop(0, n, step, (d, eye, jnp.zeros_like(d)), unroll=4)
    return xm


def chol_inv_kernel(a_ref, x_ref, w_ref, l_ref):
    n = a_ref.shape[0]
    nb = n // LEAF
    w_ref[...] = a_ref[...]
    for kb in range(nb):
        o = kb * LEAF
        blk = pl.ds(o, LEAF)
        xkk = leaf_inverse(w_ref[blk, blk])
        x_ref[blk, blk] = xkk
        if kb + 1 < nb:
            rest = pl.ds(o + LEAF, n - o - LEAF)
            panel = mm3(w_ref[rest, blk], xkk, NT)
            l_ref[rest, blk] = panel
            w_ref[rest, rest] = w_ref[rest, rest] - mm3(panel, panel, NT)
    for i in range(1, nb):
        bi = pl.ds(i * LEAF, LEAF)
        xii = x_ref[bi, bi]
        for j in range(i):
            bj = pl.ds(j * LEAF, LEAF)
            acc = None
            for k in range(j, i):
                bk = pl.ds(k * LEAF, LEAF)
                term = mm3(l_ref[bi, bk], x_ref[bk, bj], NN)
                acc = term if acc is None else acc + term
            x_ref[bi, bj] = -mm3(xii, acc, NN)
        for j in range(i + 1, nb):
            x_ref[bi, pl.ds(j * LEAF, LEAF)] = jnp.zeros((LEAF, LEAF), jnp.float32)
    x_ref[pl.ds(0, LEAF), pl.ds(LEAF, n - LEAF)] = jnp.zeros((LEAF, n - LEAF), jnp.float32)


def chol_inverse(a):
    n = a.shape[0]
    return pl.pallas_call(
        chol_inv_kernel,
        out_shape=jax.ShapeDtypeStruct((n, n), jnp.float32),
        cost_estimate=pl.CostEstimate(flops=800 * n ** 3, transcendentals=n, bytes_accessed=8 * n * n),
        in_specs=[pl.BlockSpec(memory_space=pltpu.VMEM)],
        out_specs=pl.BlockSpec(memory_space=pltpu.VMEM),
        scratch_shapes=[pltpu.VMEM((n, n), jnp.float32), pltpu.VMEM((n, n), jnp.float32)],
    )(a)


def split_bf16(x):
    hi = lax.reduce_precision(x, exponent_bits=8, mantissa_bits=7)
    return hi.astype(jnp.bfloat16), (x - hi).astype(jnp.bfloat16)


def update_kernel(kind, tm, width, nbase, flags_ref, info_ref, slots_ref, *refs):
    base_refs = refs[:nbase]
    a_ref, bhi_ref, blo_ref, out_ref = refs[nbase:]
    i = pl.program_id(0)
    active = flags_ref[i] != 0

    def base_cols(g):
        cols = pl.ds(g * PANEL, PANEL)
        if kind == "gather":
            return base_refs[g][0]
        if kind == "diag":
            rows = info_ref[2] + i * tm + lax.broadcasted_iota(jnp.int32, (tm, PANEL), 0)
            ids = info_ref[1] + g * PANEL + lax.broadcasted_iota(jnp.int32, (tm, PANEL), 1)
            return jnp.where(rows == ids, base_refs[0][...], 0.0)
        return base_refs[0][:, cols]

    @pl.when(active)
    def _():
        a = a_ref[...]
        a_hi = a.astype(jnp.bfloat16)
        a_lo = (a - a_hi.astype(jnp.float32)).astype(jnp.bfloat16)
        dn = (((1,), (1,)), ((), ()))
        for g in range(width // PANEL):
            rows = pl.ds(g * PANEL, PANEL)
            b_hi = bhi_ref[rows, :]
            acc = lax.dot_general(a_hi, b_hi, dn, preferred_element_type=jnp.float32)
            acc = acc + lax.dot_general(a_hi, blo_ref[rows, :], dn, preferred_element_type=jnp.float32)
            acc = acc + lax.dot_general(a_lo, b_hi, dn, preferred_element_type=jnp.float32)
            out_ref[:, pl.ds(g * PANEL, PANEL)] = base_cols(g) - acc

    @pl.when(jnp.logical_not(active))
    def _():
        for g in range(width // PANEL):
            out_ref[:, pl.ds(g * PANEL, PANEL)] = base_cols(g)

    @pl.when((info_ref[0] == 1) & (info_ref[1] == 0))
    def _():
        out_ref[:, pl.ds(0, PANEL)] = a_ref[...]


def panel_update(kind, base, a, b_hi, b_lo, flags, info, slots, rows, width):
    tm = MSLOT
    nseg = width // PANEL
    if kind == "gather":
        bases = [base] * nseg
        base_specs = [
            pl.BlockSpec((1, tm, PANEL), lambda i, f, n, s, g=g: (s[i * nseg + g], 0, 0)) for g in range(nseg)
        ]
    elif kind == "diag":
        bases = [base]
        base_specs = [pl.BlockSpec((tm, 1), lambda i, f, n, s: (i, 0))]
    else:
        bases = [base]
        base_specs = [pl.BlockSpec((tm, width), lambda i, f, n, s: (i, 0))]
    grid_spec = pltpu.PrefetchScalarGridSpec(
        num_scalar_prefetch=3,
        grid=(rows // tm,),
        in_specs=base_specs + [
            pl.BlockSpec((tm, PANEL), lambda i, f, n, s: (i, 0)),
            pl.BlockSpec((width, PANEL), lambda i, f, n, s: (0, 0)),
            pl.BlockSpec((width, PANEL), lambda i, f, n, s: (0, 0)),
        ],
        out_specs=pl.BlockSpec((tm, width), lambda i, f, n, s: (i, 0)),
    )
    flops = 6 * rows * width * PANEL
    cost = pl.CostEstimate(flops=flops, transcendentals=0, bytes_accessed=rows * width * 8 + width * PANEL * 4)
    return pl.pallas_call(
        functools.partial(update_kernel, kind, tm, width, len(bases)),
        grid_spec=grid_spec,
        out_shape=jax.ShapeDtypeStruct((rows, width), jnp.float32),
        cost_estimate=cost,
        compiler_params=pltpu.CompilerParams(vmem_limit_bytes=48 * 1024 * 1024),
    )(flags, info, slots, *bases, a, b_hi, b_lo)


def solve_kernel(x_ref, fhi_ref, flo_ref, out_ref, hi_ref, lo_ref):
    x = x_ref[...]
    x_hi = x.astype(jnp.bfloat16)
    x_lo = (x - x_hi.astype(jnp.float32)).astype(jnp.bfloat16)
    f_hi = fhi_ref[...]
    acc = lax.dot_general(x_hi, f_hi, NT, preferred_element_type=jnp.float32)
    acc = acc + lax.dot_general(x_hi, flo_ref[...], NT, preferred_element_type=jnp.float32)
    acc = acc + lax.dot_general(x_lo, f_hi, NT, preferred_element_type=jnp.float32)
    out_ref[...] = acc
    hi = acc.astype(jnp.bfloat16)
    hi_ref[...] = hi
    lo_ref[...] = (acc - hi.astype(jnp.float32)).astype(jnp.bfloat16)


def apply_inverse(x, f_hi, f_lo):
    rows = x.shape[0]
    tm = 256 if rows % 256 == 0 else MSLOT
    spec = pl.BlockSpec((tm, PANEL), lambda i: (i, 0))
    return pl.pallas_call(
        solve_kernel,
        grid=(rows // tm,),
        in_specs=[
            spec,
            pl.BlockSpec((PANEL, PANEL), lambda i: (0, 0)),
            pl.BlockSpec((PANEL, PANEL), lambda i: (0, 0)),
        ],
        out_specs=[spec, spec, spec],
        out_shape=[
            jax.ShapeDtypeStruct((rows, PANEL), jnp.float32),
            jax.ShapeDtypeStruct((rows, PANEL), jnp.bfloat16),
            jax.ShapeDtypeStruct((rows, PANEL), jnp.bfloat16),
        ],
        cost_estimate=pl.CostEstimate(flops=6 * rows * PANEL * PANEL, transcendentals=0, bytes_accessed=8 * rows * PANEL),
    )(x, f_hi, f_lo)


def dot_t(left, right):
    contract = (((1,), (1,)), ((), ()))
    l_hi, l_lo = split_bf16(left)
    r_hi, r_lo = split_bf16(right)
    out = lax.dot_general(l_hi, r_hi, contract, preferred_element_type=jnp.float32)
    out = out + lax.dot_general(l_hi, r_lo, contract, preferred_element_type=jnp.float32)
    return out + lax.dot_general(l_lo, r_hi, contract, preferred_element_type=jnp.float32)


def pick(index, options):
    out = options[0]
    for i in range(1, len(options)):
        out = jnp.where(index == i, options[i], out)
    return out


def seg0_slots(tseg, cap0):
    has0 = jnp.any(tseg == 0, axis=1)
    rank0 = jnp.cumsum(has0.astype(jnp.int32)) - 1
    slot = jnp.where(has0, rank0, cap0)
    return has0, rank0, slot


def per_device(eigvecs, coupling, mode_counts, tree_segments, eigvals, stiff):
    R = lax.axis_size("row")
    C = lax.axis_size("col")
    r = lax.axis_index("row")
    c = lax.axis_index("col")
    nsub = eigvecs.shape[0]
    H, W = stiff.shape
    Ec = coupling.shape[3]
    G = W // PANEL
    ratio = R // C
    npair = 2 * nsub
    cap = min(MOST * G * ((nsub + SUB_ROW - 1) // SUB_ROW), npair)
    cap0 = min(MOST * ((nsub + SUB_ROW - 1) // SUB_ROW), nsub)

    live = jnp.arange(MSLOT, dtype=jnp.int32)[None, :] < mode_counts[:, None]
    pieces = jnp.einsum("sim,sitp->stmp", eigvecs, coupling, preferred_element_type=jnp.float32)
    pieces = pieces * live.astype(jnp.float32)[:, None, :, None]
    flat = pieces.reshape(npair, MSLOT, Ec)
    flat_pad = jnp.concatenate([flat, jnp.zeros((1, MSLOT, Ec), jnp.float32)], axis=0)

    kpp_src = stiff[:PANEL, :PANEL]
    rs = PANEL // R
    got = [kpp_src[:rs]]
    for i in range(1, R):
        got.append(lax.ppermute(kpp_src[i * rs:(i + 1) * rs], AXES, [(0, i * C)]))
    kpp_part = pick(r, got)
    kpp_col0 = lax.all_gather(kpp_part, "row", axis=0, tiled=True)
    cs = PANEL // C
    got = [kpp_col0[:cs]]
    for k in range(1, C):
        got.append(lax.ppermute(kpp_col0[k * cs:(k + 1) * cs], AXES, [(i * C, i * C + k) for i in range(R)]))
    kpp = lax.all_gather(pick(c, got), "col", axis=0, tiled=True)

    finv = chol_inverse(kpp)

    tseg = tree_segments
    dest = (tseg // G).reshape(npair)
    onehot = dest[:, None] == jnp.arange(C, dtype=jnp.int32)[None, :]
    rank_pd = jnp.cumsum(onehot.astype(jnp.int32), axis=0) - 1
    rank = jnp.sum(jnp.where(onehot, rank_pd, 0), axis=1)
    match = onehot[:, :, None] & (rank_pd[:, :, None] == jnp.arange(cap, dtype=jnp.int32)[None, None, :])
    send_idx = jnp.where(jnp.any(match, axis=0), jnp.argmax(match, axis=0), npair)
    send = flat_pad[send_idx]
    send, _ = lax.optimization_barrier((send, kpp))
    shifted = [send[c]]
    for k in range(1, C):
        out_k = lax.dynamic_index_in_dim(send, (c + k) % C, axis=0, keepdims=False)
        shifted.append(lax.ppermute(out_k, "col", [(i, (i + k) % C) for i in range(C)]))
    shifted = jnp.stack(shifted)
    recv = shifted[(c - jnp.arange(C, dtype=jnp.int32)) % C]
    recv_t = recv.transpose(1, 2, 0, 3).reshape(cap, MSLOT, C * Ec)
    recv_t = jnp.concatenate([recv_t, jnp.zeros((1, MSLOT, PANEL), jnp.float32)], axis=0)
    my_seg = c * G + jnp.arange(G, dtype=jnp.int32)
    seg_hit = tseg[:, :, None] == my_seg[None, None, :]
    rank2 = rank.reshape(nsub, 2)
    slot_tab = jnp.where(
        jnp.any(seg_hit, axis=1), jnp.sum(jnp.where(seg_hit, rank2[:, :, None], 0), axis=1), cap
    )

    has0, rank0, slot_r = seg0_slots(tseg, cap0)
    t0 = jnp.where(tseg[:, 0] == 0, 0, 1)
    sel = has0[:, None] & (rank0[:, None] == jnp.arange(cap0, dtype=jnp.int32)[None, :])
    sel_sub = jnp.argmax(sel, axis=0)
    zidx = jnp.where(jnp.any(sel, axis=0), sel_sub * 2 + t0[sel_sub], npair)
    z_local = flat_pad[zidx]
    z_all = lax.all_gather(z_local, "col", axis=0, tiled=False)
    z_rows = z_all.transpose(1, 2, 0, 3).reshape(cap0 * MSLOT, C * Ec)

    m_src = stiff[:, :PANEL]
    rps = W // R
    zps = cap0 * MSLOT // C
    got = [m_src[:rps]]
    for k in range(1, C):
        got.append(lax.ppermute(m_src[k * rps:(k + 1) * rps], AXES, [(i * C, i * C + k) for i in range(R)]))
    a_slice = pick(c, got)
    m_row = lax.all_gather(a_slice, "col", axis=0, tiled=True)
    slot_row = jnp.zeros((8, PANEL), jnp.float32).at[0, :nsub].set(slot_r.astype(jnp.float32))
    payload = jnp.concatenate([a_slice, lax.dynamic_slice_in_dim(z_rows, c * zps, zps), slot_row], axis=0)
    perm = [(i * C + k, ((i % ratio) * C + k) * C + i // ratio) for i in range(R) for k in range(C)]
    b_slice = lax.ppermute(payload, AXES, perm)
    col_parts = lax.all_gather(b_slice, "row", axis=0, tiled=False)
    m_col = col_parts[:, :rps].reshape(W, PANEL)
    z_col = col_parts[:, rps:rps + zps].reshape(ratio * cap0 * MSLOT, PANEL)

    slot_c = []
    for j in range(ratio):
        got_slot = col_parts[j * C, rps + zps, :nsub].astype(jnp.int32)
        slot_c.append(jnp.where(got_slot < cap0, j * cap0 + got_slot, ratio * cap0))
    slot_c = jnp.concatenate(slot_c)

    f_hi, f_lo = split_bf16(finv)
    low_r, _, _ = apply_inverse(m_row, f_hi, f_lo)
    _, lowc_hi, lowc_lo = apply_inverse(m_col, f_hi, f_lo)
    lowmi_r, _, _ = apply_inverse(z_rows, f_hi, f_lo)
    _, lmc_hi, lmc_lo = apply_inverse(z_col, f_hi, f_lo)

    ones = jnp.ones((H // MSLOT,), jnp.int32)
    none = jnp.zeros((1,), jnp.int32)
    info = jnp.stack([jnp.int32(1), c * W, r * H, jnp.int32(0)]).astype(jnp.int32)
    reduced_ii = panel_update("array", stiff, low_r, lowc_hi, lowc_lo, ones, info, none, H, W)

    lmi = jnp.concatenate(
        [lowmi_r.reshape(cap0, MSLOT, PANEL), jnp.zeros((1, MSLOT, PANEL), jnp.float32)], axis=0
    )
    lmi_full = lmi[slot_r].reshape(nsub * MSLOT, PANEL)
    flags = has0.astype(jnp.int32)
    reduced_mi = panel_update(
        "gather", recv_t, lmi_full, lowc_hi, lowc_lo, flags, info, slot_tab.reshape(-1).astype(jnp.int32), nsub * MSLOT, W
    )

    nc = ratio * cap0
    mode_width = ratio * nsub * MSLOT

    def spread_cols(part):
        part = jnp.concatenate([part.reshape(nc, MSLOT, PANEL), jnp.zeros((1, MSLOT, PANEL), part.dtype)], axis=0)
        return part[slot_c].reshape(mode_width, PANEL)

    diag_values = jnp.where(live, eigvals, 1.0).reshape(-1, 1)
    mode_rows = diag_values.shape[0]
    info_mm = jnp.stack([jnp.int32(0), c * mode_width, r * mode_rows, jnp.int32(0)]).astype(jnp.int32)
    reduced_mm = panel_update("diag", diag_values, lmi_full, spread_cols(lmc_hi), spread_cols(lmc_lo), flags, info_mm, none, mode_rows, mode_width)
    return (reduced_ii, reduced_mi, reduced_mm)


def solution(mesh):
    in_specs = (
        P("row", None, None),
        P("row", None, None, "col"),
        P("row"),
        P("row", None),
        P("row", None),
        P("row", "col"),
    )
    out_specs = (P("row", "col"), P("row", "col"), P("row", "col"))
    return jax.shard_map(
        per_device, mesh=mesh, in_specs=in_specs, out_specs=out_specs, check_vma=False
    )
```

```python
import functools

import jax
import jax.numpy as jnp
from jax import lax
from jax.sharding import PartitionSpec as P
from jax.experimental import pallas as pl
from jax.experimental.pallas import tpu as pltpu

MSLOT = 128
PANEL = 512
MOST = 2
SUB_ROW = 8

AXES = ("row", "col")
LEAF = 128


def mm3(a, b, dn):
    a_hi = a.astype(jnp.bfloat16)
    a_lo = (a - a_hi.astype(jnp.float32)).astype(jnp.bfloat16)
    b_hi = b.astype(jnp.bfloat16)
    b_lo = (b - b_hi.astype(jnp.float32)).astype(jnp.bfloat16)
    out = lax.dot_general(a_hi, b_hi, dn, preferred_element_type=jnp.float32)
    out = out + lax.dot_general(a_hi, b_lo, dn, preferred_element_type=jnp.float32)
    return out + lax.dot_general(a_lo, b_hi, dn, preferred_element_type=jnp.float32)


NN = (((1,), (0,)), ((), ()))
NT = (((1,), (1,)), ((), ()))


def leaf_inverse(d, d_ref, e_ref, x_ref):
    n = d.shape[0]
    sub = lax.broadcasted_iota(jnp.int32, (n, n), 0)
    lane = lax.broadcasted_iota(jnp.int32, (n, n), 1)
    sub_c = lax.broadcasted_iota(jnp.int32, (n, 1), 0)
    lane_r = lax.broadcasted_iota(jnp.int32, (1, n), 1)
    d_ref[...] = d
    e_ref[...] = jnp.where(sub == lane, 1.0, 0.0).astype(jnp.float32)
    x_ref[...] = jnp.zeros((n, n), jnp.float32)

    def step(k, carry):
        dm = d_ref[...]
        colk = jnp.sum(jnp.where(lane == k, dm, 0.0), axis=1, keepdims=True)
        rowk = d_ref[pl.ds(k, 1), :]
        dkk = jnp.sum(jnp.where(lane_r == k, rowk, 0.0), axis=1, keepdims=True)
        s = lax.rsqrt(dkk)
        lc = jnp.where(sub_c > k, colk * s, 0.0)
        lr = jnp.where(lane_r > k, rowk * s, 0.0)
        d_ref[...] = dm - lc * lr
        xk = e_ref[pl.ds(k, 1), :] * s
        x_ref[pl.ds(k, 1), :] = xk
        e_ref[...] = e_ref[...] - lc * xk
        return carry

    lax.fori_loop(0, n, step, 0, unroll=4)
    return x_ref[...]


def chol_inv_kernel(a_ref, x_ref, w_ref, l_ref, d_ref, e_ref, xl_ref):
    n = a_ref.shape[0]
    nb = n // LEAF
    w_ref[...] = a_ref[...]
    for kb in range(nb):
        o = kb * LEAF
        blk = pl.ds(o, LEAF)
        xkk = leaf_inverse(w_ref[blk, blk], d_ref, e_ref, xl_ref)
        x_ref[blk, blk] = xkk
        if kb + 1 < nb:
            rest = pl.ds(o + LEAF, n - o - LEAF)
            panel = mm3(w_ref[rest, blk], xkk, NT)
            l_ref[rest, blk] = panel
            w_ref[rest, rest] = w_ref[rest, rest] - mm3(panel, panel, NT)
    for i in range(1, nb):
        bi = pl.ds(i * LEAF, LEAF)
        xii = x_ref[bi, bi]
        for j in range(i):
            bj = pl.ds(j * LEAF, LEAF)
            acc = None
            for k in range(j, i):
                bk = pl.ds(k * LEAF, LEAF)
                term = mm3(l_ref[bi, bk], x_ref[bk, bj], NN)
                acc = term if acc is None else acc + term
            x_ref[bi, bj] = -mm3(xii, acc, NN)
        for j in range(i + 1, nb):
            x_ref[bi, pl.ds(j * LEAF, LEAF)] = jnp.zeros((LEAF, LEAF), jnp.float32)
    x_ref[pl.ds(0, LEAF), pl.ds(LEAF, n - LEAF)] = jnp.zeros((LEAF, n - LEAF), jnp.float32)


def chol_inverse(a):
    n = a.shape[0]
    return pl.pallas_call(
        chol_inv_kernel,
        out_shape=jax.ShapeDtypeStruct((n, n), jnp.float32),
        cost_estimate=pl.CostEstimate(flops=800 * n ** 3, transcendentals=n, bytes_accessed=8 * n * n),
        in_specs=[pl.BlockSpec(memory_space=pltpu.VMEM)],
        out_specs=pl.BlockSpec(memory_space=pltpu.VMEM),
        scratch_shapes=[pltpu.VMEM((n, n), jnp.float32), pltpu.VMEM((n, n), jnp.float32)]
        + [pltpu.VMEM((LEAF, LEAF), jnp.float32)] * 3,
    )(a)


def split_bf16(x):
    hi = lax.reduce_precision(x, exponent_bits=8, mantissa_bits=7)
    return hi.astype(jnp.bfloat16), (x - hi).astype(jnp.bfloat16)


def update_kernel(kind, tm, width, nbase, flags_ref, info_ref, slots_ref, *refs):
    base_refs = refs[:nbase]
    a_ref, bhi_ref, blo_ref, out_ref = refs[nbase:]
    i = pl.program_id(0)
    active = flags_ref[i] != 0

    def base_cols(g):
        cols = pl.ds(g * PANEL, PANEL)
        if kind == "gather":
            return base_refs[g][0]
        if kind == "diag":
            rows = info_ref[2] + i * tm + lax.broadcasted_iota(jnp.int32, (tm, PANEL), 0)
            ids = info_ref[1] + g * PANEL + lax.broadcasted_iota(jnp.int32, (tm, PANEL), 1)
            return jnp.where(rows == ids, base_refs[0][...], 0.0)
        return base_refs[0][:, cols]

    @pl.when(active)
    def _():
        a = a_ref[...]
        a_hi = a.astype(jnp.bfloat16)
        a_lo = (a - a_hi.astype(jnp.float32)).astype(jnp.bfloat16)
        dn = (((1,), (1,)), ((), ()))
        for g in range(width // PANEL):
            rows = pl.ds(g * PANEL, PANEL)
            b_hi = bhi_ref[rows, :]
            acc = lax.dot_general(a_hi, b_hi, dn, preferred_element_type=jnp.float32)
            acc = acc + lax.dot_general(a_hi, blo_ref[rows, :], dn, preferred_element_type=jnp.float32)
            acc = acc + lax.dot_general(a_lo, b_hi, dn, preferred_element_type=jnp.float32)
            out_ref[:, pl.ds(g * PANEL, PANEL)] = base_cols(g) - acc

    @pl.when(jnp.logical_not(active))
    def _():
        for g in range(width // PANEL):
            out_ref[:, pl.ds(g * PANEL, PANEL)] = base_cols(g)

    @pl.when((info_ref[0] == 1) & (info_ref[1] == 0))
    def _():
        out_ref[:, pl.ds(0, PANEL)] = a_ref[...]


def panel_update(kind, base, a, b_hi, b_lo, flags, info, slots, rows, width):
    tm = MSLOT
    nseg = width // PANEL
    if kind == "gather":
        bases = [base] * nseg
        base_specs = [
            pl.BlockSpec((1, tm, PANEL), lambda i, f, n, s, g=g: (s[i * nseg + g], 0, 0)) for g in range(nseg)
        ]
    elif kind == "diag":
        bases = [base]
        base_specs = [pl.BlockSpec((tm, 1), lambda i, f, n, s: (i, 0))]
    else:
        bases = [base]
        base_specs = [pl.BlockSpec((tm, width), lambda i, f, n, s: (i, 0))]
    grid_spec = pltpu.PrefetchScalarGridSpec(
        num_scalar_prefetch=3,
        grid=(rows // tm,),
        in_specs=base_specs + [
            pl.BlockSpec((tm, PANEL), lambda i, f, n, s: (i, 0)),
            pl.BlockSpec((width, PANEL), lambda i, f, n, s: (0, 0)),
            pl.BlockSpec((width, PANEL), lambda i, f, n, s: (0, 0)),
        ],
        out_specs=pl.BlockSpec((tm, width), lambda i, f, n, s: (i, 0)),
    )
    flops = 6 * rows * width * PANEL
    cost = pl.CostEstimate(flops=flops, transcendentals=0, bytes_accessed=rows * width * 8 + width * PANEL * 4)
    return pl.pallas_call(
        functools.partial(update_kernel, kind, tm, width, len(bases)),
        grid_spec=grid_spec,
        out_shape=jax.ShapeDtypeStruct((rows, width), jnp.float32),
        cost_estimate=cost,
        compiler_params=pltpu.CompilerParams(vmem_limit_bytes=48 * 1024 * 1024),
    )(flags, info, slots, *bases, a, b_hi, b_lo)


def solve_kernel(x_ref, fhi_ref, flo_ref, out_ref, hi_ref, lo_ref):
    x = x_ref[...]
    x_hi = x.astype(jnp.bfloat16)
    x_lo = (x - x_hi.astype(jnp.float32)).astype(jnp.bfloat16)
    f_hi = fhi_ref[...]
    acc = lax.dot_general(x_hi, f_hi, NT, preferred_element_type=jnp.float32)
    acc = acc + lax.dot_general(x_hi, flo_ref[...], NT, preferred_element_type=jnp.float32)
    acc = acc + lax.dot_general(x_lo, f_hi, NT, preferred_element_type=jnp.float32)
    out_ref[...] = acc
    hi = acc.astype(jnp.bfloat16)
    hi_ref[...] = hi
    lo_ref[...] = (acc - hi.astype(jnp.float32)).astype(jnp.bfloat16)


def apply_inverse(x, f_hi, f_lo):
    rows = x.shape[0]
    tm = 256 if rows % 256 == 0 else MSLOT
    spec = pl.BlockSpec((tm, PANEL), lambda i: (i, 0))
    return pl.pallas_call(
        solve_kernel,
        grid=(rows // tm,),
        in_specs=[
            spec,
            pl.BlockSpec((PANEL, PANEL), lambda i: (0, 0)),
            pl.BlockSpec((PANEL, PANEL), lambda i: (0, 0)),
        ],
        out_specs=[spec, spec, spec],
        out_shape=[
            jax.ShapeDtypeStruct((rows, PANEL), jnp.float32),
            jax.ShapeDtypeStruct((rows, PANEL), jnp.bfloat16),
            jax.ShapeDtypeStruct((rows, PANEL), jnp.bfloat16),
        ],
        cost_estimate=pl.CostEstimate(flops=6 * rows * PANEL * PANEL, transcendentals=0, bytes_accessed=8 * rows * PANEL),
    )(x, f_hi, f_lo)


def dot_t(left, right):
    contract = (((1,), (1,)), ((), ()))
    l_hi, l_lo = split_bf16(left)
    r_hi, r_lo = split_bf16(right)
    out = lax.dot_general(l_hi, r_hi, contract, preferred_element_type=jnp.float32)
    out = out + lax.dot_general(l_hi, r_lo, contract, preferred_element_type=jnp.float32)
    return out + lax.dot_general(l_lo, r_hi, contract, preferred_element_type=jnp.float32)


def pick(index, options):
    out = options[0]
    for i in range(1, len(options)):
        out = jnp.where(index == i, options[i], out)
    return out


def seg0_slots(tseg, cap0):
    has0 = jnp.any(tseg == 0, axis=1)
    rank0 = jnp.cumsum(has0.astype(jnp.int32)) - 1
    slot = jnp.where(has0, rank0, cap0)
    return has0, rank0, slot


def per_device(eigvecs, coupling, mode_counts, tree_segments, eigvals, stiff):
    R = lax.axis_size("row")
    C = lax.axis_size("col")
    r = lax.axis_index("row")
    c = lax.axis_index("col")
    nsub = eigvecs.shape[0]
    H, W = stiff.shape
    Ec = coupling.shape[3]
    G = W // PANEL
    ratio = R // C
    npair = 2 * nsub
    cap = min(MOST * G * ((nsub + SUB_ROW - 1) // SUB_ROW), npair)
    cap0 = min(MOST * ((nsub + SUB_ROW - 1) // SUB_ROW), nsub)

    live = jnp.arange(MSLOT, dtype=jnp.int32)[None, :] < mode_counts[:, None]
    pieces = jnp.einsum("sim,sitp->stmp", eigvecs, coupling, preferred_element_type=jnp.float32)
    pieces = pieces * live.astype(jnp.float32)[:, None, :, None]
    flat = pieces.reshape(npair, MSLOT, Ec)
    flat_pad = jnp.concatenate([flat, jnp.zeros((1, MSLOT, Ec), jnp.float32)], axis=0)

    kpp_src = stiff[:PANEL, :PANEL]
    rs = PANEL // R
    got = [kpp_src[:rs]]
    for i in range(1, R):
        got.append(lax.ppermute(kpp_src[i * rs:(i + 1) * rs], AXES, [(0, i * C)]))
    kpp_part = pick(r, got)
    kpp_col0 = lax.all_gather(kpp_part, "row", axis=0, tiled=True)
    cs = PANEL // C
    got = [kpp_col0[:cs]]
    for k in range(1, C):
        got.append(lax.ppermute(kpp_col0[k * cs:(k + 1) * cs], AXES, [(i * C, i * C + k) for i in range(R)]))
    kpp = lax.all_gather(pick(c, got), "col", axis=0, tiled=True)

    finv = chol_inverse(kpp)

    tseg = tree_segments
    dest = (tseg // G).reshape(npair)
    onehot = dest[:, None] == jnp.arange(C, dtype=jnp.int32)[None, :]
    rank_pd = jnp.cumsum(onehot.astype(jnp.int32), axis=0) - 1
    rank = jnp.sum(jnp.where(onehot, rank_pd, 0), axis=1)
    match = onehot[:, :, None] & (rank_pd[:, :, None] == jnp.arange(cap, dtype=jnp.int32)[None, None, :])
    send_idx = jnp.where(jnp.any(match, axis=0), jnp.argmax(match, axis=0), npair)
    send = flat_pad[send_idx]
    send, _ = lax.optimization_barrier((send, kpp))
    shifted = [send[c]]
    for k in range(1, C):
        out_k = lax.dynamic_index_in_dim(send, (c + k) % C, axis=0, keepdims=False)
        shifted.append(lax.ppermute(out_k, "col", [(i, (i + k) % C) for i in range(C)]))
    shifted = jnp.stack(shifted)
    recv = shifted[(c - jnp.arange(C, dtype=jnp.int32)) % C]
    recv_t = recv.transpose(1, 2, 0, 3).reshape(cap, MSLOT, C * Ec)
    recv_t = jnp.concatenate([recv_t, jnp.zeros((1, MSLOT, PANEL), jnp.float32)], axis=0)
    my_seg = c * G + jnp.arange(G, dtype=jnp.int32)
    seg_hit = tseg[:, :, None] == my_seg[None, None, :]
    rank2 = rank.reshape(nsub, 2)
    slot_tab = jnp.where(
        jnp.any(seg_hit, axis=1), jnp.sum(jnp.where(seg_hit, rank2[:, :, None], 0), axis=1), cap
    )

    has0, rank0, slot_r = seg0_slots(tseg, cap0)
    t0 = jnp.where(tseg[:, 0] == 0, 0, 1)
    sel = has0[:, None] & (rank0[:, None] == jnp.arange(cap0, dtype=jnp.int32)[None, :])
    sel_sub = jnp.argmax(sel, axis=0)
    zidx = jnp.where(jnp.any(sel, axis=0), sel_sub * 2 + t0[sel_sub], npair)
    z_local = flat_pad[zidx]
    z_all = lax.all_gather(z_local, "col", axis=0, tiled=False)
    z_rows = z_all.transpose(1, 2, 0, 3).reshape(cap0 * MSLOT, C * Ec)

    m_src = stiff[:, :PANEL]
    rps = W // R
    zps = cap0 * MSLOT // C
    got = [m_src[:rps]]
    for k in range(1, C):
        got.append(lax.ppermute(m_src[k * rps:(k + 1) * rps], AXES, [(i * C, i * C + k) for i in range(R)]))
    a_slice = pick(c, got)
    m_row = lax.all_gather(a_slice, "col", axis=0, tiled=True)
    slot_row = jnp.zeros((8, PANEL), jnp.float32).at[0, :nsub].set(slot_r.astype(jnp.float32))
    payload = jnp.concatenate([a_slice, lax.dynamic_slice_in_dim(z_rows, c * zps, zps), slot_row], axis=0)
    perm = [(i * C + k, ((i % ratio) * C + k) * C + i // ratio) for i in range(R) for k in range(C)]
    b_slice = lax.ppermute(payload, AXES, perm)
    col_parts = lax.all_gather(b_slice, "row", axis=0, tiled=False)
    m_col = col_parts[:, :rps].reshape(W, PANEL)
    z_col = col_parts[:, rps:rps + zps].reshape(ratio * cap0 * MSLOT, PANEL)

    slot_c = []
    for j in range(ratio):
        got_slot = col_parts[j * C, rps + zps, :nsub].astype(jnp.int32)
        slot_c.append(jnp.where(got_slot < cap0, j * cap0 + got_slot, ratio * cap0))
    slot_c = jnp.concatenate(slot_c)

    f_hi, f_lo = split_bf16(finv)
    low_r, _, _ = apply_inverse(m_row, f_hi, f_lo)
    _, lowc_hi, lowc_lo = apply_inverse(m_col, f_hi, f_lo)
    lowmi_r, _, _ = apply_inverse(z_rows, f_hi, f_lo)
    _, lmc_hi, lmc_lo = apply_inverse(z_col, f_hi, f_lo)

    ones = jnp.ones((H // MSLOT,), jnp.int32)
    none = jnp.zeros((1,), jnp.int32)
    info = jnp.stack([jnp.int32(1), c * W, r * H, jnp.int32(0)]).astype(jnp.int32)
    reduced_ii = panel_update("array", stiff, low_r, lowc_hi, lowc_lo, ones, info, none, H, W)

    lmi = jnp.concatenate(
        [lowmi_r.reshape(cap0, MSLOT, PANEL), jnp.zeros((1, MSLOT, PANEL), jnp.float32)], axis=0
    )
    lmi_full = lmi[slot_r].reshape(nsub * MSLOT, PANEL)
    flags = has0.astype(jnp.int32)
    reduced_mi = panel_update(
        "gather", recv_t, lmi_full, lowc_hi, lowc_lo, flags, info, slot_tab.reshape(-1).astype(jnp.int32), nsub * MSLOT, W
    )

    nc = ratio * cap0
    mode_width = ratio * nsub * MSLOT

    def spread_cols(part):
        part = jnp.concatenate([part.reshape(nc, MSLOT, PANEL), jnp.zeros((1, MSLOT, PANEL), part.dtype)], axis=0)
        return part[slot_c].reshape(mode_width, PANEL)

    diag_values = jnp.where(live, eigvals, 1.0).reshape(-1, 1)
    mode_rows = diag_values.shape[0]
    info_mm = jnp.stack([jnp.int32(0), c * mode_width, r * mode_rows, jnp.int32(0)]).astype(jnp.int32)
    reduced_mm = panel_update("diag", diag_values, lmi_full, spread_cols(lmc_hi), spread_cols(lmc_lo), flags, info_mm, none, mode_rows, mode_width)
    return (reduced_ii, reduced_mi, reduced_mm)


def solution(mesh):
    in_specs = (
        P("row", None, None),
        P("row", None, None, "col"),
        P("row"),
        P("row", None),
        P("row", None),
        P("row", "col"),
    )
    out_specs = (P("row", "col"), P("row", "col"), P("row", "col"))
    return jax.shard_map(
        per_device, mesh=mesh, in_specs=in_specs, out_specs=out_specs, check_vma=False
    )
```

```python
import functools

import jax
import jax.numpy as jnp
from jax import lax
from jax.sharding import PartitionSpec as P
from jax.experimental import pallas as pl
from jax.experimental.pallas import tpu as pltpu

MSLOT = 128
PANEL = 512
MOST = 2
SUB_ROW = 8

AXES = ("row", "col")
LEAF = 128


def mm3(a, b, dn):
    a_hi = a.astype(jnp.bfloat16)
    a_lo = (a - a_hi.astype(jnp.float32)).astype(jnp.bfloat16)
    b_hi = b.astype(jnp.bfloat16)
    b_lo = (b - b_hi.astype(jnp.float32)).astype(jnp.bfloat16)
    out = lax.dot_general(a_hi, b_hi, dn, preferred_element_type=jnp.float32)
    out = out + lax.dot_general(a_hi, b_lo, dn, preferred_element_type=jnp.float32)
    return out + lax.dot_general(a_lo, b_hi, dn, preferred_element_type=jnp.float32)


NN = (((1,), (0,)), ((), ()))
NT = (((1,), (1,)), ((), ()))


def leaf_inverse(d, d_ref, e_ref, x_ref):
    n = d.shape[0]
    sub = lax.broadcasted_iota(jnp.int32, (n, n), 0)
    lane = lax.broadcasted_iota(jnp.int32, (n, n), 1)
    sub_c = lax.broadcasted_iota(jnp.int32, (n, 1), 0)
    lane_r = lax.broadcasted_iota(jnp.int32, (1, n), 1)
    d_ref[...] = d
    e_ref[...] = jnp.where(sub == lane, 1.0, 0.0).astype(jnp.float32)
    x_ref[...] = jnp.zeros((n, n), jnp.float32)

    def step(k, carry):
        dm = d_ref[...]
        colk = jnp.sum(jnp.where(lane == k, dm, 0.0), axis=1, keepdims=True)
        rowk = d_ref[pl.ds(k, 1), :]
        dkk = jnp.sum(jnp.where(lane_r == k, rowk, 0.0), axis=1, keepdims=True)
        s = lax.rsqrt(dkk)
        lc = jnp.where(sub_c > k, colk * s, 0.0)
        lr = jnp.where(lane_r > k, rowk * s, 0.0)
        d_ref[...] = dm - lc * lr
        xk = e_ref[pl.ds(k, 1), :] * s
        x_ref[pl.ds(k, 1), :] = xk
        e_ref[...] = e_ref[...] - lc * xk
        return carry

    lax.fori_loop(0, n, step, 0, unroll=8)
    return x_ref[...]


def chol_inv_kernel(a_ref, x_ref, w_ref, l_ref, d_ref, e_ref, xl_ref):
    n = a_ref.shape[0]
    nb = n // LEAF
    w_ref[...] = a_ref[...]
    for kb in range(nb):
        o = kb * LEAF
        blk = pl.ds(o, LEAF)
        xkk = leaf_inverse(w_ref[blk, blk], d_ref, e_ref, xl_ref)
        x_ref[blk, blk] = xkk
        if kb + 1 < nb:
            rest = pl.ds(o + LEAF, n - o - LEAF)
            panel = mm3(w_ref[rest, blk], xkk, NT)
            l_ref[rest, blk] = panel
            w_ref[rest, rest] = w_ref[rest, rest] - mm3(panel, panel, NT)
    for i in range(1, nb):
        bi = pl.ds(i * LEAF, LEAF)
        xii = x_ref[bi, bi]
        for j in range(i):
            bj = pl.ds(j * LEAF, LEAF)
            acc = None
            for k in range(j, i):
                bk = pl.ds(k * LEAF, LEAF)
                term = mm3(l_ref[bi, bk], x_ref[bk, bj], NN)
                acc = term if acc is None else acc + term
            x_ref[bi, bj] = -mm3(xii, acc, NN)
        for j in range(i + 1, nb):
            x_ref[bi, pl.ds(j * LEAF, LEAF)] = jnp.zeros((LEAF, LEAF), jnp.float32)
    x_ref[pl.ds(0, LEAF), pl.ds(LEAF, n - LEAF)] = jnp.zeros((LEAF, n - LEAF), jnp.float32)


def chol_inverse(a):
    n = a.shape[0]
    return pl.pallas_call(
        chol_inv_kernel,
        out_shape=jax.ShapeDtypeStruct((n, n), jnp.float32),
        cost_estimate=pl.CostEstimate(flops=800 * n ** 3, transcendentals=n, bytes_accessed=8 * n * n),
        in_specs=[pl.BlockSpec(memory_space=pltpu.VMEM)],
        out_specs=pl.BlockSpec(memory_space=pltpu.VMEM),
        scratch_shapes=[pltpu.VMEM((n, n), jnp.float32), pltpu.VMEM((n, n), jnp.float32)]
        + [pltpu.VMEM((LEAF, LEAF), jnp.float32)] * 3,
    )(a)


def split_bf16(x):
    hi = lax.reduce_precision(x, exponent_bits=8, mantissa_bits=7)
    return hi.astype(jnp.bfloat16), (x - hi).astype(jnp.bfloat16)


def update_kernel(kind, tm, width, nbase, flags_ref, info_ref, slots_ref, *refs):
    base_refs = refs[:nbase]
    a_ref, bhi_ref, blo_ref, out_ref = refs[nbase:]
    i = pl.program_id(0)
    active = flags_ref[i] != 0

    def base_cols(g):
        cols = pl.ds(g * PANEL, PANEL)
        if kind == "gather":
            return base_refs[g][0]
        if kind == "diag":
            rows = info_ref[2] + i * tm + lax.broadcasted_iota(jnp.int32, (tm, PANEL), 0)
            ids = info_ref[1] + g * PANEL + lax.broadcasted_iota(jnp.int32, (tm, PANEL), 1)
            return jnp.where(rows == ids, base_refs[0][...], 0.0)
        return base_refs[0][:, cols]

    @pl.when(active)
    def _():
        a = a_ref[...]
        a_hi = a.astype(jnp.bfloat16)
        a_lo = (a - a_hi.astype(jnp.float32)).astype(jnp.bfloat16)
        dn = (((1,), (1,)), ((), ()))
        for g in range(width // PANEL):
            rows = pl.ds(g * PANEL, PANEL)
            b_hi = bhi_ref[rows, :]
            acc = lax.dot_general(a_hi, b_hi, dn, preferred_element_type=jnp.float32)
            acc = acc + lax.dot_general(a_hi, blo_ref[rows, :], dn, preferred_element_type=jnp.float32)
            acc = acc + lax.dot_general(a_lo, b_hi, dn, preferred_element_type=jnp.float32)
            out_ref[:, pl.ds(g * PANEL, PANEL)] = base_cols(g) - acc

    @pl.when(jnp.logical_not(active))
    def _():
        for g in range(width // PANEL):
            out_ref[:, pl.ds(g * PANEL, PANEL)] = base_cols(g)

    @pl.when((info_ref[0] == 1) & (info_ref[1] == 0))
    def _():
        out_ref[:, pl.ds(0, PANEL)] = a_ref[...]


def panel_update(kind, base, a, b_hi, b_lo, flags, info, slots, rows, width):
    tm = MSLOT
    nseg = width // PANEL
    if kind == "gather":
        bases = [base] * nseg
        base_specs = [
            pl.BlockSpec((1, tm, PANEL), lambda i, f, n, s, g=g: (s[i * nseg + g], 0, 0)) for g in range(nseg)
        ]
    elif kind == "diag":
        bases = [base]
        base_specs = [pl.BlockSpec((tm, 1), lambda i, f, n, s: (i, 0))]
    else:
        bases = [base]
        base_specs = [pl.BlockSpec((tm, width), lambda i, f, n, s: (i, 0))]
    grid_spec = pltpu.PrefetchScalarGridSpec(
        num_scalar_prefetch=3,
        grid=(rows // tm,),
        in_specs=base_specs + [
            pl.BlockSpec((tm, PANEL), lambda i, f, n, s: (i, 0)),
            pl.BlockSpec((width, PANEL), lambda i, f, n, s: (0, 0)),
            pl.BlockSpec((width, PANEL), lambda i, f, n, s: (0, 0)),
        ],
        out_specs=pl.BlockSpec((tm, width), lambda i, f, n, s: (i, 0)),
    )
    flops = 6 * rows * width * PANEL
    cost = pl.CostEstimate(flops=flops, transcendentals=0, bytes_accessed=rows * width * 8 + width * PANEL * 4)
    return pl.pallas_call(
        functools.partial(update_kernel, kind, tm, width, len(bases)),
        grid_spec=grid_spec,
        out_shape=jax.ShapeDtypeStruct((rows, width), jnp.float32),
        cost_estimate=cost,
        compiler_params=pltpu.CompilerParams(vmem_limit_bytes=48 * 1024 * 1024),
    )(flags, info, slots, *bases, a, b_hi, b_lo)


def solve_kernel(x_ref, fhi_ref, flo_ref, out_ref, hi_ref, lo_ref):
    x = x_ref[...]
    x_hi = x.astype(jnp.bfloat16)
    x_lo = (x - x_hi.astype(jnp.float32)).astype(jnp.bfloat16)
    f_hi = fhi_ref[...]
    acc = lax.dot_general(x_hi, f_hi, NT, preferred_element_type=jnp.float32)
    acc = acc + lax.dot_general(x_hi, flo_ref[...], NT, preferred_element_type=jnp.float32)
    acc = acc + lax.dot_general(x_lo, f_hi, NT, preferred_element_type=jnp.float32)
    out_ref[...] = acc
    hi = acc.astype(jnp.bfloat16)
    hi_ref[...] = hi
    lo_ref[...] = (acc - hi.astype(jnp.float32)).astype(jnp.bfloat16)


def apply_inverse(x, f_hi, f_lo):
    rows = x.shape[0]
    tm = 256 if rows % 256 == 0 else MSLOT
    spec = pl.BlockSpec((tm, PANEL), lambda i: (i, 0))
    return pl.pallas_call(
        solve_kernel,
        grid=(rows // tm,),
        in_specs=[
            spec,
            pl.BlockSpec((PANEL, PANEL), lambda i: (0, 0)),
            pl.BlockSpec((PANEL, PANEL), lambda i: (0, 0)),
        ],
        out_specs=[spec, spec, spec],
        out_shape=[
            jax.ShapeDtypeStruct((rows, PANEL), jnp.float32),
            jax.ShapeDtypeStruct((rows, PANEL), jnp.bfloat16),
            jax.ShapeDtypeStruct((rows, PANEL), jnp.bfloat16),
        ],
        cost_estimate=pl.CostEstimate(flops=6 * rows * PANEL * PANEL, transcendentals=0, bytes_accessed=8 * rows * PANEL),
    )(x, f_hi, f_lo)


def dot_t(left, right):
    contract = (((1,), (1,)), ((), ()))
    l_hi, l_lo = split_bf16(left)
    r_hi, r_lo = split_bf16(right)
    out = lax.dot_general(l_hi, r_hi, contract, preferred_element_type=jnp.float32)
    out = out + lax.dot_general(l_hi, r_lo, contract, preferred_element_type=jnp.float32)
    return out + lax.dot_general(l_lo, r_hi, contract, preferred_element_type=jnp.float32)


def pick(index, options):
    out = options[0]
    for i in range(1, len(options)):
        out = jnp.where(index == i, options[i], out)
    return out


def seg0_slots(tseg, cap0):
    has0 = jnp.any(tseg == 0, axis=1)
    rank0 = jnp.cumsum(has0.astype(jnp.int32)) - 1
    slot = jnp.where(has0, rank0, cap0)
    return has0, rank0, slot


def per_device(eigvecs, coupling, mode_counts, tree_segments, eigvals, stiff):
    R = lax.axis_size("row")
    C = lax.axis_size("col")
    r = lax.axis_index("row")
    c = lax.axis_index("col")
    nsub = eigvecs.shape[0]
    H, W = stiff.shape
    Ec = coupling.shape[3]
    G = W // PANEL
    ratio = R // C
    npair = 2 * nsub
    cap = min(MOST * G * ((nsub + SUB_ROW - 1) // SUB_ROW), npair)
    cap0 = min(MOST * ((nsub + SUB_ROW - 1) // SUB_ROW), nsub)

    live = jnp.arange(MSLOT, dtype=jnp.int32)[None, :] < mode_counts[:, None]
    pieces = jnp.einsum("sim,sitp->stmp", eigvecs, coupling, preferred_element_type=jnp.float32)
    pieces = pieces * live.astype(jnp.float32)[:, None, :, None]
    flat = pieces.reshape(npair, MSLOT, Ec)
    flat_pad = jnp.concatenate([flat, jnp.zeros((1, MSLOT, Ec), jnp.float32)], axis=0)

    kpp_src = stiff[:PANEL, :PANEL]
    rs = PANEL // R
    got = [kpp_src[:rs]]
    for i in range(1, R):
        got.append(lax.ppermute(kpp_src[i * rs:(i + 1) * rs], AXES, [(0, i * C)]))
    kpp_part = pick(r, got)
    kpp_col0 = lax.all_gather(kpp_part, "row", axis=0, tiled=True)
    cs = PANEL // C
    got = [kpp_col0[:cs]]
    for k in range(1, C):
        got.append(lax.ppermute(kpp_col0[k * cs:(k + 1) * cs], AXES, [(i * C, i * C + k) for i in range(R)]))
    kpp = lax.all_gather(pick(c, got), "col", axis=0, tiled=True)

    finv = chol_inverse(kpp)

    tseg = tree_segments
    dest = (tseg // G).reshape(npair)
    onehot = dest[:, None] == jnp.arange(C, dtype=jnp.int32)[None, :]
    rank_pd = jnp.cumsum(onehot.astype(jnp.int32), axis=0) - 1
    rank = jnp.sum(jnp.where(onehot, rank_pd, 0), axis=1)
    match = onehot[:, :, None] & (rank_pd[:, :, None] == jnp.arange(cap, dtype=jnp.int32)[None, None, :])
    send_idx = jnp.where(jnp.any(match, axis=0), jnp.argmax(match, axis=0), npair)
    send = flat_pad[send_idx]
    send, _ = lax.optimization_barrier((send, kpp))
    shifted = [send[c]]
    for k in range(1, C):
        out_k = lax.dynamic_index_in_dim(send, (c + k) % C, axis=0, keepdims=False)
        shifted.append(lax.ppermute(out_k, "col", [(i, (i + k) % C) for i in range(C)]))
    shifted = jnp.stack(shifted)
    recv = shifted[(c - jnp.arange(C, dtype=jnp.int32)) % C]
    recv_t = recv.transpose(1, 2, 0, 3).reshape(cap, MSLOT, C * Ec)
    recv_t = jnp.concatenate([recv_t, jnp.zeros((1, MSLOT, PANEL), jnp.float32)], axis=0)
    my_seg = c * G + jnp.arange(G, dtype=jnp.int32)
    seg_hit = tseg[:, :, None] == my_seg[None, None, :]
    rank2 = rank.reshape(nsub, 2)
    slot_tab = jnp.where(
        jnp.any(seg_hit, axis=1), jnp.sum(jnp.where(seg_hit, rank2[:, :, None], 0), axis=1), cap
    )

    has0, rank0, slot_r = seg0_slots(tseg, cap0)
    t0 = jnp.where(tseg[:, 0] == 0, 0, 1)
    sel = has0[:, None] & (rank0[:, None] == jnp.arange(cap0, dtype=jnp.int32)[None, :])
    sel_sub = jnp.argmax(sel, axis=0)
    zidx = jnp.where(jnp.any(sel, axis=0), sel_sub * 2 + t0[sel_sub], npair)
    z_local = flat_pad[zidx]
    z_all = lax.all_gather(z_local, "col", axis=0, tiled=False)
    z_rows = z_all.transpose(1, 2, 0, 3).reshape(cap0 * MSLOT, C * Ec)

    m_src = stiff[:, :PANEL]
    rps = W // R
    zps = cap0 * MSLOT // C
    got = [m_src[:rps]]
    for k in range(1, C):
        got.append(lax.ppermute(m_src[k * rps:(k + 1) * rps], AXES, [(i * C, i * C + k) for i in range(R)]))
    a_slice = pick(c, got)
    m_row = lax.all_gather(a_slice, "col", axis=0, tiled=True)
    slot_row = jnp.zeros((8, PANEL), jnp.float32).at[0, :nsub].set(slot_r.astype(jnp.float32))
    payload = jnp.concatenate([a_slice, lax.dynamic_slice_in_dim(z_rows, c * zps, zps), slot_row], axis=0)
    perm = [(i * C + k, ((i % ratio) * C + k) * C + i // ratio) for i in range(R) for k in range(C)]
    b_slice = lax.ppermute(payload, AXES, perm)
    col_parts = lax.all_gather(b_slice, "row", axis=0, tiled=False)
    m_col = col_parts[:, :rps].reshape(W, PANEL)
    z_col = col_parts[:, rps:rps + zps].reshape(ratio * cap0 * MSLOT, PANEL)

    slot_c = []
    for j in range(ratio):
        got_slot = col_parts[j * C, rps + zps, :nsub].astype(jnp.int32)
        slot_c.append(jnp.where(got_slot < cap0, j * cap0 + got_slot, ratio * cap0))
    slot_c = jnp.concatenate(slot_c)

    f_hi, f_lo = split_bf16(finv)
    low_r, _, _ = apply_inverse(m_row, f_hi, f_lo)
    _, lowc_hi, lowc_lo = apply_inverse(m_col, f_hi, f_lo)
    lowmi_r, _, _ = apply_inverse(z_rows, f_hi, f_lo)
    _, lmc_hi, lmc_lo = apply_inverse(z_col, f_hi, f_lo)

    ones = jnp.ones((H // MSLOT,), jnp.int32)
    none = jnp.zeros((1,), jnp.int32)
    info = jnp.stack([jnp.int32(1), c * W, r * H, jnp.int32(0)]).astype(jnp.int32)
    reduced_ii = panel_update("array", stiff, low_r, lowc_hi, lowc_lo, ones, info, none, H, W)

    lmi = jnp.concatenate(
        [lowmi_r.reshape(cap0, MSLOT, PANEL), jnp.zeros((1, MSLOT, PANEL), jnp.float32)], axis=0
    )
    lmi_full = lmi[slot_r].reshape(nsub * MSLOT, PANEL)
    flags = has0.astype(jnp.int32)
    reduced_mi = panel_update(
        "gather", recv_t, lmi_full, lowc_hi, lowc_lo, flags, info, slot_tab.reshape(-1).astype(jnp.int32), nsub * MSLOT, W
    )

    nc = ratio * cap0
    mode_width = ratio * nsub * MSLOT

    def spread_cols(part):
        part = jnp.concatenate([part.reshape(nc, MSLOT, PANEL), jnp.zeros((1, MSLOT, PANEL), part.dtype)], axis=0)
        return part[slot_c].reshape(mode_width, PANEL)

    diag_values = jnp.where(live, eigvals, 1.0).reshape(-1, 1)
    mode_rows = diag_values.shape[0]
    info_mm = jnp.stack([jnp.int32(0), c * mode_width, r * mode_rows, jnp.int32(0)]).astype(jnp.int32)
    reduced_mm = panel_update("diag", diag_values, lmi_full, spread_cols(lmc_hi), spread_cols(lmc_lo), flags, info_mm, none, mode_rows, mode_width)
    return (reduced_ii, reduced_mi, reduced_mm)


def solution(mesh):
    in_specs = (
        P("row", None, None),
        P("row", None, None, "col"),
        P("row"),
        P("row", None),
        P("row", None),
        P("row", "col"),
    )
    out_specs = (P("row", "col"), P("row", "col"), P("row", "col"))
    return jax.shard_map(
        per_device, mesh=mesh, in_specs=in_specs, out_specs=out_specs, check_vma=False
    )
```

```python
import functools

import jax
import jax.numpy as jnp
from jax import lax
from jax.sharding import PartitionSpec as P
from jax.experimental import pallas as pl
from jax.experimental.pallas import tpu as pltpu

MSLOT = 128
PANEL = 512
MOST = 2
SUB_ROW = 8

AXES = ("row", "col")
LEAF = 128


def mm3(a, b, dn):
    a_hi = a.astype(jnp.bfloat16)
    a_lo = (a - a_hi.astype(jnp.float32)).astype(jnp.bfloat16)
    b_hi = b.astype(jnp.bfloat16)
    b_lo = (b - b_hi.astype(jnp.float32)).astype(jnp.bfloat16)
    out = lax.dot_general(a_hi, b_hi, dn, preferred_element_type=jnp.float32)
    out = out + lax.dot_general(a_hi, b_lo, dn, preferred_element_type=jnp.float32)
    return out + lax.dot_general(a_lo, b_hi, dn, preferred_element_type=jnp.float32)


NN = (((1,), (0,)), ((), ()))
NT = (((1,), (1,)), ((), ()))


def leaf_inverse(d, d_ref, e_ref, x_ref):
    n = d.shape[0]
    sub = lax.broadcasted_iota(jnp.int32, (n, n), 0)
    lane = lax.broadcasted_iota(jnp.int32, (n, n), 1)
    sub_c = lax.broadcasted_iota(jnp.int32, (n, 1), 0)
    lane_r = lax.broadcasted_iota(jnp.int32, (1, n), 1)
    d_ref[...] = d
    e_ref[...] = jnp.where(sub == lane, 1.0, 0.0).astype(jnp.float32)
    x_ref[...] = jnp.zeros((n, n), jnp.float32)

    def step(k, carry):
        dm = d_ref[...]
        colk = jnp.sum(jnp.where(lane == k, dm, 0.0), axis=1, keepdims=True)
        rowk = d_ref[pl.ds(k, 1), :]
        dkk = jnp.sum(jnp.where(lane_r == k, rowk, 0.0), axis=1, keepdims=True)
        s = lax.rsqrt(dkk)
        lc = jnp.where(sub_c > k, colk * s, 0.0)
        lr = jnp.where(lane_r > k, rowk * s, 0.0)
        d_ref[...] = dm - lc * lr
        xk = e_ref[pl.ds(k, 1), :] * s
        x_ref[pl.ds(k, 1), :] = xk
        e_ref[...] = e_ref[...] - lc * xk
        return carry

    lax.fori_loop(0, n, step, 0, unroll=8)
    return x_ref[...]


def chol_inv_kernel(a_ref, x_ref, w_ref, l_ref, d_ref, e_ref, xl_ref):
    n = a_ref.shape[0]
    nb = n // LEAF
    w_ref[...] = a_ref[...]
    for kb in range(nb):
        o = kb * LEAF
        blk = pl.ds(o, LEAF)
        xkk = leaf_inverse(w_ref[blk, blk], d_ref, e_ref, xl_ref)
        x_ref[blk, blk] = xkk
        if kb + 1 < nb:
            rest = pl.ds(o + LEAF, n - o - LEAF)
            panel = mm3(w_ref[rest, blk], xkk, NT)
            l_ref[rest, blk] = panel
            w_ref[rest, rest] = w_ref[rest, rest] - mm3(panel, panel, NT)
    for i in range(1, nb):
        bi = pl.ds(i * LEAF, LEAF)
        xii = x_ref[bi, bi]
        for j in range(i):
            bj = pl.ds(j * LEAF, LEAF)
            acc = None
            for k in range(j, i):
                bk = pl.ds(k * LEAF, LEAF)
                term = mm3(l_ref[bi, bk], x_ref[bk, bj], NN)
                acc = term if acc is None else acc + term
            x_ref[bi, bj] = -mm3(xii, acc, NN)
        for j in range(i + 1, nb):
            x_ref[bi, pl.ds(j * LEAF, LEAF)] = jnp.zeros((LEAF, LEAF), jnp.float32)
    x_ref[pl.ds(0, LEAF), pl.ds(LEAF, n - LEAF)] = jnp.zeros((LEAF, n - LEAF), jnp.float32)


def chol_inverse(a):
    n = a.shape[0]
    return pl.pallas_call(
        chol_inv_kernel,
        out_shape=jax.ShapeDtypeStruct((n, n), jnp.float32),
        cost_estimate=pl.CostEstimate(flops=800 * n ** 3, transcendentals=n, bytes_accessed=8 * n * n),
        in_specs=[pl.BlockSpec(memory_space=pltpu.VMEM)],
        out_specs=pl.BlockSpec(memory_space=pltpu.VMEM),
        scratch_shapes=[pltpu.VMEM((n, n), jnp.float32), pltpu.VMEM((n, n), jnp.float32)]
        + [pltpu.VMEM((LEAF, LEAF), jnp.float32)] * 3,
    )(a)


def split_bf16(x):
    hi = lax.reduce_precision(x, exponent_bits=8, mantissa_bits=7)
    return hi.astype(jnp.bfloat16), (x - hi).astype(jnp.bfloat16)


def update_kernel(kind, tm, width, nbase, flags_ref, info_ref, slots_ref, *refs):
    base_refs = refs[:nbase]
    a_ref, bhi_ref, blo_ref, out_ref = refs[nbase:]
    i = pl.program_id(0)
    active = flags_ref[i] != 0

    def base_cols(g):
        cols = pl.ds(g * PANEL, PANEL)
        if kind == "gather":
            return base_refs[g][0]
        if kind == "diag":
            rows = info_ref[2] + i * tm + lax.broadcasted_iota(jnp.int32, (tm, PANEL), 0)
            ids = info_ref[1] + g * PANEL + lax.broadcasted_iota(jnp.int32, (tm, PANEL), 1)
            return jnp.where(rows == ids, base_refs[0][...], 0.0)
        return base_refs[0][:, cols]

    @pl.when(active)
    def _():
        a = a_ref[...]
        a_hi = a.astype(jnp.bfloat16)
        a_lo = (a - a_hi.astype(jnp.float32)).astype(jnp.bfloat16)
        dn = (((1,), (1,)), ((), ()))
        for g in range(width // PANEL):
            rows = pl.ds(g * PANEL, PANEL)
            b_hi = bhi_ref[rows, :]
            acc = lax.dot_general(a_hi, b_hi, dn, preferred_element_type=jnp.float32)
            acc = acc + lax.dot_general(a_hi, blo_ref[rows, :], dn, preferred_element_type=jnp.float32)
            acc = acc + lax.dot_general(a_lo, b_hi, dn, preferred_element_type=jnp.float32)
            out_ref[:, pl.ds(g * PANEL, PANEL)] = base_cols(g) - acc

    @pl.when(jnp.logical_not(active))
    def _():
        for g in range(width // PANEL):
            out_ref[:, pl.ds(g * PANEL, PANEL)] = base_cols(g)

    @pl.when((info_ref[0] == 1) & (info_ref[1] == 0))
    def _():
        out_ref[:, pl.ds(0, PANEL)] = a_ref[...]


def panel_update(kind, base, a, b_hi, b_lo, flags, info, slots, rows, width):
    tm = MSLOT
    nseg = width // PANEL
    if kind == "gather":
        bases = [base] * nseg
        base_specs = [
            pl.BlockSpec((1, tm, PANEL), lambda i, f, n, s, g=g: (s[i * nseg + g], 0, 0)) for g in range(nseg)
        ]
    elif kind == "diag":
        bases = [base]
        base_specs = [pl.BlockSpec((tm, 1), lambda i, f, n, s: (i, 0))]
    else:
        bases = [base]
        base_specs = [pl.BlockSpec((tm, width), lambda i, f, n, s: (i, 0))]
    grid_spec = pltpu.PrefetchScalarGridSpec(
        num_scalar_prefetch=3,
        grid=(rows // tm,),
        in_specs=base_specs + [
            pl.BlockSpec((tm, PANEL), lambda i, f, n, s: (i, 0)),
            pl.BlockSpec((width, PANEL), lambda i, f, n, s: (0, 0)),
            pl.BlockSpec((width, PANEL), lambda i, f, n, s: (0, 0)),
        ],
        out_specs=pl.BlockSpec((tm, width), lambda i, f, n, s: (i, 0)),
    )
    flops = 6 * rows * width * PANEL
    cost = pl.CostEstimate(flops=flops, transcendentals=0, bytes_accessed=rows * width * 8 + width * PANEL * 4)
    return pl.pallas_call(
        functools.partial(update_kernel, kind, tm, width, len(bases)),
        grid_spec=grid_spec,
        out_shape=jax.ShapeDtypeStruct((rows, width), jnp.float32),
        cost_estimate=cost,
        compiler_params=pltpu.CompilerParams(vmem_limit_bytes=48 * 1024 * 1024),
    )(flags, info, slots, *bases, a, b_hi, b_lo)


def solve_kernel(x_ref, fhi_ref, flo_ref, out_ref, hi_ref, lo_ref):
    x = x_ref[...]
    x_hi = x.astype(jnp.bfloat16)
    x_lo = (x - x_hi.astype(jnp.float32)).astype(jnp.bfloat16)
    f_hi = fhi_ref[...]
    acc = lax.dot_general(x_hi, f_hi, NT, preferred_element_type=jnp.float32)
    acc = acc + lax.dot_general(x_hi, flo_ref[...], NT, preferred_element_type=jnp.float32)
    acc = acc + lax.dot_general(x_lo, f_hi, NT, preferred_element_type=jnp.float32)
    out_ref[...] = acc
    hi = acc.astype(jnp.bfloat16)
    hi_ref[...] = hi
    lo_ref[...] = (acc - hi.astype(jnp.float32)).astype(jnp.bfloat16)


def apply_inverse(x, f_hi, f_lo, parts=None):
    if parts is None:
        rows = x.shape[0]
        tm = 256 if rows % 256 == 0 else MSLOT
        grid = rows // tm
        x_spec = pl.BlockSpec((tm, PANEL), lambda i: (i, 0))
    else:
        tm, at = parts
        grid = x.shape[0]
        rows = grid * tm
        x_spec = pl.BlockSpec((None, tm, PANEL), lambda i: (i, at, 0))
    spec = pl.BlockSpec((tm, PANEL), lambda i: (i, 0))
    return pl.pallas_call(
        solve_kernel,
        grid=(grid,),
        in_specs=[
            x_spec,
            pl.BlockSpec((PANEL, PANEL), lambda i: (0, 0)),
            pl.BlockSpec((PANEL, PANEL), lambda i: (0, 0)),
        ],
        out_specs=[spec, spec, spec],
        out_shape=[
            jax.ShapeDtypeStruct((rows, PANEL), jnp.float32),
            jax.ShapeDtypeStruct((rows, PANEL), jnp.bfloat16),
            jax.ShapeDtypeStruct((rows, PANEL), jnp.bfloat16),
        ],
        cost_estimate=pl.CostEstimate(flops=6 * rows * PANEL * PANEL, transcendentals=0, bytes_accessed=8 * rows * PANEL),
    )(x, f_hi, f_lo)


def dot_t(left, right):
    contract = (((1,), (1,)), ((), ()))
    l_hi, l_lo = split_bf16(left)
    r_hi, r_lo = split_bf16(right)
    out = lax.dot_general(l_hi, r_hi, contract, preferred_element_type=jnp.float32)
    out = out + lax.dot_general(l_hi, r_lo, contract, preferred_element_type=jnp.float32)
    return out + lax.dot_general(l_lo, r_hi, contract, preferred_element_type=jnp.float32)


def pick(index, options):
    out = options[0]
    for i in range(1, len(options)):
        out = jnp.where(index == i, options[i], out)
    return out


def seg0_slots(tseg, cap0):
    has0 = jnp.any(tseg == 0, axis=1)
    rank0 = jnp.cumsum(has0.astype(jnp.int32)) - 1
    slot = jnp.where(has0, rank0, cap0)
    return has0, rank0, slot


def per_device(eigvecs, coupling, mode_counts, tree_segments, eigvals, stiff):
    R = lax.axis_size("row")
    C = lax.axis_size("col")
    r = lax.axis_index("row")
    c = lax.axis_index("col")
    nsub = eigvecs.shape[0]
    H, W = stiff.shape
    Ec = coupling.shape[3]
    G = W // PANEL
    ratio = R // C
    npair = 2 * nsub
    cap = min(MOST * G * ((nsub + SUB_ROW - 1) // SUB_ROW), npair)
    cap0 = min(MOST * ((nsub + SUB_ROW - 1) // SUB_ROW), nsub)

    live = jnp.arange(MSLOT, dtype=jnp.int32)[None, :] < mode_counts[:, None]
    pieces = jnp.einsum("sim,sitp->stmp", eigvecs, coupling, preferred_element_type=jnp.float32)
    pieces = pieces * live.astype(jnp.float32)[:, None, :, None]
    flat = pieces.reshape(npair, MSLOT, Ec)
    flat_pad = jnp.concatenate([flat, jnp.zeros((1, MSLOT, Ec), jnp.float32)], axis=0)

    kpp_src = stiff[:PANEL, :PANEL]
    rs = PANEL // R
    got = [kpp_src[:rs]]
    for i in range(1, R):
        got.append(lax.ppermute(kpp_src[i * rs:(i + 1) * rs], AXES, [(0, i * C)]))
    kpp_part = pick(r, got)
    kpp_col0 = lax.all_gather(kpp_part, "row", axis=0, tiled=True)
    cs = PANEL // C
    got = [kpp_col0[:cs]]
    for k in range(1, C):
        got.append(lax.ppermute(kpp_col0[k * cs:(k + 1) * cs], AXES, [(i * C, i * C + k) for i in range(R)]))
    kpp = lax.all_gather(pick(c, got), "col", axis=0, tiled=True)

    finv = chol_inverse(kpp)

    tseg = tree_segments
    dest = (tseg // G).reshape(npair)
    onehot = dest[:, None] == jnp.arange(C, dtype=jnp.int32)[None, :]
    rank_pd = jnp.cumsum(onehot.astype(jnp.int32), axis=0) - 1
    rank = jnp.sum(jnp.where(onehot, rank_pd, 0), axis=1)
    match = onehot[:, :, None] & (rank_pd[:, :, None] == jnp.arange(cap, dtype=jnp.int32)[None, None, :])
    send_idx = jnp.where(jnp.any(match, axis=0), jnp.argmax(match, axis=0), npair)
    send = flat_pad[send_idx]
    send, _ = lax.optimization_barrier((send, kpp))
    shifted = [send[c]]
    for k in range(1, C):
        out_k = lax.dynamic_index_in_dim(send, (c + k) % C, axis=0, keepdims=False)
        shifted.append(lax.ppermute(out_k, "col", [(i, (i + k) % C) for i in range(C)]))
    shifted = jnp.stack(shifted)
    recv = shifted[(c - jnp.arange(C, dtype=jnp.int32)) % C]
    recv_t = recv.transpose(1, 2, 0, 3).reshape(cap, MSLOT, C * Ec)
    recv_t = jnp.concatenate([recv_t, jnp.zeros((1, MSLOT, PANEL), jnp.float32)], axis=0)
    my_seg = c * G + jnp.arange(G, dtype=jnp.int32)
    seg_hit = tseg[:, :, None] == my_seg[None, None, :]
    rank2 = rank.reshape(nsub, 2)
    slot_tab = jnp.where(
        jnp.any(seg_hit, axis=1), jnp.sum(jnp.where(seg_hit, rank2[:, :, None], 0), axis=1), cap
    )

    has0, rank0, slot_r = seg0_slots(tseg, cap0)
    t0 = jnp.where(tseg[:, 0] == 0, 0, 1)
    sel = has0[:, None] & (rank0[:, None] == jnp.arange(cap0, dtype=jnp.int32)[None, :])
    sel_sub = jnp.argmax(sel, axis=0)
    zidx = jnp.where(jnp.any(sel, axis=0), sel_sub * 2 + t0[sel_sub], npair)
    z_local = flat_pad[zidx]
    z_all = lax.all_gather(z_local, "col", axis=0, tiled=False)
    z_rows = z_all.transpose(1, 2, 0, 3).reshape(cap0 * MSLOT, C * Ec)

    m_src = stiff[:, :PANEL]
    rps = W // R
    zps = cap0 * MSLOT // C
    got = [m_src[:rps]]
    for k in range(1, C):
        got.append(lax.ppermute(m_src[k * rps:(k + 1) * rps], AXES, [(i * C, i * C + k) for i in range(R)]))
    a_slice = pick(c, got)
    m_row = lax.all_gather(a_slice, "col", axis=0, tiled=True)
    slot_row = jnp.zeros((8, PANEL), jnp.float32).at[0, :nsub].set(slot_r.astype(jnp.float32))
    payload = jnp.concatenate([a_slice, lax.dynamic_slice_in_dim(z_rows, c * zps, zps), slot_row], axis=0)
    perm = [(i * C + k, ((i % ratio) * C + k) * C + i // ratio) for i in range(R) for k in range(C)]
    b_slice = lax.ppermute(payload, AXES, perm)
    col_parts = lax.all_gather(b_slice, "row", axis=0, tiled=False)

    slot_c = []
    for j in range(ratio):
        got_slot = col_parts[j * C, rps + zps, :nsub].astype(jnp.int32)
        slot_c.append(jnp.where(got_slot < cap0, j * cap0 + got_slot, ratio * cap0))
    slot_c = jnp.concatenate(slot_c)

    f_hi, f_lo = split_bf16(finv)
    low_r, _, _ = apply_inverse(m_row, f_hi, f_lo)
    _, lowc_hi, lowc_lo = apply_inverse(col_parts, f_hi, f_lo, (rps, 0))
    lowmi_r, _, _ = apply_inverse(z_rows, f_hi, f_lo)
    _, lmc_hi, lmc_lo = apply_inverse(col_parts, f_hi, f_lo, (zps, rps // zps))

    ones = jnp.ones((H // MSLOT,), jnp.int32)
    none = jnp.zeros((1,), jnp.int32)
    info = jnp.stack([jnp.int32(1), c * W, r * H, jnp.int32(0)]).astype(jnp.int32)
    reduced_ii = panel_update("array", stiff, low_r, lowc_hi, lowc_lo, ones, info, none, H, W)

    lmi = jnp.concatenate(
        [lowmi_r.reshape(cap0, MSLOT, PANEL), jnp.zeros((1, MSLOT, PANEL), jnp.float32)], axis=0
    )
    lmi_full = lmi[slot_r].reshape(nsub * MSLOT, PANEL)
    flags = has0.astype(jnp.int32)
    reduced_mi = panel_update(
        "gather", recv_t, lmi_full, lowc_hi, lowc_lo, flags, info, slot_tab.reshape(-1).astype(jnp.int32), nsub * MSLOT, W
    )

    nc = ratio * cap0
    mode_width = ratio * nsub * MSLOT

    def spread_cols(part):
        part = jnp.concatenate([part.reshape(nc, MSLOT, PANEL), jnp.zeros((1, MSLOT, PANEL), part.dtype)], axis=0)
        return part[slot_c].reshape(mode_width, PANEL)

    diag_values = jnp.where(live, eigvals, 1.0).reshape(-1, 1)
    mode_rows = diag_values.shape[0]
    info_mm = jnp.stack([jnp.int32(0), c * mode_width, r * mode_rows, jnp.int32(0)]).astype(jnp.int32)
    reduced_mm = panel_update("diag", diag_values, lmi_full, spread_cols(lmc_hi), spread_cols(lmc_lo), flags, info_mm, none, mode_rows, mode_width)
    return (reduced_ii, reduced_mi, reduced_mm)


def solution(mesh):
    in_specs = (
        P("row", None, None),
        P("row", None, None, "col"),
        P("row"),
        P("row", None),
        P("row", None),
        P("row", "col"),
    )
    out_specs = (P("row", "col"), P("row", "col"), P("row", "col"))
    return jax.shard_map(
        per_device, mesh=mesh, in_specs=in_specs, out_specs=out_specs, check_vma=False
    )
```

```python
import functools

import jax
import jax.numpy as jnp
from jax import lax
from jax.sharding import PartitionSpec as P
from jax.experimental import pallas as pl
from jax.experimental.pallas import tpu as pltpu

MSLOT = 128
PANEL = 512
MOST = 2
SUB_ROW = 8

AXES = ("row", "col")
LEAF = 128


def mm3(a, b, dn):
    a_hi = a.astype(jnp.bfloat16)
    a_lo = (a - a_hi.astype(jnp.float32)).astype(jnp.bfloat16)
    b_hi = b.astype(jnp.bfloat16)
    b_lo = (b - b_hi.astype(jnp.float32)).astype(jnp.bfloat16)
    out = lax.dot_general(a_hi, b_hi, dn, preferred_element_type=jnp.float32)
    out = out + lax.dot_general(a_hi, b_lo, dn, preferred_element_type=jnp.float32)
    return out + lax.dot_general(a_lo, b_hi, dn, preferred_element_type=jnp.float32)


NN = (((1,), (0,)), ((), ()))
NT = (((1,), (1,)), ((), ()))


def leaf_inverse(d, d_ref, e_ref, x_ref):
    n = d.shape[0]
    sub = lax.broadcasted_iota(jnp.int32, (n, n), 0)
    lane = lax.broadcasted_iota(jnp.int32, (n, n), 1)
    sub_c = lax.broadcasted_iota(jnp.int32, (n, 1), 0)
    lane_r = lax.broadcasted_iota(jnp.int32, (1, n), 1)
    d_ref[...] = d
    e_ref[...] = jnp.where(sub == lane, 1.0, 0.0).astype(jnp.float32)
    x_ref[...] = jnp.zeros((n, n), jnp.float32)

    def step(k, carry):
        dm = d_ref[...]
        colk = jnp.sum(jnp.where(lane == k, dm, 0.0), axis=1, keepdims=True)
        rowk = d_ref[pl.ds(k, 1), :]
        dkk = jnp.sum(jnp.where(lane_r == k, rowk, 0.0), axis=1, keepdims=True)
        s = lax.rsqrt(dkk)
        lc = jnp.where(sub_c > k, colk * s, 0.0)
        lr = jnp.where(lane_r > k, rowk * s, 0.0)
        d_ref[...] = dm - lc * lr
        xk = e_ref[pl.ds(k, 1), :] * s
        x_ref[pl.ds(k, 1), :] = xk
        e_ref[...] = e_ref[...] - lc * xk
        return carry

    lax.fori_loop(0, n, step, 0, unroll=8)
    return x_ref[...]


def chol_inv_kernel(a_ref, x_ref, w_ref, l_ref, d_ref, e_ref, xl_ref):
    n = a_ref.shape[0]
    nb = n // LEAF
    w_ref[...] = a_ref[...]
    for kb in range(nb):
        o = kb * LEAF
        blk = pl.ds(o, LEAF)
        xkk = leaf_inverse(w_ref[blk, blk], d_ref, e_ref, xl_ref)
        x_ref[blk, blk] = xkk
        if kb + 1 < nb:
            rest = pl.ds(o + LEAF, n - o - LEAF)
            panel = mm3(w_ref[rest, blk], xkk, NT)
            l_ref[rest, blk] = panel
            w_ref[rest, rest] = w_ref[rest, rest] - mm3(panel, panel, NT)
    for i in range(1, nb):
        bi = pl.ds(i * LEAF, LEAF)
        xii = x_ref[bi, bi]
        for j in range(i):
            bj = pl.ds(j * LEAF, LEAF)
            acc = None
            for k in range(j, i):
                bk = pl.ds(k * LEAF, LEAF)
                term = mm3(l_ref[bi, bk], x_ref[bk, bj], NN)
                acc = term if acc is None else acc + term
            x_ref[bi, bj] = -mm3(xii, acc, NN)
        for j in range(i + 1, nb):
            x_ref[bi, pl.ds(j * LEAF, LEAF)] = jnp.zeros((LEAF, LEAF), jnp.float32)
    x_ref[pl.ds(0, LEAF), pl.ds(LEAF, n - LEAF)] = jnp.zeros((LEAF, n - LEAF), jnp.float32)


def chol_inverse(a):
    n = a.shape[0]
    return pl.pallas_call(
        chol_inv_kernel,
        out_shape=jax.ShapeDtypeStruct((n, n), jnp.float32),
        cost_estimate=pl.CostEstimate(flops=800 * n ** 3, transcendentals=n, bytes_accessed=8 * n * n),
        in_specs=[pl.BlockSpec(memory_space=pltpu.VMEM)],
        out_specs=pl.BlockSpec(memory_space=pltpu.VMEM),
        scratch_shapes=[pltpu.VMEM((n, n), jnp.float32), pltpu.VMEM((n, n), jnp.float32)]
        + [pltpu.VMEM((LEAF, LEAF), jnp.float32)] * 3,
    )(a)


def split_bf16(x):
    hi = lax.reduce_precision(x, exponent_bits=8, mantissa_bits=7)
    return hi.astype(jnp.bfloat16), (x - hi).astype(jnp.bfloat16)


def update_kernel(kind, tm, width, nbase, flags_ref, info_ref, slots_ref, *refs):
    base_refs = refs[:nbase]
    a_ref, bhi_ref, blo_ref, out_ref = refs[nbase:]
    i = pl.program_id(0)
    per = tm // MSLOT
    active = flags_ref[i * per] != 0
    for q in range(1, per):
        active = jnp.logical_or(active, flags_ref[i * per + q] != 0)

    def base_cols(g):
        cols = pl.ds(g * PANEL, PANEL)
        if kind == "gather":
            return base_refs[g][0]
        if kind == "diag":
            rows = info_ref[2] + i * tm + lax.broadcasted_iota(jnp.int32, (tm, PANEL), 0)
            ids = info_ref[1] + g * PANEL + lax.broadcasted_iota(jnp.int32, (tm, PANEL), 1)
            return jnp.where(rows == ids, base_refs[0][...], 0.0)
        return base_refs[0][:, cols]

    @pl.when(active)
    def _():
        a = a_ref[...]
        a_hi = a.astype(jnp.bfloat16)
        a_lo = (a - a_hi.astype(jnp.float32)).astype(jnp.bfloat16)
        dn = (((1,), (1,)), ((), ()))
        for g in range(width // PANEL):
            rows = pl.ds(g * PANEL, PANEL)
            b_hi = bhi_ref[rows, :]
            acc = lax.dot_general(a_hi, b_hi, dn, preferred_element_type=jnp.float32)
            acc = acc + lax.dot_general(a_hi, blo_ref[rows, :], dn, preferred_element_type=jnp.float32)
            acc = acc + lax.dot_general(a_lo, b_hi, dn, preferred_element_type=jnp.float32)
            out_ref[:, pl.ds(g * PANEL, PANEL)] = base_cols(g) - acc

    @pl.when(jnp.logical_not(active))
    def _():
        for g in range(width // PANEL):
            out_ref[:, pl.ds(g * PANEL, PANEL)] = base_cols(g)

    @pl.when((info_ref[0] == 1) & (info_ref[1] == 0))
    def _():
        out_ref[:, pl.ds(0, PANEL)] = a_ref[...]


def panel_update(kind, base, a, b_hi, b_lo, flags, info, slots, rows, width):
    tm = MSLOT if kind == "gather" or rows % (2 * MSLOT) else 2 * MSLOT
    nseg = width // PANEL
    if kind == "gather":
        bases = [base] * nseg
        base_specs = [
            pl.BlockSpec((1, tm, PANEL), lambda i, f, n, s, g=g: (s[i * nseg + g], 0, 0)) for g in range(nseg)
        ]
    elif kind == "diag":
        bases = [base]
        base_specs = [pl.BlockSpec((tm, 1), lambda i, f, n, s: (i, 0))]
    else:
        bases = [base]
        base_specs = [pl.BlockSpec((tm, width), lambda i, f, n, s: (i, 0))]
    grid_spec = pltpu.PrefetchScalarGridSpec(
        num_scalar_prefetch=3,
        grid=(rows // tm,),
        in_specs=base_specs + [
            pl.BlockSpec((tm, PANEL), lambda i, f, n, s: (i, 0)),
            pl.BlockSpec((width, PANEL), lambda i, f, n, s: (0, 0)),
            pl.BlockSpec((width, PANEL), lambda i, f, n, s: (0, 0)),
        ],
        out_specs=pl.BlockSpec((tm, width), lambda i, f, n, s: (i, 0)),
    )
    flops = 6 * rows * width * PANEL
    cost = pl.CostEstimate(flops=flops, transcendentals=0, bytes_accessed=rows * width * 8 + width * PANEL * 4)
    return pl.pallas_call(
        functools.partial(update_kernel, kind, tm, width, len(bases)),
        grid_spec=grid_spec,
        out_shape=jax.ShapeDtypeStruct((rows, width), jnp.float32),
        cost_estimate=cost,
        compiler_params=pltpu.CompilerParams(vmem_limit_bytes=48 * 1024 * 1024),
    )(flags, info, slots, *bases, a, b_hi, b_lo)


def solve_kernel(x_ref, fhi_ref, flo_ref, out_ref, hi_ref, lo_ref):
    x = x_ref[...]
    x_hi = x.astype(jnp.bfloat16)
    x_lo = (x - x_hi.astype(jnp.float32)).astype(jnp.bfloat16)
    f_hi = fhi_ref[...]
    acc = lax.dot_general(x_hi, f_hi, NT, preferred_element_type=jnp.float32)
    acc = acc + lax.dot_general(x_hi, flo_ref[...], NT, preferred_element_type=jnp.float32)
    acc = acc + lax.dot_general(x_lo, f_hi, NT, preferred_element_type=jnp.float32)
    out_ref[...] = acc
    hi = acc.astype(jnp.bfloat16)
    hi_ref[...] = hi
    lo_ref[...] = (acc - hi.astype(jnp.float32)).astype(jnp.bfloat16)


def apply_inverse(x, f_hi, f_lo, parts=None):
    if parts is None:
        rows = x.shape[0]
        tm = 256 if rows % 256 == 0 else MSLOT
        grid = rows // tm
        x_spec = pl.BlockSpec((tm, PANEL), lambda i: (i, 0))
    else:
        tm, at = parts
        grid = x.shape[0]
        rows = grid * tm
        x_spec = pl.BlockSpec((None, tm, PANEL), lambda i: (i, at, 0))
    spec = pl.BlockSpec((tm, PANEL), lambda i: (i, 0))
    return pl.pallas_call(
        solve_kernel,
        grid=(grid,),
        in_specs=[
            x_spec,
            pl.BlockSpec((PANEL, PANEL), lambda i: (0, 0)),
            pl.BlockSpec((PANEL, PANEL), lambda i: (0, 0)),
        ],
        out_specs=[spec, spec, spec],
        out_shape=[
            jax.ShapeDtypeStruct((rows, PANEL), jnp.float32),
            jax.ShapeDtypeStruct((rows, PANEL), jnp.bfloat16),
            jax.ShapeDtypeStruct((rows, PANEL), jnp.bfloat16),
        ],
        cost_estimate=pl.CostEstimate(flops=6 * rows * PANEL * PANEL, transcendentals=0, bytes_accessed=8 * rows * PANEL),
    )(x, f_hi, f_lo)


def dot_t(left, right):
    contract = (((1,), (1,)), ((), ()))
    l_hi, l_lo = split_bf16(left)
    r_hi, r_lo = split_bf16(right)
    out = lax.dot_general(l_hi, r_hi, contract, preferred_element_type=jnp.float32)
    out = out + lax.dot_general(l_hi, r_lo, contract, preferred_element_type=jnp.float32)
    return out + lax.dot_general(l_lo, r_hi, contract, preferred_element_type=jnp.float32)


def pick(index, options):
    out = options[0]
    for i in range(1, len(options)):
        out = jnp.where(index == i, options[i], out)
    return out


def seg0_slots(tseg, cap0):
    has0 = jnp.any(tseg == 0, axis=1)
    rank0 = jnp.cumsum(has0.astype(jnp.int32)) - 1
    slot = jnp.where(has0, rank0, cap0)
    return has0, rank0, slot


def per_device(eigvecs, coupling, mode_counts, tree_segments, eigvals, stiff):
    R = lax.axis_size("row")
    C = lax.axis_size("col")
    r = lax.axis_index("row")
    c = lax.axis_index("col")
    nsub = eigvecs.shape[0]
    H, W = stiff.shape
    Ec = coupling.shape[3]
    G = W // PANEL
    ratio = R // C
    npair = 2 * nsub
    cap = min(MOST * G * ((nsub + SUB_ROW - 1) // SUB_ROW), npair)
    cap0 = min(MOST * ((nsub + SUB_ROW - 1) // SUB_ROW), nsub)

    live = jnp.arange(MSLOT, dtype=jnp.int32)[None, :] < mode_counts[:, None]
    pieces = jnp.einsum("sim,sitp->stmp", eigvecs, coupling, preferred_element_type=jnp.float32)
    pieces = pieces * live.astype(jnp.float32)[:, None, :, None]
    flat = pieces.reshape(npair, MSLOT, Ec)
    flat_pad = jnp.concatenate([flat, jnp.zeros((1, MSLOT, Ec), jnp.float32)], axis=0)

    kpp_src = stiff[:PANEL, :PANEL]
    rs = PANEL // R
    got = [kpp_src[:rs]]
    for i in range(1, R):
        got.append(lax.ppermute(kpp_src[i * rs:(i + 1) * rs], AXES, [(0, i * C)]))
    kpp_part = pick(r, got)
    kpp_col0 = lax.all_gather(kpp_part, "row", axis=0, tiled=True)
    cs = PANEL // C
    got = [kpp_col0[:cs]]
    for k in range(1, C):
        got.append(lax.ppermute(kpp_col0[k * cs:(k + 1) * cs], AXES, [(i * C, i * C + k) for i in range(R)]))
    kpp = lax.all_gather(pick(c, got), "col", axis=0, tiled=True)

    finv = chol_inverse(kpp)

    tseg = tree_segments
    dest = (tseg // G).reshape(npair)
    onehot = dest[:, None] == jnp.arange(C, dtype=jnp.int32)[None, :]
    rank_pd = jnp.cumsum(onehot.astype(jnp.int32), axis=0) - 1
    rank = jnp.sum(jnp.where(onehot, rank_pd, 0), axis=1)
    match = onehot[:, :, None] & (rank_pd[:, :, None] == jnp.arange(cap, dtype=jnp.int32)[None, None, :])
    send_idx = jnp.where(jnp.any(match, axis=0), jnp.argmax(match, axis=0), npair)
    send = flat_pad[send_idx]
    send, _ = lax.optimization_barrier((send, kpp))
    shifted = [send[c]]
    for k in range(1, C):
        out_k = lax.dynamic_index_in_dim(send, (c + k) % C, axis=0, keepdims=False)
        shifted.append(lax.ppermute(out_k, "col", [(i, (i + k) % C) for i in range(C)]))
    shifted = jnp.stack(shifted)
    recv = shifted[(c - jnp.arange(C, dtype=jnp.int32)) % C]
    recv_t = recv.transpose(1, 2, 0, 3).reshape(cap, MSLOT, C * Ec)
    recv_t = jnp.concatenate([recv_t, jnp.zeros((1, MSLOT, PANEL), jnp.float32)], axis=0)
    my_seg = c * G + jnp.arange(G, dtype=jnp.int32)
    seg_hit = tseg[:, :, None] == my_seg[None, None, :]
    rank2 = rank.reshape(nsub, 2)
    slot_tab = jnp.where(
        jnp.any(seg_hit, axis=1), jnp.sum(jnp.where(seg_hit, rank2[:, :, None], 0), axis=1), cap
    )

    has0, rank0, slot_r = seg0_slots(tseg, cap0)
    t0 = jnp.where(tseg[:, 0] == 0, 0, 1)
    sel = has0[:, None] & (rank0[:, None] == jnp.arange(cap0, dtype=jnp.int32)[None, :])
    sel_sub = jnp.argmax(sel, axis=0)
    zidx = jnp.where(jnp.any(sel, axis=0), sel_sub * 2 + t0[sel_sub], npair)
    z_local = flat_pad[zidx]
    z_all = lax.all_gather(z_local, "col", axis=0, tiled=False)
    z_rows = z_all.transpose(1, 2, 0, 3).reshape(cap0 * MSLOT, C * Ec)

    m_src = stiff[:, :PANEL]
    rps = W // R
    zps = cap0 * MSLOT // C
    got = [m_src[:rps]]
    for k in range(1, C):
        got.append(lax.ppermute(m_src[k * rps:(k + 1) * rps], AXES, [(i * C, i * C + k) for i in range(R)]))
    a_slice = pick(c, got)
    m_row = lax.all_gather(a_slice, "col", axis=0, tiled=True)
    slot_row = jnp.zeros((8, PANEL), jnp.float32).at[0, :nsub].set(slot_r.astype(jnp.float32))
    payload = jnp.concatenate([a_slice, lax.dynamic_slice_in_dim(z_rows, c * zps, zps), slot_row], axis=0)
    perm = [(i * C + k, ((i % ratio) * C + k) * C + i // ratio) for i in range(R) for k in range(C)]
    b_slice = lax.ppermute(payload, AXES, perm)
    col_parts = lax.all_gather(b_slice, "row", axis=0, tiled=False)

    slot_c = []
    for j in range(ratio):
        got_slot = col_parts[j * C, rps + zps, :nsub].astype(jnp.int32)
        slot_c.append(jnp.where(got_slot < cap0, j * cap0 + got_slot, ratio * cap0))
    slot_c = jnp.concatenate(slot_c)

    f_hi, f_lo = split_bf16(finv)
    low_r, _, _ = apply_inverse(m_row, f_hi, f_lo)
    _, lowc_hi, lowc_lo = apply_inverse(col_parts, f_hi, f_lo, (rps, 0))
    lowmi_r, _, _ = apply_inverse(z_rows, f_hi, f_lo)
    _, lmc_hi, lmc_lo = apply_inverse(col_parts, f_hi, f_lo, (zps, rps // zps))

    ones = jnp.ones((H // MSLOT,), jnp.int32)
    none = jnp.zeros((1,), jnp.int32)
    info = jnp.stack([jnp.int32(1), c * W, r * H, jnp.int32(0)]).astype(jnp.int32)
    reduced_ii = panel_update("array", stiff, low_r, lowc_hi, lowc_lo, ones, info, none, H, W)

    lmi = jnp.concatenate(
        [lowmi_r.reshape(cap0, MSLOT, PANEL), jnp.zeros((1, MSLOT, PANEL), jnp.float32)], axis=0
    )
    lmi_full = lmi[slot_r].reshape(nsub * MSLOT, PANEL)
    flags = has0.astype(jnp.int32)
    reduced_mi = panel_update(
        "gather", recv_t, lmi_full, lowc_hi, lowc_lo, flags, info, slot_tab.reshape(-1).astype(jnp.int32), nsub * MSLOT, W
    )

    nc = ratio * cap0
    mode_width = ratio * nsub * MSLOT

    def spread_cols(part):
        part = jnp.concatenate([part.reshape(nc, MSLOT, PANEL), jnp.zeros((1, MSLOT, PANEL), part.dtype)], axis=0)
        return part[slot_c].reshape(mode_width, PANEL)

    diag_values = jnp.where(live, eigvals, 1.0).reshape(-1, 1)
    mode_rows = diag_values.shape[0]
    info_mm = jnp.stack([jnp.int32(0), c * mode_width, r * mode_rows, jnp.int32(0)]).astype(jnp.int32)
    reduced_mm = panel_update("diag", diag_values, lmi_full, spread_cols(lmc_hi), spread_cols(lmc_lo), flags, info_mm, none, mode_rows, mode_width)
    return (reduced_ii, reduced_mi, reduced_mm)


def solution(mesh):
    in_specs = (
        P("row", None, None),
        P("row", None, None, "col"),
        P("row"),
        P("row", None),
        P("row", None),
        P("row", "col"),
    )
    out_specs = (P("row", "col"), P("row", "col"), P("row", "col"))
    return jax.shard_map(
        per_device, mesh=mesh, in_specs=in_specs, out_specs=out_specs, check_vma=False
    )
```

```python
import functools

import jax
import jax.numpy as jnp
from jax import lax
from jax.sharding import PartitionSpec as P
from jax.experimental import pallas as pl
from jax.experimental.pallas import tpu as pltpu

MSLOT = 128
PANEL = 512
MOST = 2
SUB_ROW = 8

AXES = ("row", "col")
LEAF = 128


def mm3(a, b, dn):
    a_hi = a.astype(jnp.bfloat16)
    a_lo = (a - a_hi.astype(jnp.float32)).astype(jnp.bfloat16)
    b_hi = b.astype(jnp.bfloat16)
    b_lo = (b - b_hi.astype(jnp.float32)).astype(jnp.bfloat16)
    out = lax.dot_general(a_hi, b_hi, dn, preferred_element_type=jnp.float32)
    out = out + lax.dot_general(a_hi, b_lo, dn, preferred_element_type=jnp.float32)
    return out + lax.dot_general(a_lo, b_hi, dn, preferred_element_type=jnp.float32)


NN = (((1,), (0,)), ((), ()))
NT = (((1,), (1,)), ((), ()))


def leaf_inverse(d, d_ref, e_ref, x_ref):
    n = d.shape[0]
    sub = lax.broadcasted_iota(jnp.int32, (n, n), 0)
    lane = lax.broadcasted_iota(jnp.int32, (n, n), 1)
    sub_c = lax.broadcasted_iota(jnp.int32, (n, 1), 0)
    lane_r = lax.broadcasted_iota(jnp.int32, (1, n), 1)
    d_ref[...] = d
    e_ref[...] = jnp.where(sub == lane, 1.0, 0.0).astype(jnp.float32)
    x_ref[...] = jnp.zeros((n, n), jnp.float32)

    def step(k, carry):
        dm = d_ref[...]
        colk = jnp.sum(jnp.where(lane == k, dm, 0.0), axis=1, keepdims=True)
        rowk = d_ref[pl.ds(k, 1), :]
        dkk = jnp.sum(jnp.where(lane_r == k, rowk, 0.0), axis=1, keepdims=True)
        s = lax.rsqrt(dkk)
        lc = jnp.where(sub_c > k, colk * s, 0.0)
        lr = jnp.where(lane_r > k, rowk * s, 0.0)
        d_ref[...] = dm - lc * lr
        xk = e_ref[pl.ds(k, 1), :] * s
        x_ref[pl.ds(k, 1), :] = xk
        e_ref[...] = e_ref[...] - lc * xk
        return carry

    lax.fori_loop(0, n, step, 0, unroll=8)
    return x_ref[...]


def chol_inv_kernel(a_ref, x_ref, w_ref, l_ref, d_ref, e_ref, xl_ref):
    n = a_ref.shape[0]
    nb = n // LEAF
    w_ref[...] = a_ref[...]
    for kb in range(nb):
        o = kb * LEAF
        blk = pl.ds(o, LEAF)
        xkk = leaf_inverse(w_ref[blk, blk], d_ref, e_ref, xl_ref)
        x_ref[blk, blk] = xkk
        if kb + 1 < nb:
            rest = pl.ds(o + LEAF, n - o - LEAF)
            panel = mm3(w_ref[rest, blk], xkk, NT)
            l_ref[rest, blk] = panel
            w_ref[rest, rest] = w_ref[rest, rest] - mm3(panel, panel, NT)
    for i in range(1, nb):
        bi = pl.ds(i * LEAF, LEAF)
        xii = x_ref[bi, bi]
        for j in range(i):
            bj = pl.ds(j * LEAF, LEAF)
            acc = None
            for k in range(j, i):
                bk = pl.ds(k * LEAF, LEAF)
                term = mm3(l_ref[bi, bk], x_ref[bk, bj], NN)
                acc = term if acc is None else acc + term
            x_ref[bi, bj] = -mm3(xii, acc, NN)
        for j in range(i + 1, nb):
            x_ref[bi, pl.ds(j * LEAF, LEAF)] = jnp.zeros((LEAF, LEAF), jnp.float32)
    x_ref[pl.ds(0, LEAF), pl.ds(LEAF, n - LEAF)] = jnp.zeros((LEAF, n - LEAF), jnp.float32)


def chol_inverse(a):
    n = a.shape[0]
    return pl.pallas_call(
        chol_inv_kernel,
        out_shape=jax.ShapeDtypeStruct((n, n), jnp.float32),
        cost_estimate=pl.CostEstimate(flops=800 * n ** 3, transcendentals=n, bytes_accessed=8 * n * n),
        in_specs=[pl.BlockSpec(memory_space=pltpu.VMEM)],
        out_specs=pl.BlockSpec(memory_space=pltpu.VMEM),
        scratch_shapes=[pltpu.VMEM((n, n), jnp.float32), pltpu.VMEM((n, n), jnp.float32)]
        + [pltpu.VMEM((LEAF, LEAF), jnp.float32)] * 3,
    )(a)


def split_bf16(x):
    hi = lax.reduce_precision(x, exponent_bits=8, mantissa_bits=7)
    return hi.astype(jnp.bfloat16), (x - hi).astype(jnp.bfloat16)


def update_kernel(kind, tm, width, nbase, flags_ref, info_ref, slots_ref, *refs):
    base_refs = refs[:nbase]
    a_ref, bhi_ref, blo_ref, out_ref = refs[nbase:]
    i = pl.program_id(0)
    per = tm // MSLOT
    active = flags_ref[i * per] != 0
    for q in range(1, per):
        active = jnp.logical_or(active, flags_ref[i * per + q] != 0)

    def base_cols(g):
        cols = pl.ds(g * PANEL, PANEL)
        if kind == "gather":
            return base_refs[g][0]
        if kind == "diag":
            rows = info_ref[2] + i * tm + lax.broadcasted_iota(jnp.int32, (tm, PANEL), 0)
            ids = info_ref[1] + g * PANEL + lax.broadcasted_iota(jnp.int32, (tm, PANEL), 1)
            return jnp.where(rows == ids, base_refs[0][...], 0.0)
        return base_refs[0][:, cols]

    @pl.when(active)
    def _():
        a = a_ref[...]
        a_hi = a.astype(jnp.bfloat16)
        a_lo = (a - a_hi.astype(jnp.float32)).astype(jnp.bfloat16)
        dn = (((1,), (1,)), ((), ()))
        for g in range(width // PANEL):
            rows = pl.ds(g * PANEL, PANEL)
            b_hi = bhi_ref[rows, :]
            acc = lax.dot_general(a_hi, b_hi, dn, preferred_element_type=jnp.float32)
            acc = acc + lax.dot_general(a_hi, blo_ref[rows, :], dn, preferred_element_type=jnp.float32)
            acc = acc + lax.dot_general(a_lo, b_hi, dn, preferred_element_type=jnp.float32)
            out_ref[:, pl.ds(g * PANEL, PANEL)] = base_cols(g) - acc

    @pl.when(jnp.logical_not(active))
    def _():
        for g in range(width // PANEL):
            out_ref[:, pl.ds(g * PANEL, PANEL)] = base_cols(g)

    @pl.when((info_ref[0] == 1) & (info_ref[1] == 0))
    def _():
        out_ref[:, pl.ds(0, PANEL)] = a_ref[...]


def panel_update(kind, base, a, b_hi, b_lo, flags, info, slots, rows, width):
    tm = MSLOT if kind == "gather" or rows % (4 * MSLOT) else 4 * MSLOT
    nseg = width // PANEL
    if kind == "gather":
        bases = [base] * nseg
        base_specs = [
            pl.BlockSpec((1, tm, PANEL), lambda i, f, n, s, g=g: (s[i * nseg + g], 0, 0)) for g in range(nseg)
        ]
    elif kind == "diag":
        bases = [base]
        base_specs = [pl.BlockSpec((tm, 1), lambda i, f, n, s: (i, 0))]
    else:
        bases = [base]
        base_specs = [pl.BlockSpec((tm, width), lambda i, f, n, s: (i, 0))]
    grid_spec = pltpu.PrefetchScalarGridSpec(
        num_scalar_prefetch=3,
        grid=(rows // tm,),
        in_specs=base_specs + [
            pl.BlockSpec((tm, PANEL), lambda i, f, n, s: (i, 0)),
            pl.BlockSpec((width, PANEL), lambda i, f, n, s: (0, 0)),
            pl.BlockSpec((width, PANEL), lambda i, f, n, s: (0, 0)),
        ],
        out_specs=pl.BlockSpec((tm, width), lambda i, f, n, s: (i, 0)),
    )
    flops = 6 * rows * width * PANEL
    cost = pl.CostEstimate(flops=flops, transcendentals=0, bytes_accessed=rows * width * 8 + width * PANEL * 4)
    return pl.pallas_call(
        functools.partial(update_kernel, kind, tm, width, len(bases)),
        grid_spec=grid_spec,
        out_shape=jax.ShapeDtypeStruct((rows, width), jnp.float32),
        cost_estimate=cost,
        compiler_params=pltpu.CompilerParams(vmem_limit_bytes=48 * 1024 * 1024),
    )(flags, info, slots, *bases, a, b_hi, b_lo)


def solve_kernel(x_ref, fhi_ref, flo_ref, out_ref, hi_ref, lo_ref):
    x = x_ref[...]
    x_hi = x.astype(jnp.bfloat16)
    x_lo = (x - x_hi.astype(jnp.float32)).astype(jnp.bfloat16)
    f_hi = fhi_ref[...]
    acc = lax.dot_general(x_hi, f_hi, NT, preferred_element_type=jnp.float32)
    acc = acc + lax.dot_general(x_hi, flo_ref[...], NT, preferred_element_type=jnp.float32)
    acc = acc + lax.dot_general(x_lo, f_hi, NT, preferred_element_type=jnp.float32)
    out_ref[...] = acc
    hi = acc.astype(jnp.bfloat16)
    hi_ref[...] = hi
    lo_ref[...] = (acc - hi.astype(jnp.float32)).astype(jnp.bfloat16)


def apply_inverse(x, f_hi, f_lo, parts=None):
    if parts is None:
        rows = x.shape[0]
        tm = 256 if rows % 256 == 0 else MSLOT
        grid = rows // tm
        x_spec = pl.BlockSpec((tm, PANEL), lambda i: (i, 0))
    else:
        tm, at = parts
        grid = x.shape[0]
        rows = grid * tm
        x_spec = pl.BlockSpec((None, tm, PANEL), lambda i: (i, at, 0))
    spec = pl.BlockSpec((tm, PANEL), lambda i: (i, 0))
    return pl.pallas_call(
        solve_kernel,
        grid=(grid,),
        in_specs=[
            x_spec,
            pl.BlockSpec((PANEL, PANEL), lambda i: (0, 0)),
            pl.BlockSpec((PANEL, PANEL), lambda i: (0, 0)),
        ],
        out_specs=[spec, spec, spec],
        out_shape=[
            jax.ShapeDtypeStruct((rows, PANEL), jnp.float32),
            jax.ShapeDtypeStruct((rows, PANEL), jnp.bfloat16),
            jax.ShapeDtypeStruct((rows, PANEL), jnp.bfloat16),
        ],
        cost_estimate=pl.CostEstimate(flops=6 * rows * PANEL * PANEL, transcendentals=0, bytes_accessed=8 * rows * PANEL),
    )(x, f_hi, f_lo)


def dot_t(left, right):
    contract = (((1,), (1,)), ((), ()))
    l_hi, l_lo = split_bf16(left)
    r_hi, r_lo = split_bf16(right)
    out = lax.dot_general(l_hi, r_hi, contract, preferred_element_type=jnp.float32)
    out = out + lax.dot_general(l_hi, r_lo, contract, preferred_element_type=jnp.float32)
    return out + lax.dot_general(l_lo, r_hi, contract, preferred_element_type=jnp.float32)


def pick(index, options):
    out = options[0]
    for i in range(1, len(options)):
        out = jnp.where(index == i, options[i], out)
    return out


def seg0_slots(tseg, cap0):
    has0 = jnp.any(tseg == 0, axis=1)
    rank0 = jnp.cumsum(has0.astype(jnp.int32)) - 1
    slot = jnp.where(has0, rank0, cap0)
    return has0, rank0, slot


def per_device(eigvecs, coupling, mode_counts, tree_segments, eigvals, stiff):
    R = lax.axis_size("row")
    C = lax.axis_size("col")
    r = lax.axis_index("row")
    c = lax.axis_index("col")
    nsub = eigvecs.shape[0]
    H, W = stiff.shape
    Ec = coupling.shape[3]
    G = W // PANEL
    ratio = R // C
    npair = 2 * nsub
    cap = min(MOST * G * ((nsub + SUB_ROW - 1) // SUB_ROW), npair)
    cap0 = min(MOST * ((nsub + SUB_ROW - 1) // SUB_ROW), nsub)

    live = jnp.arange(MSLOT, dtype=jnp.int32)[None, :] < mode_counts[:, None]
    pieces = jnp.einsum("sim,sitp->stmp", eigvecs, coupling, preferred_element_type=jnp.float32)
    pieces = pieces * live.astype(jnp.float32)[:, None, :, None]
    flat = pieces.reshape(npair, MSLOT, Ec)
    flat_pad = jnp.concatenate([flat, jnp.zeros((1, MSLOT, Ec), jnp.float32)], axis=0)

    kpp_src = stiff[:PANEL, :PANEL]
    rs = PANEL // R
    got = [kpp_src[:rs]]
    for i in range(1, R):
        got.append(lax.ppermute(kpp_src[i * rs:(i + 1) * rs], AXES, [(0, i * C)]))
    kpp_part = pick(r, got)
    kpp_col0 = lax.all_gather(kpp_part, "row", axis=0, tiled=True)
    cs = PANEL // C
    got = [kpp_col0[:cs]]
    for k in range(1, C):
        got.append(lax.ppermute(kpp_col0[k * cs:(k + 1) * cs], AXES, [(i * C, i * C + k) for i in range(R)]))
    kpp = lax.all_gather(pick(c, got), "col", axis=0, tiled=True)

    finv = chol_inverse(kpp)

    tseg = tree_segments
    dest = (tseg // G).reshape(npair)
    onehot = dest[:, None] == jnp.arange(C, dtype=jnp.int32)[None, :]
    rank_pd = jnp.cumsum(onehot.astype(jnp.int32), axis=0) - 1
    rank = jnp.sum(jnp.where(onehot, rank_pd, 0), axis=1)
    match = onehot[:, :, None] & (rank_pd[:, :, None] == jnp.arange(cap, dtype=jnp.int32)[None, None, :])
    send_idx = jnp.where(jnp.any(match, axis=0), jnp.argmax(match, axis=0), npair)
    send = flat_pad[send_idx]
    send, _ = lax.optimization_barrier((send, kpp))
    shifted = [send[c]]
    for k in range(1, C):
        out_k = lax.dynamic_index_in_dim(send, (c + k) % C, axis=0, keepdims=False)
        shifted.append(lax.ppermute(out_k, "col", [(i, (i + k) % C) for i in range(C)]))
    shifted = jnp.stack(shifted)
    recv = shifted[(c - jnp.arange(C, dtype=jnp.int32)) % C]
    recv_t = recv.transpose(1, 2, 0, 3).reshape(cap, MSLOT, C * Ec)
    recv_t = jnp.concatenate([recv_t, jnp.zeros((1, MSLOT, PANEL), jnp.float32)], axis=0)
    my_seg = c * G + jnp.arange(G, dtype=jnp.int32)
    seg_hit = tseg[:, :, None] == my_seg[None, None, :]
    rank2 = rank.reshape(nsub, 2)
    slot_tab = jnp.where(
        jnp.any(seg_hit, axis=1), jnp.sum(jnp.where(seg_hit, rank2[:, :, None], 0), axis=1), cap
    )

    has0, rank0, slot_r = seg0_slots(tseg, cap0)
    t0 = jnp.where(tseg[:, 0] == 0, 0, 1)
    sel = has0[:, None] & (rank0[:, None] == jnp.arange(cap0, dtype=jnp.int32)[None, :])
    sel_sub = jnp.argmax(sel, axis=0)
    zidx = jnp.where(jnp.any(sel, axis=0), sel_sub * 2 + t0[sel_sub], npair)
    z_local = flat_pad[zidx]
    z_all = lax.all_gather(z_local, "col", axis=0, tiled=False)
    z_rows = z_all.transpose(1, 2, 0, 3).reshape(cap0 * MSLOT, C * Ec)

    m_src = stiff[:, :PANEL]
    rps = W // R
    zps = cap0 * MSLOT // C
    got = [m_src[:rps]]
    for k in range(1, C):
        got.append(lax.ppermute(m_src[k * rps:(k + 1) * rps], AXES, [(i * C, i * C + k) for i in range(R)]))
    a_slice = pick(c, got)
    m_row = lax.all_gather(a_slice, "col", axis=0, tiled=True)
    slot_row = jnp.zeros((8, PANEL), jnp.float32).at[0, :nsub].set(slot_r.astype(jnp.float32))
    payload = jnp.concatenate([a_slice, lax.dynamic_slice_in_dim(z_rows, c * zps, zps), slot_row], axis=0)
    perm = [(i * C + k, ((i % ratio) * C + k) * C + i // ratio) for i in range(R) for k in range(C)]
    b_slice = lax.ppermute(payload, AXES, perm)
    col_parts = lax.all_gather(b_slice, "row", axis=0, tiled=False)

    slot_c = []
    for j in range(ratio):
        got_slot = col_parts[j * C, rps + zps, :nsub].astype(jnp.int32)
        slot_c.append(jnp.where(got_slot < cap0, j * cap0 + got_slot, ratio * cap0))
    slot_c = jnp.concatenate(slot_c)

    f_hi, f_lo = split_bf16(finv)
    low_r, _, _ = apply_inverse(m_row, f_hi, f_lo)
    _, lowc_hi, lowc_lo = apply_inverse(col_parts, f_hi, f_lo, (rps, 0))
    lowmi_r, _, _ = apply_inverse(z_rows, f_hi, f_lo)
    _, lmc_hi, lmc_lo = apply_inverse(col_parts, f_hi, f_lo, (zps, rps // zps))

    ones = jnp.ones((H // MSLOT,), jnp.int32)
    none = jnp.zeros((1,), jnp.int32)
    info = jnp.stack([jnp.int32(1), c * W, r * H, jnp.int32(0)]).astype(jnp.int32)
    reduced_ii = panel_update("array", stiff, low_r, lowc_hi, lowc_lo, ones, info, none, H, W)

    lmi = jnp.concatenate(
        [lowmi_r.reshape(cap0, MSLOT, PANEL), jnp.zeros((1, MSLOT, PANEL), jnp.float32)], axis=0
    )
    lmi_full = lmi[slot_r].reshape(nsub * MSLOT, PANEL)
    flags = has0.astype(jnp.int32)
    reduced_mi = panel_update(
        "gather", recv_t, lmi_full, lowc_hi, lowc_lo, flags, info, slot_tab.reshape(-1).astype(jnp.int32), nsub * MSLOT, W
    )

    nc = ratio * cap0
    mode_width = ratio * nsub * MSLOT

    def spread_cols(part):
        part = jnp.concatenate([part.reshape(nc, MSLOT, PANEL), jnp.zeros((1, MSLOT, PANEL), part.dtype)], axis=0)
        return part[slot_c].reshape(mode_width, PANEL)

    diag_values = jnp.where(live, eigvals, 1.0).reshape(-1, 1)
    mode_rows = diag_values.shape[0]
    info_mm = jnp.stack([jnp.int32(0), c * mode_width, r * mode_rows, jnp.int32(0)]).astype(jnp.int32)
    reduced_mm = panel_update("diag", diag_values, lmi_full, spread_cols(lmc_hi), spread_cols(lmc_lo), flags, info_mm, none, mode_rows, mode_width)
    return (reduced_ii, reduced_mi, reduced_mm)


def solution(mesh):
    in_specs = (
        P("row", None, None),
        P("row", None, None, "col"),
        P("row"),
        P("row", None),
        P("row", None),
        P("row", "col"),
    )
    out_specs = (P("row", "col"), P("row", "col"), P("row", "col"))
    return jax.shard_map(
        per_device, mesh=mesh, in_specs=in_specs, out_specs=out_specs, check_vma=False
    )
```
